32 devices in a mesh: dp: 2 (over x), seq: 16 (over z, y, core).
Axes of the slice: x: 2, y: 2, z: 4, core: 2. Of those that a mesh axis runs over, the one named last changes fastest.
Arguments:
- first_query: bfloat16 [2, 16, 128, 1024], P('dp', 'seq'), may hold values from -6 to 6
- first_key: bfloat16 [2, 16, 128, 1024], P('dp', 'seq'), may hold values from -6 to 6
- first_value: bfloat16 [2, 16, 128, 1024], P('dp', 'seq'), may hold values from -6 to 6
- out_weight: bfloat16 [1024, 1024], replicated, may hold values from -1 to 1
- norm_gain: float32 [1024], replicated, may hold values from 0.5 to 2
- joint_weight: bfloat16 [1024, 3072], replicated, may hold values from -1 to 1
- upstream: bfloat16 [2, 16, 128, 1024], P('dp', 'seq'), may hold values from -6 to 6
Outputs:
- grad_query: bfloat16 [2, 16, 128, 1024], P('dp', 'seq')
- grad_key: bfloat16 [2, 16, 128, 1024], P('dp', 'seq')
- grad_value: bfloat16 [2, 16, 128, 1024], P('dp', 'seq')
- column_out: bfloat16 [2, 16, 128, 1024], P('dp', 'seq')
- grad_joint: bfloat16 [1024, 3072], P('seq')
- grad_projection: bfloat16 [1024, 1024], P('seq')
- grad_gain: float32 [1024], P('seq')
The draws below stay inside these ranges and needn't reach their ends.
All inputs are finite; a program needn't handle non-finite values.
Results may differ from the reference program's by a relative error of at most 0.019.
The reference program's roundings to bfloat16 on the way count: a program that leaves them out, or rounds other values in their place, can miss the bound.
Values may be sent and summed in bfloat16 or wider, within the bound.
No kernel may reach another device: no remote copies, remote signals or barrier semaphores. Data moves between devices by JAX's collectives and lax.ppermute only.
A program may use at most 128 MiB of HBM per device.

```python
import math
import jax
import jax.numpy as jnp
from jax import lax

D = 1024
HEAD_DIM = 128
HW = 1024
BATCH = 2
ROWS = 16
COLS = 128


def clipped_normal(key, shape, scale):
    return jnp.clip(jax.random.normal(key, shape, jnp.float32), -6.0, 6.0) * scale


def draw_first_query(key, part):
    base = clipped_normal(jax.random.fold_in(key, 11), (BATCH, ROWS, COLS, HW), 1.0)
    return base.astype(jnp.bfloat16)


def draw_first_key(key, part):
    base = clipped_normal(jax.random.fold_in(key, 12), (BATCH, ROWS, COLS, HW), 1.0)
    return base.astype(jnp.bfloat16)


def draw_first_value(key, part):
    noise = jax.random.normal(jax.random.fold_in(key, 13), (BATCH, ROWS, COLS, HW), jnp.float32)
    return jnp.clip(noise, -6.0, 6.0).astype(jnp.bfloat16)


def draw_out_weight(key, part):
    base = clipped_normal(jax.random.fold_in(key, 14), (HW, D), HW ** (-0.5))
    return base.astype(jnp.bfloat16)


def draw_joint_weight(key, part):
    base = clipped_normal(jax.random.fold_in(key, 15), (D, 3 * HW), D ** (-0.5))
    return base.astype(jnp.bfloat16)


def levels(key, shape, cuts, low, largest):
    def one(axis_at, parts):
        heights = jax.random.uniform(jax.random.fold_in(jax.random.fold_in(key, 6), axis_at), (parts,), jnp.float32, low / len(cuts), largest / len(cuts))
        return jnp.repeat(jnp.exp(heights), shape[axis_at] // parts).reshape((-1,) + (1,) * (len(shape) - axis_at - 1))

    gain = one(*cuts[0])
    for cut in cuts[1:]:
        gain = gain * one(*cut)
    return gain


def normal_values(own_key, shape, spread, limit, cuts=(), dtype=jnp.bfloat16):
    values = jax.random.normal(own_key, shape, jnp.float32) * spread
    if len(cuts) > 0:
        values = levels(own_key, shape, cuts, -0.22, 0.18) * values
    return jnp.clip(values, min=-limit, max=limit).astype(dtype)


def setup_inputs(seed: int = 0) -> dict:
    seeds = jax.random.split(jax.random.key(seed), 8)
    first_query = draw_first_query(jax.random.fold_in(seeds[7], 71), 0)
    first_key = draw_first_key(jax.random.fold_in(seeds[7], 71), 0)
    first_value = draw_first_value(jax.random.fold_in(seeds[7], 71), 0)
    out_weight = draw_out_weight(jax.random.fold_in(seeds[7], 71), 0)
    norm_gain = jnp.clip(jnp.exp(jax.random.uniform(seeds[4], (D,), jnp.float32, math.log(0.5), math.log(2.0))), 0.5, 2.0)
    joint_weight = draw_joint_weight(jax.random.fold_in(seeds[7], 71), 0)
    upstream = normal_values(seeds[6], (BATCH, ROWS, COLS, HW), 1.0, 6.0, ((0, 2), (1, 16)))
    return dict(first_query=first_query, first_key=first_key, first_value=first_value, out_weight=out_weight, norm_gain=norm_gain, joint_weight=joint_weight, upstream=upstream)


epsilon = 1e-06

def attend(queries, key_table, values, layout, scores_form):
    keyed = layout.replace('l', 'm')
    scaling = HEAD_DIM ** (-0.5)
    scores = jnp.einsum(layout + ',' + keyed + '->' + scores_form, queries.astype(jnp.float32), key_table.astype(jnp.float32)) * scaling
    extent = scores.shape[-1]
    causal = jnp.arange(extent)[:, None] >= jnp.arange(extent)[None, :]
    scores = jnp.where(causal, scores, -1e+30)
    peak = lax.optimization_barrier(jnp.max(scores, axis=-1, keepdims=True))
    weights = jnp.exp(scores - peak)
    prob_table = weights / lax.optimization_barrier(jnp.sum(weights, axis=-1, keepdims=True))
    rounded = prob_table.astype(jnp.bfloat16)
    output = jnp.einsum(scores_form + ',' + keyed + '->' + layout, rounded.astype(jnp.float32), values.astype(jnp.float32))
    return (output.astype(jnp.bfloat16), prob_table)

def attend_back(queries, key_table, values, prob_table, upstream_part, layout, scores_form):
    keyed = layout.replace('l', 'm')
    scaling = HEAD_DIM ** (-0.5)
    grad_prob = jnp.einsum(layout + ',' + keyed + '->' + scores_form, upstream_part.astype(jnp.float32), values.astype(jnp.float32))
    row_inner = lax.optimization_barrier(jnp.sum(prob_table * grad_prob, axis=-1, keepdims=True))
    grad_score = (prob_table * (grad_prob - row_inner) * scaling).astype(jnp.bfloat16).astype(jnp.float32)
    grad_query = jnp.einsum(scores_form + ',' + keyed + '->' + layout, grad_score, key_table.astype(jnp.float32))
    grad_key = jnp.einsum(scores_form + ',' + layout + '->' + keyed, grad_score, queries.astype(jnp.float32))
    rounded = prob_table.astype(jnp.bfloat16).astype(jnp.float32)
    grad_value = jnp.einsum(scores_form + ',' + layout + '->' + keyed, rounded, upstream_part.astype(jnp.float32))
    return (grad_query.astype(jnp.bfloat16), grad_key.astype(jnp.bfloat16), grad_value.astype(jnp.bfloat16))

def reference(first_query, first_key, first_value, out_weight, norm_gain, joint_weight, upstream):

    def one_sequence(operands):
        query_seq, key_seq, value_seq, upstream_seq = operands
        grid_rows, grid_cols, feature = query_seq.shape
        head_count = feature // HEAD_DIM

        def to_heads(tensor):
            return tensor.reshape(grid_rows, grid_cols, head_count, HEAD_DIM)
        out_first, probs_first = attend(to_heads(query_seq), to_heads(key_seq), to_heads(value_seq), 'glhe', 'ghlm')
        flat_first = out_first.reshape(grid_rows * grid_cols, feature)
        hidden = jnp.dot(flat_first, out_weight, preferred_element_type=jnp.float32)
        inverse = lax.rsqrt(lax.optimization_barrier(jnp.mean(hidden * hidden, axis=-1, keepdims=True)) + epsilon)
        normed = (hidden * inverse * norm_gain).astype(jnp.bfloat16)
        joint_proj = jnp.dot(normed, joint_weight, preferred_element_type=jnp.float32).astype(jnp.bfloat16)
        pieces = joint_proj.reshape(1, grid_rows, grid_cols, 3, head_count, HEAD_DIM)
        query_cols, key_cols, value_cols = (pieces[:, :, :, 0], pieces[:, :, :, 1], pieces[:, :, :, 2])
        out_cols, probs_cols = attend(query_cols, key_cols, value_cols, 'blche', 'bchlm')
        column_seq = out_cols.reshape(grid_rows, grid_cols, feature)
        upstream_cols = upstream_seq.reshape(1, grid_rows, grid_cols, head_count, HEAD_DIM)
        grads_cols = attend_back(query_cols, key_cols, value_cols, probs_cols, upstream_cols, 'blche', 'bchlm')
        stacked = jnp.stack(grads_cols, axis=3).reshape(grid_rows * grid_cols, 3 * feature)
        joint_term = jnp.dot(normed.T, stacked, preferred_element_type=jnp.float32)
        grad_normed = jnp.dot(stacked, joint_weight.T, preferred_element_type=jnp.float32).astype(jnp.bfloat16).astype(jnp.float32)
        gain_term = lax.optimization_barrier(jnp.sum(grad_normed * hidden * inverse, axis=0))
        scaled = norm_gain * grad_normed
        grad_hidden = (inverse * scaled - hidden * inverse ** 3 * lax.optimization_barrier(jnp.mean(scaled * hidden, axis=-1, keepdims=True))).astype(jnp.bfloat16)
        out_term = jnp.dot(flat_first.T, grad_hidden, preferred_element_type=jnp.float32)
        grad_first = jnp.dot(grad_hidden, out_weight.T, preferred_element_type=jnp.float32).astype(jnp.bfloat16)
        grads_rows = attend_back(to_heads(query_seq), to_heads(key_seq), to_heads(value_seq), probs_first, to_heads(grad_first), 'glhe', 'ghlm')
        grads_rows = tuple((item.reshape(grid_rows, grid_cols, feature) for item in grads_rows))
        return (grads_rows[0], grads_rows[1], grads_rows[2], column_seq, joint_term, out_term, gain_term)
    results = lax.map(one_sequence, (first_query, first_key, first_value, upstream))
    grad_query, grad_key, grad_value, column_out, joint_terms, out_terms, gain_terms = results
    grad_joint = lax.optimization_barrier(jnp.sum(joint_terms, axis=0)).astype(jnp.bfloat16)
    grad_projection = lax.optimization_barrier(jnp.sum(out_terms, axis=0)).astype(jnp.bfloat16)
    grad_gain = lax.optimization_barrier(jnp.sum(gain_terms, axis=0))
    return (grad_query, grad_key, grad_value, column_out, grad_joint, grad_projection, grad_gain)
```

```python
import jax
import jax.numpy as jnp
from jax import lax
from jax.sharding import PartitionSpec as P

HEAD_DIM = 128


epsilon = 1e-06


def attend(queries, key_table, values, layout, scores_form):
    keyed = layout.replace("l", "m")
    scaling = HEAD_DIM ** (-0.5)
    scores = (
        jnp.einsum(
            layout + "," + keyed + "->" + scores_form,
            queries,
            key_table,
            preferred_element_type=jnp.float32,
        )
        * scaling
    )
    extent = scores.shape[-1]
    causal = jnp.arange(extent)[:, None] >= jnp.arange(extent)[None, :]
    scores = jnp.where(causal, scores, -1e30)
    peak = jnp.max(scores, axis=-1, keepdims=True)
    weights = jnp.exp(scores - peak)
    prob_table = weights / jnp.sum(weights, axis=-1, keepdims=True)
    rounded = prob_table.astype(jnp.bfloat16)
    output = jnp.einsum(
        scores_form + "," + keyed + "->" + layout,
        rounded,
        values,
        preferred_element_type=jnp.float32,
    )
    return (output.astype(jnp.bfloat16), prob_table)


def attend_back(queries, key_table, values, prob_table, upstream_part, layout, scores_form):
    keyed = layout.replace("l", "m")
    scaling = HEAD_DIM ** (-0.5)
    grad_prob = jnp.einsum(
        layout + "," + keyed + "->" + scores_form,
        upstream_part,
        values,
        preferred_element_type=jnp.float32,
    )
    row_inner = jnp.sum(prob_table * grad_prob, axis=-1, keepdims=True)
    grad_score = (prob_table * (grad_prob - row_inner) * scaling).astype(jnp.bfloat16)
    grad_query = jnp.einsum(
        scores_form + "," + keyed + "->" + layout,
        grad_score,
        key_table,
        preferred_element_type=jnp.float32,
    )
    grad_key = jnp.einsum(
        scores_form + "," + layout + "->" + keyed,
        grad_score,
        queries,
        preferred_element_type=jnp.float32,
    )
    rounded = prob_table.astype(jnp.bfloat16)
    grad_value = jnp.einsum(
        scores_form + "," + layout + "->" + keyed,
        rounded,
        upstream_part,
        preferred_element_type=jnp.float32,
    )
    return (
        grad_query.astype(jnp.bfloat16),
        grad_key.astype(jnp.bfloat16),
        grad_value.astype(jnp.bfloat16),
    )


def split_orders(seq_n):
    bits = seq_n.bit_length() - 1
    assert 1 << bits == seq_n
    even = list(range(bits))
    odd = list(even)
    if bits >= 3:
        odd[1], odd[2] = odd[2], odd[1]
    return even, odd


def by_split_order(matrix, orders, core_odd, seq_n):
    bits = seq_n.bit_length() - 1
    lead = matrix.shape[0]
    block = matrix.shape[1] // seq_n
    grid = matrix.reshape((lead,) + (2,) * bits + (matrix.shape[1] // seq_n,))

    def arrange(order):
        axes = (0,) + tuple(1 + (bits - 1 - bit) for bit in order) + (bits + 1,)
        return jnp.transpose(grid, axes).reshape(lead, seq_n * block)

    even, odd = orders
    if even == odd:
        return arrange(even)
    return jnp.where(core_odd, arrange(odd), arrange(even))


def reduce_rows(parts, orders, seq_n, dp_n):
    bits = seq_n.bit_length() - 1
    index = lax.axis_index("seq")
    accs = tuple(p.reshape((2,) * bits + (p.shape[0] // seq_n, p.shape[1])) for p in parts)
    even, odd = orders
    for step in range(bits):
        perm = []
        for member in range(seq_n):
            bit = (odd if member % 2 else even)[step]
            perm.append((member, member ^ (1 << bit)))
        bit_even, bit_odd = even[step], odd[step]
        keep_even = (index // (1 << bit_even)) % 2
        keep_odd = (index // (1 << bit_odd)) % 2
        keep_at = jnp.where(index % 2 == 1, keep_odd, keep_even)
        kept = tuple(lax.dynamic_index_in_dim(acc, keep_at, 0, keepdims=False) for acc in accs)
        given = tuple(
            lax.dynamic_index_in_dim(acc, 1 - keep_at, 0, keepdims=False).astype(jnp.bfloat16)
            for acc in accs
        )
        if step == 0 and even != odd:
            given = tuple(jnp.swapaxes(g, 0, 1) for g in given)
        got = lax.ppermute(given, "seq", perm)
        accs = tuple(k + g.astype(jnp.float32) for k, g in zip(kept, got))
    dp_bits = dp_n.bit_length() - 1
    assert 1 << dp_bits == dp_n
    for step in range(dp_bits):
        perm = [(member, member ^ (1 << step)) for member in range(dp_n)]
        mine = tuple(acc.astype(jnp.bfloat16) for acc in accs)
        got = lax.ppermute(mine, "dp", perm)
        accs = tuple(m.astype(jnp.float32) + g.astype(jnp.float32) for m, g in zip(mine, got))
    return accs

def on_device(first_query, first_key, first_value, out_weight, norm_gain, joint_weight, upstream):
    batches, local_rows, columns, feature = first_query.shape
    head_count = feature // HEAD_DIM
    model_width = out_weight.shape[1]
    groups = batches * local_rows

    def to_heads(tensor):
        return tensor.reshape(groups, columns, head_count, HEAD_DIM)

    out_first, probs_first = attend(
        to_heads(first_query), to_heads(first_key), to_heads(first_value), "glhe", "ghlm"
    )
    flat_first = out_first.reshape(groups * columns, feature)
    hidden = jnp.dot(flat_first, out_weight, preferred_element_type=jnp.float32)
    inverse = lax.rsqrt(jnp.mean(hidden * hidden, axis=-1, keepdims=True) + epsilon)
    normed = (hidden * inverse * norm_gain).astype(jnp.bfloat16)
    normed_cols = lax.all_to_all(
        normed.reshape(batches, local_rows, columns, model_width),
        "seq",
        split_axis=2,
        concat_axis=1,
        tiled=True,
    )
    joint_flat = jnp.dot(
        normed_cols.reshape(-1, model_width), joint_weight, preferred_element_type=jnp.float32
    )
    joint_cols = joint_flat.astype(jnp.bfloat16).reshape(
        batches, normed_cols.shape[1], normed_cols.shape[2], 3 * feature
    )
    all_rows, col_share = (joint_cols.shape[1], joint_cols.shape[2])
    pieces = joint_cols.reshape(batches, all_rows, col_share, 3, head_count, HEAD_DIM)
    query_cols, key_cols, value_cols = (pieces[:, :, :, 0], pieces[:, :, :, 1], pieces[:, :, :, 2])
    out_cols, probs_cols = attend(query_cols, key_cols, value_cols, "blche", "bchlm")
    column_out = lax.all_to_all(
        out_cols.reshape(batches, all_rows, col_share, feature),
        "seq",
        split_axis=1,
        concat_axis=2,
        tiled=True,
    )
    upstream_cols = lax.all_to_all(upstream, "seq", split_axis=2, concat_axis=1, tiled=True)
    upstream_cols = upstream_cols.reshape(batches, all_rows, col_share, head_count, HEAD_DIM)
    grads_cols = attend_back(
        query_cols, key_cols, value_cols, probs_cols, upstream_cols, "blche", "bchlm"
    )
    stacked = jnp.stack(grads_cols, axis=3).reshape(batches, all_rows, col_share, 3 * feature)
    used_normed = normed_cols.reshape(-1, model_width)
    used_grads = stacked.reshape(-1, 3 * feature)
    grad_local = jnp.dot(used_grads, joint_weight.T, preferred_element_type=jnp.float32).astype(
        jnp.bfloat16
    )
    grad_normed = lax.all_to_all(
        grad_local.reshape(batches, all_rows, col_share, model_width),
        "seq",
        split_axis=1,
        concat_axis=2,
        tiled=True,
    )
    grad_normed = grad_normed.reshape(-1, model_width)
    seq_n = lax.axis_size("seq")
    dp_n = lax.axis_size("dp")
    orders = split_orders(seq_n)
    core_odd = lax.axis_index("seq") % 2 == 1
    joint_term = jnp.dot(
        by_split_order(used_normed, orders, core_odd, seq_n).T,
        used_grads,
        preferred_element_type=jnp.float32,
    )
    grad_float = grad_normed.astype(jnp.float32)
    gain_term = jnp.sum(grad_float * hidden * inverse, axis=0)
    scaled = norm_gain * grad_float
    grad_hidden = (
        inverse * scaled - hidden * inverse**3 * jnp.mean(scaled * hidden, axis=-1, keepdims=True)
    ).astype(jnp.bfloat16)
    out_term = jnp.dot(
        by_split_order(flat_first, orders, core_odd, seq_n).T,
        grad_hidden,
        preferred_element_type=jnp.float32,
    )
    gain_term = by_split_order(gain_term[None, :], orders, core_odd, seq_n)[0][:, None]
    joint_sum, out_sum, gain_sum = reduce_rows((joint_term, out_term, gain_term), orders, seq_n, dp_n)
    replicas = (joint_sum, out_sum, gain_sum[:, 0])
    grad_first = jnp.dot(grad_hidden, out_weight.T, preferred_element_type=jnp.float32).astype(
        jnp.bfloat16
    )
    grads_rows = attend_back(
        to_heads(first_query),
        to_heads(first_key),
        to_heads(first_value),
        probs_first,
        to_heads(grad_first),
        "glhe",
        "ghlm",
    )
    grad_query = grads_rows[0].reshape(batches, local_rows, columns, feature)
    grad_key = grads_rows[1].reshape(batches, local_rows, columns, feature)
    grad_value = grads_rows[2].reshape(batches, local_rows, columns, feature)
    return (
        grad_query,
        grad_key,
        grad_value,
        column_out,
        replicas[0].astype(jnp.bfloat16),
        replicas[1].astype(jnp.bfloat16),
        replicas[2],
    )


def solution(mesh):
    placed = (
        P("dp", "seq", None, None),
        P("dp", "seq", None, None),
        P("dp", "seq", None, None),
        P(),
        P(),
        P(),
        P("dp", "seq", None, None),
    )
    return jax.shard_map(
        on_device,
        mesh=mesh,
        in_specs=placed,
        out_specs=(
            P("dp", "seq", None, None),
            P("dp", "seq", None, None),
            P("dp", "seq", None, None),
            P("dp", "seq", None, None),
            P("seq", None),
            P("seq", None),
            P("seq"),
        ),
        check_vma=False,
    )
```

```python
import jax
import jax.numpy as jnp
from jax import lax
from jax.sharding import PartitionSpec as P

HEAD_DIM = 128


epsilon = 1e-06


def attend(queries, key_table, values, layout, scores_form):
    keyed = layout.replace("l", "m")
    scaling = HEAD_DIM ** (-0.5)
    scores = (
        jnp.einsum(
            layout + "," + keyed + "->" + scores_form,
            queries,
            key_table,
            preferred_element_type=jnp.float32,
        )
        * scaling
    )
    extent = scores.shape[-1]
    causal = jnp.arange(extent)[:, None] >= jnp.arange(extent)[None, :]
    scores = jnp.where(causal, scores, -1e30)
    peak = jnp.max(scores, axis=-1, keepdims=True)
    weights = jnp.exp(scores - peak)
    prob_table = weights / jnp.sum(weights, axis=-1, keepdims=True)
    rounded = prob_table.astype(jnp.bfloat16)
    output = jnp.einsum(
        scores_form + "," + keyed + "->" + layout,
        rounded,
        values,
        preferred_element_type=jnp.float32,
    )
    return (output.astype(jnp.bfloat16), prob_table)


def attend_back(queries, key_table, values, prob_table, upstream_part, layout, scores_form):
    keyed = layout.replace("l", "m")
    scaling = HEAD_DIM ** (-0.5)
    grad_prob = jnp.einsum(
        layout + "," + keyed + "->" + scores_form,
        upstream_part,
        values,
        preferred_element_type=jnp.float32,
    )
    row_inner = jnp.sum(prob_table * grad_prob, axis=-1, keepdims=True)
    grad_score = (prob_table * (grad_prob - row_inner) * scaling).astype(jnp.bfloat16)
    grad_query = jnp.einsum(
        scores_form + "," + keyed + "->" + layout,
        grad_score,
        key_table,
        preferred_element_type=jnp.float32,
    )
    grad_key = jnp.einsum(
        scores_form + "," + layout + "->" + keyed,
        grad_score,
        queries,
        preferred_element_type=jnp.float32,
    )
    rounded = prob_table.astype(jnp.bfloat16)
    grad_value = jnp.einsum(
        scores_form + "," + layout + "->" + keyed,
        rounded,
        upstream_part,
        preferred_element_type=jnp.float32,
    )
    return (
        grad_query.astype(jnp.bfloat16),
        grad_key.astype(jnp.bfloat16),
        grad_value.astype(jnp.bfloat16),
    )


def split_orders(seq_n):
    bits = seq_n.bit_length() - 1
    assert 1 << bits == seq_n
    even = list(range(bits))
    odd = list(even)
    if bits >= 3:
        odd[1], odd[2] = odd[2], odd[1]
    return even, odd


def by_split_order(matrix, orders, core_odd, seq_n):
    bits = seq_n.bit_length() - 1
    lead = matrix.shape[0]
    block = matrix.shape[1] // seq_n
    grid = matrix.reshape((lead,) + (2,) * bits + (matrix.shape[1] // seq_n,))

    def arrange(order):
        axes = (0,) + tuple(1 + (bits - 1 - bit) for bit in order) + (bits + 1,)
        return jnp.transpose(grid, axes).reshape(lead, seq_n * block)

    even, odd = orders
    if even == odd:
        return arrange(even)
    return jnp.where(core_odd, arrange(odd), arrange(even))


def reduce_rows(parts, orders, seq_n, dp_n):
    bits = seq_n.bit_length() - 1
    index = lax.axis_index("seq")
    accs = tuple(p.reshape((2,) * (bits - 1) + (2 * p.shape[0] // seq_n, p.shape[1])) for p in parts)
    even, odd = orders
    for step in range(1, bits):
        perm = []
        for member in range(seq_n):
            bit = (odd if member % 2 else even)[step]
            perm.append((member, member ^ (1 << bit)))
        bit_even, bit_odd = even[step], odd[step]
        keep_even = (index // (1 << bit_even)) % 2
        keep_odd = (index // (1 << bit_odd)) % 2
        keep_at = jnp.where(index % 2 == 1, keep_odd, keep_even)
        kept = tuple(lax.dynamic_index_in_dim(acc, keep_at, 0, keepdims=False) for acc in accs)
        given = tuple(
            lax.dynamic_index_in_dim(acc, 1 - keep_at, 0, keepdims=False).astype(jnp.bfloat16)
            for acc in accs
        )
        got = lax.ppermute(given, "seq", perm)
        accs = tuple(k + g.astype(jnp.float32) for k, g in zip(kept, got))
    dp_bits = dp_n.bit_length() - 1
    assert 1 << dp_bits == dp_n
    for step in range(dp_bits):
        perm = [(member, member ^ (1 << step)) for member in range(dp_n)]
        mine = tuple(acc.astype(jnp.bfloat16) for acc in accs)
        got = lax.ppermute(mine, "dp", perm)
        accs = tuple(m.astype(jnp.float32) + g.astype(jnp.float32) for m, g in zip(mine, got))
    return accs

def on_device(first_query, first_key, first_value, out_weight, norm_gain, joint_weight, upstream):
    batches, local_rows, columns, feature = first_query.shape
    head_count = feature // HEAD_DIM
    model_width = out_weight.shape[1]
    groups = batches * local_rows

    def to_heads(tensor):
        return tensor.reshape(groups, columns, head_count, HEAD_DIM)

    out_first, probs_first = attend(
        to_heads(first_query), to_heads(first_key), to_heads(first_value), "glhe", "ghlm"
    )
    flat_first = out_first.reshape(groups * columns, feature)
    hidden = jnp.dot(flat_first, out_weight, preferred_element_type=jnp.float32)
    inverse = lax.rsqrt(jnp.mean(hidden * hidden, axis=-1, keepdims=True) + epsilon)
    normed = (hidden * inverse * norm_gain).astype(jnp.bfloat16)
    normed_cols = lax.all_to_all(
        normed.reshape(batches, local_rows, columns, model_width),
        "seq",
        split_axis=2,
        concat_axis=1,
        tiled=True,
    )
    joint_flat = jnp.dot(
        normed_cols.reshape(-1, model_width), joint_weight, preferred_element_type=jnp.float32
    )
    joint_cols = joint_flat.astype(jnp.bfloat16).reshape(
        batches, normed_cols.shape[1], normed_cols.shape[2], 3 * feature
    )
    all_rows, col_share = (joint_cols.shape[1], joint_cols.shape[2])
    pieces = joint_cols.reshape(batches, all_rows, col_share, 3, head_count, HEAD_DIM)
    query_cols, key_cols, value_cols = (pieces[:, :, :, 0], pieces[:, :, :, 1], pieces[:, :, :, 2])
    out_cols, probs_cols = attend(query_cols, key_cols, value_cols, "blche", "bchlm")
    column_out = lax.all_to_all(
        out_cols.reshape(batches, all_rows, col_share, feature),
        "seq",
        split_axis=1,
        concat_axis=2,
        tiled=True,
    )
    upstream_cols = lax.all_to_all(upstream, "seq", split_axis=2, concat_axis=1, tiled=True)
    upstream_cols = upstream_cols.reshape(batches, all_rows, col_share, head_count, HEAD_DIM)
    grads_cols = attend_back(
        query_cols, key_cols, value_cols, probs_cols, upstream_cols, "blche", "bchlm"
    )
    stacked = jnp.stack(grads_cols, axis=3).reshape(batches, all_rows, col_share, 3 * feature)
    used_normed = normed_cols.reshape(-1, model_width)
    used_grads = stacked.reshape(-1, 3 * feature)
    grad_local = jnp.dot(used_grads, joint_weight.T, preferred_element_type=jnp.float32).astype(
        jnp.bfloat16
    )
    grad_normed = lax.all_to_all(
        grad_local.reshape(batches, all_rows, col_share, model_width),
        "seq",
        split_axis=1,
        concat_axis=2,
        tiled=True,
    )
    grad_normed = grad_normed.reshape(-1, model_width)
    seq_n = lax.axis_size("seq")
    dp_n = lax.axis_size("dp")
    orders = split_orders(seq_n)
    core_odd = lax.axis_index("seq") % 2 == 1
    pair = [(member, member ^ 1) for member in range(seq_n)]
    core = lax.axis_index("seq") % 2

    def my_half(factor):
        arranged = by_split_order(factor, orders, core_odd, seq_n)
        half = arranged.shape[1] // 2
        return lax.dynamic_slice_in_dim(arranged, core * half, half, axis=1)

    normed_peer, grads_peer = lax.ppermute((used_normed, used_grads), "seq", pair)
    joint_term = jnp.dot(
        my_half(jnp.concatenate([used_normed, normed_peer], axis=0)).T,
        jnp.concatenate([used_grads, grads_peer], axis=0),
        preferred_element_type=jnp.float32,
    )
    grad_float = grad_normed.astype(jnp.float32)
    gain_term = jnp.sum(grad_float * hidden * inverse, axis=0)
    scaled = norm_gain * grad_float
    grad_hidden = (
        inverse * scaled - hidden * inverse**3 * jnp.mean(scaled * hidden, axis=-1, keepdims=True)
    ).astype(jnp.bfloat16)
    first_peer, hidden_peer, gain_peer = lax.ppermute((flat_first, grad_hidden, gain_term), "seq", pair)
    out_term = jnp.dot(
        my_half(jnp.concatenate([flat_first, first_peer], axis=0)).T,
        jnp.concatenate([grad_hidden, hidden_peer], axis=0),
        preferred_element_type=jnp.float32,
    )
    gain_term = my_half((gain_term + gain_peer)[None, :])[0][:, None]
    joint_sum, out_sum, gain_sum = reduce_rows((joint_term, out_term, gain_term), orders, seq_n, dp_n)
    replicas = (joint_sum, out_sum, gain_sum[:, 0])
    grad_first = jnp.dot(grad_hidden, out_weight.T, preferred_element_type=jnp.float32).astype(
        jnp.bfloat16
    )
    grads_rows = attend_back(
        to_heads(first_query),
        to_heads(first_key),
        to_heads(first_value),
        probs_first,
        to_heads(grad_first),
        "glhe",
        "ghlm",
    )
    grad_query = grads_rows[0].reshape(batches, local_rows, columns, feature)
    grad_key = grads_rows[1].reshape(batches, local_rows, columns, feature)
    grad_value = grads_rows[2].reshape(batches, local_rows, columns, feature)
    return (
        grad_query,
        grad_key,
        grad_value,
        column_out,
        replicas[0].astype(jnp.bfloat16),
        replicas[1].astype(jnp.bfloat16),
        replicas[2],
    )


def solution(mesh):
    placed = (
        P("dp", "seq", None, None),
        P("dp", "seq", None, None),
        P("dp", "seq", None, None),
        P(),
        P(),
        P(),
        P("dp", "seq", None, None),
    )
    return jax.shard_map(
        on_device,
        mesh=mesh,
        in_specs=placed,
        out_specs=(
            P("dp", "seq", None, None),
            P("dp", "seq", None, None),
            P("dp", "seq", None, None),
            P("dp", "seq", None, None),
            P("seq", None),
            P("seq", None),
            P("seq"),
        ),
        check_vma=False,
    )
```

```python
import jax
import jax.numpy as jnp
from jax import lax
from jax.sharding import PartitionSpec as P

HEAD_DIM = 128


epsilon = 1e-06


def attend(queries, key_table, values, layout, scores_form):
    keyed = layout.replace("l", "m")
    scaling = HEAD_DIM ** (-0.5)
    scores = (
        jnp.einsum(
            layout + "," + keyed + "->" + scores_form,
            queries,
            key_table,
            preferred_element_type=jnp.float32,
        )
        * scaling
    )
    extent = scores.shape[-1]
    causal = jnp.arange(extent)[:, None] >= jnp.arange(extent)[None, :]
    scores = jnp.where(causal, scores, -1e30)
    peak = jnp.max(scores, axis=-1, keepdims=True)
    weights = jnp.exp(scores - peak)
    prob_table = weights / jnp.sum(weights, axis=-1, keepdims=True)
    rounded = prob_table.astype(jnp.bfloat16)
    output = jnp.einsum(
        scores_form + "," + keyed + "->" + layout,
        rounded,
        values,
        preferred_element_type=jnp.float32,
    )
    return (output.astype(jnp.bfloat16), prob_table)


def attend_back(queries, key_table, values, prob_table, upstream_part, layout, scores_form):
    keyed = layout.replace("l", "m")
    scaling = HEAD_DIM ** (-0.5)
    grad_prob = jnp.einsum(
        layout + "," + keyed + "->" + scores_form,
        upstream_part,
        values,
        preferred_element_type=jnp.float32,
    )
    row_inner = jnp.sum(prob_table * grad_prob, axis=-1, keepdims=True)
    grad_score = (prob_table * (grad_prob - row_inner) * scaling).astype(jnp.bfloat16)
    grad_query = jnp.einsum(
        scores_form + "," + keyed + "->" + layout,
        grad_score,
        key_table,
        preferred_element_type=jnp.float32,
    )
    grad_key = jnp.einsum(
        scores_form + "," + layout + "->" + keyed,
        grad_score,
        queries,
        preferred_element_type=jnp.float32,
    )
    rounded = prob_table.astype(jnp.bfloat16)
    grad_value = jnp.einsum(
        scores_form + "," + layout + "->" + keyed,
        rounded,
        upstream_part,
        preferred_element_type=jnp.float32,
    )
    return (
        grad_query.astype(jnp.bfloat16),
        grad_key.astype(jnp.bfloat16),
        grad_value.astype(jnp.bfloat16),
    )


def split_orders(seq_n):
    bits = seq_n.bit_length() - 1
    assert 1 << bits == seq_n
    even = list(range(bits))
    odd = list(even)
    if bits >= 3:
        odd[1], odd[2] = odd[2], odd[1]
    return even, odd


def by_split_order(matrix, orders, core_odd, seq_n):
    bits = seq_n.bit_length() - 1
    lead = matrix.shape[0]
    block = matrix.shape[1] // seq_n
    grid = matrix.reshape((lead,) + (2,) * bits + (matrix.shape[1] // seq_n,))

    def arrange(order):
        axes = (0,) + tuple(1 + (bits - 1 - bit) for bit in order) + (bits + 1,)
        return jnp.transpose(grid, axes).reshape(lead, seq_n * block)

    even, odd = orders
    if even == odd:
        return arrange(even)
    return jnp.where(core_odd, arrange(odd), arrange(even))


def reduce_rows(parts, orders, seq_n, dp_n):
    bits = seq_n.bit_length() - 1
    index = lax.axis_index("seq")
    accs = tuple(p.reshape((2,) * (bits - 1) + (2 * p.shape[0] // seq_n, p.shape[1])) for p in parts)
    even, odd = orders
    for step in range(1, bits):
        perm = []
        for member in range(seq_n):
            bit = (odd if member % 2 else even)[step]
            perm.append((member, member ^ (1 << bit)))
        bit_even, bit_odd = even[step], odd[step]
        keep_even = (index // (1 << bit_even)) % 2
        keep_odd = (index // (1 << bit_odd)) % 2
        keep_at = jnp.where(index % 2 == 1, keep_odd, keep_even)
        kept = tuple(lax.dynamic_index_in_dim(acc, keep_at, 0, keepdims=False) for acc in accs)
        given = tuple(
            lax.dynamic_index_in_dim(acc, 1 - keep_at, 0, keepdims=False).astype(jnp.bfloat16)
            for acc in accs
        )
        got = lax.ppermute(given, "seq", perm)
        accs = tuple(k + g.astype(jnp.float32) for k, g in zip(kept, got))
    dp_bits = dp_n.bit_length() - 1
    assert 1 << dp_bits == dp_n
    for step in range(dp_bits):
        perm = [(member, member ^ (1 << step)) for member in range(dp_n)]
        mine = tuple(acc.astype(jnp.bfloat16) for acc in accs)
        got = lax.ppermute(mine, "dp", perm)
        accs = tuple(m.astype(jnp.float32) + g.astype(jnp.float32) for m, g in zip(mine, got))
    return accs

def on_device(first_query, first_key, first_value, out_weight, norm_gain, joint_weight, upstream):
    batches, local_rows, columns, feature = first_query.shape
    head_count = feature // HEAD_DIM
    model_width = out_weight.shape[1]
    groups = batches * local_rows

    def to_heads(tensor):
        return tensor.reshape(groups, columns, head_count, HEAD_DIM)

    out_first, probs_first = attend(
        to_heads(first_query), to_heads(first_key), to_heads(first_value), "glhe", "ghlm"
    )
    flat_first = out_first.reshape(groups * columns, feature)
    hidden = jnp.dot(flat_first, out_weight, preferred_element_type=jnp.float32)
    inverse = lax.rsqrt(jnp.mean(hidden * hidden, axis=-1, keepdims=True) + epsilon)
    normed = (hidden * inverse * norm_gain).astype(jnp.bfloat16)
    normed_cols = lax.all_to_all(
        normed.reshape(batches, local_rows, columns, model_width),
        "seq",
        split_axis=2,
        concat_axis=1,
        tiled=True,
    )
    joint_flat = jnp.dot(
        normed_cols.reshape(-1, model_width), joint_weight, preferred_element_type=jnp.float32
    )
    joint_cols = joint_flat.astype(jnp.bfloat16).reshape(
        batches, normed_cols.shape[1], normed_cols.shape[2], 3 * feature
    )
    all_rows, col_share = (joint_cols.shape[1], joint_cols.shape[2])
    pieces = joint_cols.reshape(batches, all_rows, col_share, 3, head_count, HEAD_DIM)
    query_cols, key_cols, value_cols = (pieces[:, :, :, 0], pieces[:, :, :, 1], pieces[:, :, :, 2])
    out_cols, probs_cols = attend(query_cols, key_cols, value_cols, "blche", "bchlm")
    column_out = lax.all_to_all(
        out_cols.reshape(batches, all_rows, col_share, feature),
        "seq",
        split_axis=1,
        concat_axis=2,
        tiled=True,
    )
    upstream_cols = lax.all_to_all(upstream, "seq", split_axis=2, concat_axis=1, tiled=True)
    upstream_cols = upstream_cols.reshape(batches, all_rows, col_share, head_count, HEAD_DIM)
    grads_cols = attend_back(
        query_cols, key_cols, value_cols, probs_cols, upstream_cols, "blche", "bchlm"
    )
    stacked = jnp.stack(grads_cols, axis=3).reshape(batches, all_rows, col_share, 3 * feature)
    used_normed = normed_cols.reshape(-1, model_width)
    used_grads = stacked.reshape(-1, 3 * feature)
    grad_local = jnp.dot(used_grads, joint_weight.T, preferred_element_type=jnp.float32).astype(
        jnp.bfloat16
    )
    seq_n = lax.axis_size("seq")
    dp_n = lax.axis_size("dp")
    orders = split_orders(seq_n)
    core_odd = lax.axis_index("seq") % 2 == 1
    pair = [(member, member ^ 1) for member in range(seq_n)]
    core = lax.axis_index("seq") % 2

    def my_half(factor):
        arranged = by_split_order(factor, orders, core_odd, seq_n)
        half = arranged.shape[1] // 2
        return lax.dynamic_slice_in_dim(arranged, core * half, half, axis=1)

    normed_peer, grads_peer = lax.ppermute((used_normed, used_grads), "seq", pair)
    joint_term = jnp.dot(
        my_half(jnp.concatenate([used_normed, normed_peer], axis=0)).T,
        jnp.concatenate([used_grads, grads_peer], axis=0),
        preferred_element_type=jnp.float32,
    )
    grad_normed = lax.all_to_all(
        grad_local.reshape(batches, all_rows, col_share, model_width),
        "seq",
        split_axis=1,
        concat_axis=2,
        tiled=True,
    )
    grad_normed = grad_normed.reshape(-1, model_width)
    joint_term, grad_normed = lax.optimization_barrier((joint_term, grad_normed))
    grad_float = grad_normed.astype(jnp.float32)
    gain_term = jnp.sum(grad_float * hidden * inverse, axis=0)
    scaled = norm_gain * grad_float
    grad_hidden = (
        inverse * scaled - hidden * inverse**3 * jnp.mean(scaled * hidden, axis=-1, keepdims=True)
    ).astype(jnp.bfloat16)
    first_peer, hidden_peer, gain_peer = lax.ppermute((flat_first, grad_hidden, gain_term), "seq", pair)
    out_term = jnp.dot(
        my_half(jnp.concatenate([flat_first, first_peer], axis=0)).T,
        jnp.concatenate([grad_hidden, hidden_peer], axis=0),
        preferred_element_type=jnp.float32,
    )
    gain_term = my_half((gain_term + gain_peer)[None, :])[0][:, None]
    out_width = out_term.shape[1]
    joint_sum, out_sum = reduce_rows(
        (joint_term, jnp.concatenate([out_term, gain_term], axis=1)), orders, seq_n, dp_n
    )
    replicas = (joint_sum, out_sum[:, :out_width], out_sum[:, out_width])
    grad_first = jnp.dot(grad_hidden, out_weight.T, preferred_element_type=jnp.float32).astype(
        jnp.bfloat16
    )
    grads_rows = attend_back(
        to_heads(first_query),
        to_heads(first_key),
        to_heads(first_value),
        probs_first,
        to_heads(grad_first),
        "glhe",
        "ghlm",
    )
    grad_query = grads_rows[0].reshape(batches, local_rows, columns, feature)
    grad_key = grads_rows[1].reshape(batches, local_rows, columns, feature)
    grad_value = grads_rows[2].reshape(batches, local_rows, columns, feature)
    return (
        grad_query,
        grad_key,
        grad_value,
        column_out,
        replicas[0].astype(jnp.bfloat16),
        replicas[1].astype(jnp.bfloat16),
        replicas[2],
    )


def solution(mesh):
    placed = (
        P("dp", "seq", None, None),
        P("dp", "seq", None, None),
        P("dp", "seq", None, None),
        P(),
        P(),
        P(),
        P("dp", "seq", None, None),
    )
    return jax.shard_map(
        on_device,
        mesh=mesh,
        in_specs=placed,
        out_specs=(
            P("dp", "seq", None, None),
            P("dp", "seq", None, None),
            P("dp", "seq", None, None),
            P("dp", "seq", None, None),
            P("seq", None),
            P("seq", None),
            P("seq"),
        ),
        check_vma=False,
    )
```

```python
import jax
import jax.numpy as jnp
from jax import lax
from jax.sharding import PartitionSpec as P

HEAD_DIM = 128


epsilon = 1e-06


def attend(queries, key_table, values, layout, scores_form):
    keyed = layout.replace("l", "m")
    scaling = HEAD_DIM ** (-0.5)
    scores = (
        jnp.einsum(
            layout + "," + keyed + "->" + scores_form,
            queries,
            key_table,
            preferred_element_type=jnp.float32,
        )
        * scaling
    )
    extent = scores.shape[-1]
    causal = jnp.arange(extent)[:, None] >= jnp.arange(extent)[None, :]
    scores = jnp.where(causal, scores, -1e30)
    peak = jnp.max(scores, axis=-1, keepdims=True)
    weights = jnp.exp(scores - peak)
    prob_table = weights / jnp.sum(weights, axis=-1, keepdims=True)
    rounded = prob_table.astype(jnp.bfloat16)
    output = jnp.einsum(
        scores_form + "," + keyed + "->" + layout,
        rounded,
        values,
        preferred_element_type=jnp.float32,
    )
    return (output.astype(jnp.bfloat16), prob_table)


def attend_back(queries, key_table, values, prob_table, upstream_part, layout, scores_form):
    keyed = layout.replace("l", "m")
    scaling = HEAD_DIM ** (-0.5)
    grad_prob = jnp.einsum(
        layout + "," + keyed + "->" + scores_form,
        upstream_part,
        values,
        preferred_element_type=jnp.float32,
    )
    row_inner = jnp.sum(prob_table * grad_prob, axis=-1, keepdims=True)
    grad_score = (prob_table * (grad_prob - row_inner) * scaling).astype(jnp.bfloat16)
    grad_query = jnp.einsum(
        scores_form + "," + keyed + "->" + layout,
        grad_score,
        key_table,
        preferred_element_type=jnp.float32,
    )
    grad_key = jnp.einsum(
        scores_form + "," + layout + "->" + keyed,
        grad_score,
        queries,
        preferred_element_type=jnp.float32,
    )
    rounded = prob_table.astype(jnp.bfloat16)
    grad_value = jnp.einsum(
        scores_form + "," + layout + "->" + keyed,
        rounded,
        upstream_part,
        preferred_element_type=jnp.float32,
    )
    return (
        grad_query.astype(jnp.bfloat16),
        grad_key.astype(jnp.bfloat16),
        grad_value.astype(jnp.bfloat16),
    )


def split_orders(seq_n, dp_n):
    bits = seq_n.bit_length() - 1
    dp_bits = dp_n.bit_length() - 1
    assert 1 << bits == seq_n and 1 << dp_bits == dp_n and bits >= 1
    seq_rest = [("s", k) for k in range(1, bits)]
    dp_all = [("d", k) for k in range(dp_bits)]
    even = seq_rest[:1] + dp_all[:1] + seq_rest[1:] + dp_all[1:]
    odd = list(even)
    if bits >= 3 and dp_bits >= 1:
        odd = dp_all[:1] + [seq_rest[1], seq_rest[0]] + seq_rest[2:] + dp_all[1:]
    assert sorted(even) == sorted(odd)
    return even, odd


def by_split_order(matrix, orders, core_odd, seq_n, dp_n):
    bits = seq_n.bit_length() - 1
    dp_bits = dp_n.bit_length() - 1
    lead = matrix.shape[0]
    sub = matrix.shape[1] // (seq_n * dp_n)
    grid = matrix.reshape((lead,) + (2,) * (bits + dp_bits) + (sub,))

    def axis_of(item):
        kind, k = item
        return 1 + (bits - 1 - k) if kind == "s" else 1 + bits + (dp_bits - 1 - k)

    def arrange(order):
        axes = (0, axis_of(("s", 0))) + tuple(axis_of(item) for item in order) + (bits + dp_bits + 1,)
        return jnp.transpose(grid, axes).reshape(matrix.shape)

    even, odd = orders
    if even == odd:
        return arrange(even)
    return jnp.where(core_odd, arrange(odd), arrange(even))


def reduce_rows(parts, orders, seq_n, dp_n):
    seq_at = lax.axis_index("seq")
    dp_at = lax.axis_index("dp")
    even, odd = orders
    steps = len(even)
    accs = tuple(p.reshape((2,) * steps + (p.shape[0] >> steps, p.shape[1])) for p in parts)

    def bit_value(item, seq_i, dp_i):
        kind, k = item
        return ((seq_i if kind == "s" else dp_i) >> k) & 1

    def flip(item, seq_i, dp_i):
        kind, k = item
        if kind == "s":
            return seq_i ^ (1 << k), dp_i
        return seq_i, dp_i ^ (1 << k)

    for step in range(steps):
        perm = []
        for dp_i in range(dp_n):
            for seq_i in range(seq_n):
                item = (odd if seq_i % 2 else even)[step]
                seq_j, dp_j = flip(item, seq_i, dp_i)
                perm.append((dp_i * seq_n + seq_i, dp_j * seq_n + seq_j))

        def traced_bit(item):
            kind, k = item
            return ((seq_at if kind == "s" else dp_at) // (1 << k)) % 2

        keep_at = jnp.where(seq_at % 2 == 1, traced_bit(odd[step]), traced_bit(even[step]))
        kept = tuple(lax.dynamic_index_in_dim(acc, keep_at, 0, keepdims=False) for acc in accs)
        given = tuple(
            lax.dynamic_index_in_dim(acc, 1 - keep_at, 0, keepdims=False).astype(jnp.bfloat16)
            for acc in accs
        )
        got = lax.ppermute(given, ("dp", "seq"), perm)
        accs = tuple(k + g.astype(jnp.float32) for k, g in zip(kept, got))
    accs = tuple(acc.astype(jnp.bfloat16) for acc in accs)
    for step in range(dp_n.bit_length() - 1):
        perm = [(member, member ^ (1 << step)) for member in range(dp_n)]
        got = lax.ppermute(accs, "dp", perm)
        upper = (dp_at // (1 << step)) % 2 == 1
        accs = tuple(
            jnp.where(upper, jnp.concatenate([g, acc], axis=0), jnp.concatenate([acc, g], axis=0))
            for acc, g in zip(accs, got)
        )
    return accs


def on_device(first_query, first_key, first_value, out_weight, norm_gain, joint_weight, upstream):
    batches, local_rows, columns, feature = first_query.shape
    head_count = feature // HEAD_DIM
    model_width = out_weight.shape[1]
    groups = batches * local_rows

    def to_heads(tensor):
        return tensor.reshape(groups, columns, head_count, HEAD_DIM)

    out_first, probs_first = attend(
        to_heads(first_query), to_heads(first_key), to_heads(first_value), "glhe", "ghlm"
    )
    flat_first = out_first.reshape(groups * columns, feature)
    hidden = jnp.dot(flat_first, out_weight, preferred_element_type=jnp.float32)
    inverse = lax.rsqrt(jnp.mean(hidden * hidden, axis=-1, keepdims=True) + epsilon)
    normed = (hidden * inverse * norm_gain).astype(jnp.bfloat16)
    normed_cols = lax.all_to_all(
        normed.reshape(batches, local_rows, columns, model_width),
        "seq",
        split_axis=2,
        concat_axis=1,
        tiled=True,
    )
    joint_flat = jnp.dot(
        normed_cols.reshape(-1, model_width), joint_weight, preferred_element_type=jnp.float32
    )
    joint_cols = joint_flat.astype(jnp.bfloat16).reshape(
        batches, normed_cols.shape[1], normed_cols.shape[2], 3 * feature
    )
    all_rows, col_share = (joint_cols.shape[1], joint_cols.shape[2])
    pieces = joint_cols.reshape(batches, all_rows, col_share, 3, head_count, HEAD_DIM)
    query_cols, key_cols, value_cols = (pieces[:, :, :, 0], pieces[:, :, :, 1], pieces[:, :, :, 2])
    out_cols, probs_cols = attend(query_cols, key_cols, value_cols, "blche", "bchlm")
    column_out = lax.all_to_all(
        out_cols.reshape(batches, all_rows, col_share, feature),
        "seq",
        split_axis=1,
        concat_axis=2,
        tiled=True,
    )
    upstream_cols = lax.all_to_all(upstream, "seq", split_axis=2, concat_axis=1, tiled=True)
    upstream_cols = upstream_cols.reshape(batches, all_rows, col_share, head_count, HEAD_DIM)
    grads_cols = attend_back(
        query_cols, key_cols, value_cols, probs_cols, upstream_cols, "blche", "bchlm"
    )
    stacked = jnp.stack(grads_cols, axis=3).reshape(batches, all_rows, col_share, 3 * feature)
    used_normed = normed_cols.reshape(-1, model_width)
    used_grads = stacked.reshape(-1, 3 * feature)
    grad_local = jnp.dot(used_grads, joint_weight.T, preferred_element_type=jnp.float32).astype(
        jnp.bfloat16
    )
    seq_n = lax.axis_size("seq")
    dp_n = lax.axis_size("dp")
    orders = split_orders(seq_n, dp_n)
    core_odd = lax.axis_index("seq") % 2 == 1
    pair = [(member, member ^ 1) for member in range(seq_n)]
    core = lax.axis_index("seq") % 2

    def my_half(factor):
        arranged = by_split_order(factor, orders, core_odd, seq_n, dp_n)
        half = arranged.shape[1] // 2
        return lax.dynamic_slice_in_dim(arranged, core * half, half, axis=1)

    normed_peer, grads_peer = lax.ppermute((used_normed, used_grads), "seq", pair)
    joint_term = jnp.dot(
        my_half(jnp.concatenate([used_normed, normed_peer], axis=0)).T,
        jnp.concatenate([used_grads, grads_peer], axis=0),
        preferred_element_type=jnp.float32,
    )
    grad_normed = lax.all_to_all(
        grad_local.reshape(batches, all_rows, col_share, model_width),
        "seq",
        split_axis=1,
        concat_axis=2,
        tiled=True,
    )
    grad_normed = grad_normed.reshape(-1, model_width)
    joint_term, grad_normed = lax.optimization_barrier((joint_term, grad_normed))
    grad_float = grad_normed.astype(jnp.float32)
    gain_term = jnp.sum(grad_float * hidden * inverse, axis=0)
    scaled = norm_gain * grad_float
    grad_hidden = (
        inverse * scaled - hidden * inverse**3 * jnp.mean(scaled * hidden, axis=-1, keepdims=True)
    ).astype(jnp.bfloat16)
    first_peer, hidden_peer, gain_peer = lax.ppermute((flat_first, grad_hidden, gain_term), "seq", pair)
    out_term = jnp.dot(
        my_half(jnp.concatenate([flat_first, first_peer], axis=0)).T,
        jnp.concatenate([grad_hidden, hidden_peer], axis=0),
        preferred_element_type=jnp.float32,
    )
    gain_term = my_half((gain_term + gain_peer)[None, :])[0][:, None]
    out_width = out_term.shape[1]
    joint_sum, out_sum = reduce_rows(
        (joint_term, jnp.concatenate([out_term, gain_term], axis=1)), orders, seq_n, dp_n
    )
    replicas = (joint_sum, out_sum[:, :out_width], out_sum[:, out_width].astype(jnp.float32))
    grad_first = jnp.dot(grad_hidden, out_weight.T, preferred_element_type=jnp.float32).astype(
        jnp.bfloat16
    )
    grads_rows = attend_back(
        to_heads(first_query),
        to_heads(first_key),
        to_heads(first_value),
        probs_first,
        to_heads(grad_first),
        "glhe",
        "ghlm",
    )
    grad_query = grads_rows[0].reshape(batches, local_rows, columns, feature)
    grad_key = grads_rows[1].reshape(batches, local_rows, columns, feature)
    grad_value = grads_rows[2].reshape(batches, local_rows, columns, feature)
    return (
        grad_query,
        grad_key,
        grad_value,
        column_out,
        replicas[0].astype(jnp.bfloat16),
        replicas[1].astype(jnp.bfloat16),
        replicas[2],
    )


def solution(mesh):
    placed = (
        P("dp", "seq", None, None),
        P("dp", "seq", None, None),
        P("dp", "seq", None, None),
        P(),
        P(),
        P(),
        P("dp", "seq", None, None),
    )
    return jax.shard_map(
        on_device,
        mesh=mesh,
        in_specs=placed,
        out_specs=(
            P("dp", "seq", None, None),
            P("dp", "seq", None, None),
            P("dp", "seq", None, None),
            P("dp", "seq", None, None),
            P("seq", None),
            P("seq", None),
            P("seq"),
        ),
        check_vma=False,
    )
```

```python
import jax
import jax.numpy as jnp
from jax import lax
from jax.sharding import PartitionSpec as P

HEAD_DIM = 128


epsilon = 1e-06


def attend(queries, key_table, values, layout, scores_form):
    keyed = layout.replace("l", "m")
    scaling = HEAD_DIM ** (-0.5)
    scores = (
        jnp.einsum(
            layout + "," + keyed + "->" + scores_form,
            queries,
            key_table,
            preferred_element_type=jnp.float32,
        )
        * scaling
    )
    extent = scores.shape[-1]
    causal = jnp.arange(extent)[:, None] >= jnp.arange(extent)[None, :]
    scores = jnp.where(causal, scores, -1e30)
    peak = jnp.max(scores, axis=-1, keepdims=True)
    weights = jnp.exp(scores - peak)
    prob_table = weights / jnp.sum(weights, axis=-1, keepdims=True)
    rounded = prob_table.astype(jnp.bfloat16)
    output = jnp.einsum(
        scores_form + "," + keyed + "->" + layout,
        rounded,
        values,
        preferred_element_type=jnp.float32,
    )
    return (output.astype(jnp.bfloat16), prob_table)


def attend_back(queries, key_table, values, prob_table, upstream_part, layout, scores_form):
    keyed = layout.replace("l", "m")
    scaling = HEAD_DIM ** (-0.5)
    grad_prob = jnp.einsum(
        layout + "," + keyed + "->" + scores_form,
        upstream_part,
        values,
        preferred_element_type=jnp.float32,
    )
    row_inner = jnp.sum(prob_table * grad_prob, axis=-1, keepdims=True)
    grad_score = (prob_table * (grad_prob - row_inner) * scaling).astype(jnp.bfloat16)
    grad_query = jnp.einsum(
        scores_form + "," + keyed + "->" + layout,
        grad_score,
        key_table,
        preferred_element_type=jnp.float32,
    )
    grad_key = jnp.einsum(
        scores_form + "," + layout + "->" + keyed,
        grad_score,
        queries,
        preferred_element_type=jnp.float32,
    )
    rounded = prob_table.astype(jnp.bfloat16)
    grad_value = jnp.einsum(
        scores_form + "," + layout + "->" + keyed,
        rounded,
        upstream_part,
        preferred_element_type=jnp.float32,
    )
    return (
        grad_query.astype(jnp.bfloat16),
        grad_key.astype(jnp.bfloat16),
        grad_value.astype(jnp.bfloat16),
    )


def split_orders(seq_n, dp_n):
    bits = seq_n.bit_length() - 1
    dp_bits = dp_n.bit_length() - 1
    assert 1 << bits == seq_n and 1 << dp_bits == dp_n and bits >= 1
    seq_rest = [("s", k) for k in range(1, bits)]
    dp_all = [("d", k) for k in range(dp_bits)]
    even = seq_rest[:1] + dp_all[:1] + seq_rest[1:] + dp_all[1:]
    odd = list(even)
    if bits >= 3 and dp_bits >= 1:
        odd = dp_all[:1] + [seq_rest[1], seq_rest[0]] + seq_rest[2:] + dp_all[1:]
    assert sorted(even) == sorted(odd)
    return even, odd


def by_split_order(matrix, orders, core_odd, seq_n, dp_n):
    bits = seq_n.bit_length() - 1
    dp_bits = dp_n.bit_length() - 1
    lead = matrix.shape[0]
    sub = matrix.shape[1] // (seq_n * dp_n)
    grid = matrix.reshape((lead,) + (2,) * (bits + dp_bits) + (sub,))

    def axis_of(item):
        kind, k = item
        return 1 + (bits - 1 - k) if kind == "s" else 1 + bits + (dp_bits - 1 - k)

    def arrange(order):
        axes = (0, axis_of(("s", 0))) + tuple(axis_of(item) for item in order) + (bits + dp_bits + 1,)
        return jnp.transpose(grid, axes).reshape(matrix.shape)

    even, odd = orders
    if even == odd:
        return arrange(even)
    return jnp.where(core_odd, arrange(odd), arrange(even))


def reduce_rows(parts, orders, seq_n, dp_n):
    seq_at = lax.axis_index("seq")
    dp_at = lax.axis_index("dp")
    even, odd = orders
    steps = len(even)
    accs = tuple(p.reshape((2,) * steps + (p.shape[0] >> steps, p.shape[1])) for p in parts)

    def bit_value(item, seq_i, dp_i):
        kind, k = item
        return ((seq_i if kind == "s" else dp_i) >> k) & 1

    def flip(item, seq_i, dp_i):
        kind, k = item
        if kind == "s":
            return seq_i ^ (1 << k), dp_i
        return seq_i, dp_i ^ (1 << k)

    for step in range(steps):
        perm = []
        for dp_i in range(dp_n):
            for seq_i in range(seq_n):
                item = (odd if seq_i % 2 else even)[step]
                seq_j, dp_j = flip(item, seq_i, dp_i)
                perm.append((dp_i * seq_n + seq_i, dp_j * seq_n + seq_j))

        def traced_bit(item):
            kind, k = item
            return ((seq_at if kind == "s" else dp_at) // (1 << k)) % 2

        keep_at = jnp.where(seq_at % 2 == 1, traced_bit(odd[step]), traced_bit(even[step]))
        kept = tuple(lax.dynamic_index_in_dim(acc, keep_at, 0, keepdims=False) for acc in accs)
        given = tuple(
            lax.dynamic_index_in_dim(acc, 1 - keep_at, 0, keepdims=False).astype(jnp.bfloat16)
            for acc in accs
        )
        got = lax.ppermute(given, ("dp", "seq"), perm)
        accs = tuple(k + g.astype(jnp.float32) for k, g in zip(kept, got))
    accs = tuple(acc.astype(jnp.bfloat16) for acc in accs)
    for step in range(dp_n.bit_length() - 1):
        perm = [(member, member ^ (1 << step)) for member in range(dp_n)]
        got = lax.ppermute(accs, "dp", perm)
        upper = (dp_at // (1 << step)) % 2 == 1
        accs = tuple(
            jnp.where(upper, jnp.concatenate([g, acc], axis=0), jnp.concatenate([acc, g], axis=0))
            for acc, g in zip(accs, got)
        )
    return accs


def on_device(first_query, first_key, first_value, out_weight, norm_gain, joint_weight, upstream):
    batches, local_rows, columns, feature = first_query.shape
    head_count = feature // HEAD_DIM
    model_width = out_weight.shape[1]
    groups = batches * local_rows

    def to_heads(tensor):
        return tensor.reshape(groups, columns, head_count, HEAD_DIM)

    out_first, probs_first = attend(
        to_heads(first_query), to_heads(first_key), to_heads(first_value), "glhe", "ghlm"
    )
    flat_first = out_first.reshape(groups * columns, feature)
    hidden = jnp.dot(flat_first, out_weight, preferred_element_type=jnp.float32)
    inverse = lax.rsqrt(jnp.mean(hidden * hidden, axis=-1, keepdims=True) + epsilon)
    normed = (hidden * inverse * norm_gain).astype(jnp.bfloat16)
    both_cols = lax.all_to_all(
        jnp.concatenate([normed.reshape(batches, local_rows, columns, model_width), upstream], axis=3),
        "seq",
        split_axis=2,
        concat_axis=1,
        tiled=True,
    )
    normed_cols = both_cols[..., :model_width]
    joint_flat = jnp.dot(
        normed_cols.reshape(-1, model_width), joint_weight, preferred_element_type=jnp.float32
    )
    joint_cols = joint_flat.astype(jnp.bfloat16).reshape(
        batches, normed_cols.shape[1], normed_cols.shape[2], 3 * feature
    )
    all_rows, col_share = (joint_cols.shape[1], joint_cols.shape[2])
    pieces = joint_cols.reshape(batches, all_rows, col_share, 3, head_count, HEAD_DIM)
    query_cols, key_cols, value_cols = (pieces[:, :, :, 0], pieces[:, :, :, 1], pieces[:, :, :, 2])
    out_cols, probs_cols = attend(query_cols, key_cols, value_cols, "blche", "bchlm")
    upstream_cols = both_cols[..., model_width:]
    upstream_cols = upstream_cols.reshape(batches, all_rows, col_share, head_count, HEAD_DIM)
    grads_cols = attend_back(
        query_cols, key_cols, value_cols, probs_cols, upstream_cols, "blche", "bchlm"
    )
    stacked = jnp.stack(grads_cols, axis=3).reshape(batches, all_rows, col_share, 3 * feature)
    used_normed = normed_cols.reshape(-1, model_width)
    used_grads = stacked.reshape(-1, 3 * feature)
    grad_local = jnp.dot(used_grads, joint_weight.T, preferred_element_type=jnp.float32).astype(
        jnp.bfloat16
    )
    seq_n = lax.axis_size("seq")
    dp_n = lax.axis_size("dp")
    orders = split_orders(seq_n, dp_n)
    core_odd = lax.axis_index("seq") % 2 == 1
    pair = [(member, member ^ 1) for member in range(seq_n)]
    core = lax.axis_index("seq") % 2

    def my_half(factor):
        arranged = by_split_order(factor, orders, core_odd, seq_n, dp_n)
        half = arranged.shape[1] // 2
        return lax.dynamic_slice_in_dim(arranged, core * half, half, axis=1)

    normed_peer, grads_peer = lax.ppermute((used_normed, used_grads), "seq", pair)
    joint_term = jnp.dot(
        my_half(jnp.concatenate([used_normed, normed_peer], axis=0)).T,
        jnp.concatenate([used_grads, grads_peer], axis=0),
        preferred_element_type=jnp.float32,
    )
    both_rows = lax.all_to_all(
        jnp.concatenate(
            [
                out_cols.reshape(batches, all_rows, col_share, feature),
                grad_local.reshape(batches, all_rows, col_share, model_width),
            ],
            axis=3,
        ),
        "seq",
        split_axis=1,
        concat_axis=2,
        tiled=True,
    )
    column_out = both_rows[..., :feature]
    grad_normed = both_rows[..., feature:].reshape(-1, model_width)
    joint_term, grad_normed = lax.optimization_barrier((joint_term, grad_normed))
    grad_float = grad_normed.astype(jnp.float32)
    gain_term = jnp.sum(grad_float * hidden * inverse, axis=0)
    scaled = norm_gain * grad_float
    grad_hidden = (
        inverse * scaled - hidden * inverse**3 * jnp.mean(scaled * hidden, axis=-1, keepdims=True)
    ).astype(jnp.bfloat16)
    first_peer, hidden_peer, gain_peer = lax.ppermute((flat_first, grad_hidden, gain_term), "seq", pair)
    out_term = jnp.dot(
        my_half(jnp.concatenate([flat_first, first_peer], axis=0)).T,
        jnp.concatenate([grad_hidden, hidden_peer], axis=0),
        preferred_element_type=jnp.float32,
    )
    gain_term = my_half((gain_term + gain_peer)[None, :])[0][:, None]
    out_width = out_term.shape[1]
    joint_sum, out_sum = reduce_rows(
        (joint_term, jnp.concatenate([out_term, gain_term], axis=1)), orders, seq_n, dp_n
    )
    replicas = (joint_sum, out_sum[:, :out_width], out_sum[:, out_width].astype(jnp.float32))
    grad_first = jnp.dot(grad_hidden, out_weight.T, preferred_element_type=jnp.float32).astype(
        jnp.bfloat16
    )
    grads_rows = attend_back(
        to_heads(first_query),
        to_heads(first_key),
        to_heads(first_value),
        probs_first,
        to_heads(grad_first),
        "glhe",
        "ghlm",
    )
    grad_query = grads_rows[0].reshape(batches, local_rows, columns, feature)
    grad_key = grads_rows[1].reshape(batches, local_rows, columns, feature)
    grad_value = grads_rows[2].reshape(batches, local_rows, columns, feature)
    return (
        grad_query,
        grad_key,
        grad_value,
        column_out,
        replicas[0].astype(jnp.bfloat16),
        replicas[1].astype(jnp.bfloat16),
        replicas[2],
    )


def solution(mesh):
    placed = (
        P("dp", "seq", None, None),
        P("dp", "seq", None, None),
        P("dp", "seq", None, None),
        P(),
        P(),
        P(),
        P("dp", "seq", None, None),
    )
    return jax.shard_map(
        on_device,
        mesh=mesh,
        in_specs=placed,
        out_specs=(
            P("dp", "seq", None, None),
            P("dp", "seq", None, None),
            P("dp", "seq", None, None),
            P("dp", "seq", None, None),
            P("seq", None),
            P("seq", None),
            P("seq"),
        ),
        check_vma=False,
    )
```

```python
import jax
import jax.numpy as jnp
from jax import lax
from jax.sharding import PartitionSpec as P

HEAD_DIM = 128


epsilon = 1e-06


def attend(queries, key_table, values, layout, scores_form):
    keyed = layout.replace("l", "m")
    scaling = HEAD_DIM ** (-0.5)
    scores = (
        jnp.einsum(
            layout + "," + keyed + "->" + scores_form,
            queries,
            key_table,
            preferred_element_type=jnp.float32,
        )
        * scaling
    )
    extent = scores.shape[-1]
    causal = jnp.arange(extent)[:, None] >= jnp.arange(extent)[None, :]
    scores = jnp.where(causal, scores, -1e30)
    peak = jnp.max(scores, axis=-1, keepdims=True)
    weights = jnp.exp(scores - peak)
    prob_table = weights / jnp.sum(weights, axis=-1, keepdims=True)
    rounded = prob_table.astype(jnp.bfloat16)
    output = jnp.einsum(
        scores_form + "," + keyed + "->" + layout,
        rounded,
        values,
        preferred_element_type=jnp.float32,
    )
    return (output.astype(jnp.bfloat16), prob_table)


def attend_back(queries, key_table, values, prob_table, upstream_part, layout, scores_form):
    keyed = layout.replace("l", "m")
    scaling = HEAD_DIM ** (-0.5)
    grad_prob = jnp.einsum(
        layout + "," + keyed + "->" + scores_form,
        upstream_part,
        values,
        preferred_element_type=jnp.float32,
    )
    row_inner = jnp.sum(prob_table * grad_prob, axis=-1, keepdims=True)
    grad_score = (prob_table * (grad_prob - row_inner) * scaling).astype(jnp.bfloat16)
    grad_query = jnp.einsum(
        scores_form + "," + keyed + "->" + layout,
        grad_score,
        key_table,
        preferred_element_type=jnp.float32,
    )
    grad_key = jnp.einsum(
        scores_form + "," + layout + "->" + keyed,
        grad_score,
        queries,
        preferred_element_type=jnp.float32,
    )
    rounded = prob_table.astype(jnp.bfloat16)
    grad_value = jnp.einsum(
        scores_form + "," + layout + "->" + keyed,
        rounded,
        upstream_part,
        preferred_element_type=jnp.float32,
    )
    return (
        grad_query.astype(jnp.bfloat16),
        grad_key.astype(jnp.bfloat16),
        grad_value.astype(jnp.bfloat16),
    )


def split_orders(seq_n, dp_n, z_first=False):
    bits = seq_n.bit_length() - 1
    dp_bits = dp_n.bit_length() - 1
    assert 1 << bits == seq_n and 1 << dp_bits == dp_n and bits >= 1
    seq_rest = [("s", k) for k in range(1, bits)]
    dp_all = [("d", k) for k in range(dp_bits)]
    even = seq_rest[:1] + dp_all[:1] + seq_rest[1:] + dp_all[1:]
    odd = list(even)
    if bits >= 3 and dp_bits >= 1:
        odd = dp_all[:1] + [seq_rest[1], seq_rest[0]] + seq_rest[2:] + dp_all[1:]
        if z_first:
            even = [seq_rest[1], seq_rest[0]] + dp_all[:1] + seq_rest[2:] + dp_all[1:]
            odd = [seq_rest[1]] + dp_all[:1] + [seq_rest[0]] + seq_rest[2:] + dp_all[1:]
    assert sorted(even) == sorted(odd)
    return even, odd


def by_split_order(matrix, orders, core_odd, seq_n, dp_n):
    bits = seq_n.bit_length() - 1
    dp_bits = dp_n.bit_length() - 1
    lead = matrix.shape[0]
    sub = matrix.shape[1] // (seq_n * dp_n)
    grid = matrix.reshape((lead,) + (2,) * (bits + dp_bits) + (sub,))

    def axis_of(item):
        kind, k = item
        return 1 + (bits - 1 - k) if kind == "s" else 1 + bits + (dp_bits - 1 - k)

    def arrange(order):
        axes = (0, axis_of(("s", 0))) + tuple(axis_of(item) for item in order) + (bits + dp_bits + 1,)
        return jnp.transpose(grid, axes).reshape(matrix.shape)

    even, odd = orders
    if even == odd:
        return arrange(even)
    return jnp.where(core_odd, arrange(odd), arrange(even))


def reduce_rows(parts, part_orders, seq_n, dp_n):
    seq_at = lax.axis_index("seq")
    dp_at = lax.axis_index("dp")
    steps = len(part_orders[0][0])
    accs = tuple(p.reshape((2,) * steps + (p.shape[0] >> steps, p.shape[1])) for p in parts)

    def bit_value(item, seq_i, dp_i):
        kind, k = item
        return ((seq_i if kind == "s" else dp_i) >> k) & 1

    def flip(item, seq_i, dp_i):
        kind, k = item
        if kind == "s":
            return seq_i ^ (1 << k), dp_i
        return seq_i, dp_i ^ (1 << k)

    def traced_bit(item):
        kind, k = item
        return ((seq_at if kind == "s" else dp_at) // (1 << k)) % 2

    for step in range(steps):
        next_accs = []
        for acc, (even, odd) in zip(accs, part_orders):
            perm = []
            for dp_i in range(dp_n):
                for seq_i in range(seq_n):
                    item = (odd if seq_i % 2 else even)[step]
                    seq_j, dp_j = flip(item, seq_i, dp_i)
                    perm.append((dp_i * seq_n + seq_i, dp_j * seq_n + seq_j))
            keep_at = jnp.where(seq_at % 2 == 1, traced_bit(odd[step]), traced_bit(even[step]))
            kept = lax.dynamic_index_in_dim(acc, keep_at, 0, keepdims=False)
            given = lax.dynamic_index_in_dim(acc, 1 - keep_at, 0, keepdims=False).astype(jnp.bfloat16)
            got = lax.ppermute(given, ("dp", "seq"), perm)
            next_accs.append(kept + got.astype(jnp.float32))
        accs = tuple(next_accs)
    accs = tuple(acc.astype(jnp.bfloat16) for acc in accs)
    for step in range(dp_n.bit_length() - 1):
        perm = [(member, member ^ (1 << step)) for member in range(dp_n)]
        got = lax.ppermute(accs, "dp", perm)
        upper = (dp_at // (1 << step)) % 2 == 1
        accs = tuple(
            jnp.where(upper, jnp.concatenate([g, acc], axis=0), jnp.concatenate([acc, g], axis=0))
            for acc, g in zip(accs, got)
        )
    return accs


def on_device(first_query, first_key, first_value, out_weight, norm_gain, joint_weight, upstream):
    batches, local_rows, columns, feature = first_query.shape
    head_count = feature // HEAD_DIM
    model_width = out_weight.shape[1]
    groups = batches * local_rows

    def to_heads(tensor):
        return tensor.reshape(groups, columns, head_count, HEAD_DIM)

    out_first, probs_first = attend(
        to_heads(first_query), to_heads(first_key), to_heads(first_value), "glhe", "ghlm"
    )
    flat_first = out_first.reshape(groups * columns, feature)
    hidden = jnp.dot(flat_first, out_weight, preferred_element_type=jnp.float32)
    inverse = lax.rsqrt(jnp.mean(hidden * hidden, axis=-1, keepdims=True) + epsilon)
    normed = (hidden * inverse * norm_gain).astype(jnp.bfloat16)
    normed_cols = lax.all_to_all(
        normed.reshape(batches, local_rows, columns, model_width),
        "seq",
        split_axis=2,
        concat_axis=1,
        tiled=True,
    )
    joint_flat = jnp.dot(
        normed_cols.reshape(-1, model_width), joint_weight, preferred_element_type=jnp.float32
    )
    joint_cols = joint_flat.astype(jnp.bfloat16).reshape(
        batches, normed_cols.shape[1], normed_cols.shape[2], 3 * feature
    )
    all_rows, col_share = (joint_cols.shape[1], joint_cols.shape[2])
    pieces = joint_cols.reshape(batches, all_rows, col_share, 3, head_count, HEAD_DIM)
    query_cols, key_cols, value_cols = (pieces[:, :, :, 0], pieces[:, :, :, 1], pieces[:, :, :, 2])
    out_cols, probs_cols = attend(query_cols, key_cols, value_cols, "blche", "bchlm")
    upstream_cols = lax.all_to_all(upstream, "seq", split_axis=2, concat_axis=1, tiled=True)
    upstream_cols = upstream_cols.reshape(batches, all_rows, col_share, head_count, HEAD_DIM)
    grads_cols = attend_back(
        query_cols, key_cols, value_cols, probs_cols, upstream_cols, "blche", "bchlm"
    )
    stacked = jnp.stack(grads_cols, axis=3).reshape(batches, all_rows, col_share, 3 * feature)
    used_normed = normed_cols.reshape(-1, model_width)
    used_grads = stacked.reshape(-1, 3 * feature)
    grad_local = jnp.dot(used_grads, joint_weight.T, preferred_element_type=jnp.float32).astype(
        jnp.bfloat16
    )
    seq_n = lax.axis_size("seq")
    dp_n = lax.axis_size("dp")
    orders = split_orders(seq_n, dp_n)
    out_orders = split_orders(seq_n, dp_n, z_first=True)
    core_odd = lax.axis_index("seq") % 2 == 1
    pair = [(member, member ^ 1) for member in range(seq_n)]
    core = lax.axis_index("seq") % 2

    def my_half(factor, orders=orders):
        arranged = by_split_order(factor, orders, core_odd, seq_n, dp_n)
        half = arranged.shape[1] // 2
        return lax.dynamic_slice_in_dim(arranged, core * half, half, axis=1)

    normed_peer, grads_peer = lax.ppermute((used_normed, used_grads), "seq", pair)
    joint_term = jnp.dot(
        my_half(jnp.concatenate([used_normed, normed_peer], axis=0)).T,
        jnp.concatenate([used_grads, grads_peer], axis=0),
        preferred_element_type=jnp.float32,
    )
    grad_normed = lax.all_to_all(
        grad_local.reshape(batches, all_rows, col_share, model_width),
        "seq",
        split_axis=1,
        concat_axis=2,
        tiled=True,
    )
    grad_normed = grad_normed.reshape(-1, model_width)
    joint_term, grad_normed = lax.optimization_barrier((joint_term, grad_normed))
    grad_float = grad_normed.astype(jnp.float32)
    gain_term = jnp.sum(grad_float * hidden * inverse, axis=0)
    scaled = norm_gain * grad_float
    grad_hidden = (
        inverse * scaled - hidden * inverse**3 * jnp.mean(scaled * hidden, axis=-1, keepdims=True)
    ).astype(jnp.bfloat16)
    out_cols, grad_hidden = lax.optimization_barrier((out_cols, grad_hidden))
    column_out = lax.all_to_all(
        out_cols.reshape(batches, all_rows, col_share, feature),
        "seq",
        split_axis=1,
        concat_axis=2,
        tiled=True,
    )
    first_peer, hidden_peer, gain_peer = lax.ppermute((flat_first, grad_hidden, gain_term), "seq", pair)
    out_term = jnp.dot(
        my_half(jnp.concatenate([flat_first, first_peer], axis=0), out_orders).T,
        jnp.concatenate([grad_hidden, hidden_peer], axis=0),
        preferred_element_type=jnp.float32,
    )
    gain_term = my_half((gain_term + gain_peer)[None, :], out_orders)[0][:, None]
    out_width = out_term.shape[1]
    joint_sum, out_sum = reduce_rows(
        (joint_term, jnp.concatenate([out_term, gain_term], axis=1)), (orders, out_orders), seq_n, dp_n
    )
    replicas = (joint_sum, out_sum[:, :out_width], out_sum[:, out_width].astype(jnp.float32))
    grad_first = jnp.dot(grad_hidden, out_weight.T, preferred_element_type=jnp.float32).astype(
        jnp.bfloat16
    )
    grads_rows = attend_back(
        to_heads(first_query),
        to_heads(first_key),
        to_heads(first_value),
        probs_first,
        to_heads(grad_first),
        "glhe",
        "ghlm",
    )
    grad_query = grads_rows[0].reshape(batches, local_rows, columns, feature)
    grad_key = grads_rows[1].reshape(batches, local_rows, columns, feature)
    grad_value = grads_rows[2].reshape(batches, local_rows, columns, feature)
    return (
        grad_query,
        grad_key,
        grad_value,
        column_out,
        replicas[0].astype(jnp.bfloat16),
        replicas[1].astype(jnp.bfloat16),
        replicas[2],
    )


def solution(mesh):
    placed = (
        P("dp", "seq", None, None),
        P("dp", "seq", None, None),
        P("dp", "seq", None, None),
        P(),
        P(),
        P(),
        P("dp", "seq", None, None),
    )
    return jax.shard_map(
        on_device,
        mesh=mesh,
        in_specs=placed,
        out_specs=(
            P("dp", "seq", None, None),
            P("dp", "seq", None, None),
            P("dp", "seq", None, None),
            P("dp", "seq", None, None),
            P("seq", None),
            P("seq", None),
            P("seq"),
        ),
        check_vma=False,
    )
```

```python
import jax
import jax.numpy as jnp
from jax import lax
from jax.sharding import PartitionSpec as P

HEAD_DIM = 128


epsilon = 1e-06


def attend(queries, key_table, values, layout, scores_form):
    keyed = layout.replace("l", "m")
    scaling = HEAD_DIM ** (-0.5)
    scores = (
        jnp.einsum(
            layout + "," + keyed + "->" + scores_form,
            queries,
            key_table,
            preferred_element_type=jnp.float32,
        )
        * scaling
    )
    extent = scores.shape[-1]
    causal = jnp.arange(extent)[:, None] >= jnp.arange(extent)[None, :]
    scores = jnp.where(causal, scores, -1e30)
    peak = jnp.max(scores, axis=-1, keepdims=True)
    weights = jnp.exp(scores - peak)
    prob_table = weights / jnp.sum(weights, axis=-1, keepdims=True)
    rounded = prob_table.astype(jnp.bfloat16)
    output = jnp.einsum(
        scores_form + "," + keyed + "->" + layout,
        rounded,
        values,
        preferred_element_type=jnp.float32,
    )
    return (output.astype(jnp.bfloat16), prob_table)


def attend_back(queries, key_table, values, prob_table, upstream_part, layout, scores_form):
    keyed = layout.replace("l", "m")
    scaling = HEAD_DIM ** (-0.5)
    grad_prob = jnp.einsum(
        layout + "," + keyed + "->" + scores_form,
        upstream_part,
        values,
        preferred_element_type=jnp.float32,
    )
    row_inner = jnp.sum(prob_table * grad_prob, axis=-1, keepdims=True)
    grad_score = (prob_table * (grad_prob - row_inner) * scaling).astype(jnp.bfloat16)
    grad_query = jnp.einsum(
        scores_form + "," + keyed + "->" + layout,
        grad_score,
        key_table,
        preferred_element_type=jnp.float32,
    )
    grad_key = jnp.einsum(
        scores_form + "," + layout + "->" + keyed,
        grad_score,
        queries,
        preferred_element_type=jnp.float32,
    )
    rounded = prob_table.astype(jnp.bfloat16)
    grad_value = jnp.einsum(
        scores_form + "," + layout + "->" + keyed,
        rounded,
        upstream_part,
        preferred_element_type=jnp.float32,
    )
    return (
        grad_query.astype(jnp.bfloat16),
        grad_key.astype(jnp.bfloat16),
        grad_value.astype(jnp.bfloat16),
    )


def split_orders(seq_n, dp_n, z_first=False):
    bits = seq_n.bit_length() - 1
    dp_bits = dp_n.bit_length() - 1
    assert 1 << bits == seq_n and 1 << dp_bits == dp_n and bits >= 1
    seq_rest = [("s", k) for k in range(1, bits)]
    dp_all = [("d", k) for k in range(dp_bits)]
    even = seq_rest[:1] + dp_all[:1] + seq_rest[1:] + dp_all[1:]
    odd = list(even)
    if bits >= 3 and dp_bits >= 1:
        odd = dp_all[:1] + [seq_rest[1], seq_rest[0]] + seq_rest[2:] + dp_all[1:]
        if z_first:
            even = [seq_rest[1], seq_rest[0]] + dp_all[:1] + seq_rest[2:] + dp_all[1:]
            odd = [seq_rest[1]] + dp_all[:1] + [seq_rest[0]] + seq_rest[2:] + dp_all[1:]
    assert sorted(even) == sorted(odd)
    return even, odd


def by_split_order(matrix, orders, core_odd, seq_n, dp_n):
    bits = seq_n.bit_length() - 1
    dp_bits = dp_n.bit_length() - 1
    lead = matrix.shape[0]
    sub = matrix.shape[1] // (seq_n * dp_n)
    grid = matrix.reshape((lead,) + (2,) * (bits + dp_bits) + (sub,))

    def axis_of(item):
        kind, k = item
        return 1 + (bits - 1 - k) if kind == "s" else 1 + bits + (dp_bits - 1 - k)

    def arrange(order):
        axes = (0, axis_of(("s", 0))) + tuple(axis_of(item) for item in order) + (bits + dp_bits + 1,)
        return jnp.transpose(grid, axes).reshape(matrix.shape)

    even, odd = orders
    if even == odd:
        return arrange(even)
    return jnp.where(core_odd, arrange(odd), arrange(even))


def reduce_rows(parts, part_orders, seq_n, dp_n, tie):
    seq_at = lax.axis_index("seq")
    dp_at = lax.axis_index("dp")
    steps = len(part_orders[0][0])
    accs = tuple(p.reshape((2,) * steps + (p.shape[0] >> steps, p.shape[1])) for p in parts)

    def bit_value(item, seq_i, dp_i):
        kind, k = item
        return ((seq_i if kind == "s" else dp_i) >> k) & 1

    def flip(item, seq_i, dp_i):
        kind, k = item
        if kind == "s":
            return seq_i ^ (1 << k), dp_i
        return seq_i, dp_i ^ (1 << k)

    def traced_bit(item):
        kind, k = item
        return ((seq_at if kind == "s" else dp_at) // (1 << k)) % 2

    for step in range(steps):
        perms, kepts, givens = [], [], []
        for acc, (even, odd) in zip(accs, part_orders):
            perm = []
            for dp_i in range(dp_n):
                for seq_i in range(seq_n):
                    item = (odd if seq_i % 2 else even)[step]
                    seq_j, dp_j = flip(item, seq_i, dp_i)
                    perm.append((dp_i * seq_n + seq_i, dp_j * seq_n + seq_j))
            keep_at = jnp.where(seq_at % 2 == 1, traced_bit(odd[step]), traced_bit(even[step]))
            perms.append(perm)
            kepts.append(lax.dynamic_index_in_dim(acc, keep_at, 0, keepdims=False))
            givens.append(
                lax.dynamic_index_in_dim(acc, 1 - keep_at, 0, keepdims=False).astype(jnp.bfloat16)
            )
        if step == 0:
            givens, tie = lax.optimization_barrier((givens, tie))
        accs = tuple(
            kept + lax.ppermute(given, ("dp", "seq"), perm).astype(jnp.float32)
            for kept, given, perm in zip(kepts, givens, perms)
        )
    accs = tuple(acc.astype(jnp.bfloat16) for acc in accs)
    for step in range(dp_n.bit_length() - 1):
        perm = [(member, member ^ (1 << step)) for member in range(dp_n)]
        got = lax.ppermute(accs, "dp", perm)
        upper = (dp_at // (1 << step)) % 2 == 1
        accs = tuple(
            jnp.where(upper, jnp.concatenate([g, acc], axis=0), jnp.concatenate([acc, g], axis=0))
            for acc, g in zip(accs, got)
        )
    return accs, tie


def on_device(first_query, first_key, first_value, out_weight, norm_gain, joint_weight, upstream):
    batches, local_rows, columns, feature = first_query.shape
    head_count = feature // HEAD_DIM
    model_width = out_weight.shape[1]
    groups = batches * local_rows

    def to_heads(tensor):
        return tensor.reshape(groups, columns, head_count, HEAD_DIM)

    out_first, probs_first = attend(
        to_heads(first_query), to_heads(first_key), to_heads(first_value), "glhe", "ghlm"
    )
    flat_first = out_first.reshape(groups * columns, feature)
    hidden = jnp.dot(flat_first, out_weight, preferred_element_type=jnp.float32)
    inverse = lax.rsqrt(jnp.mean(hidden * hidden, axis=-1, keepdims=True) + epsilon)
    normed = (hidden * inverse * norm_gain).astype(jnp.bfloat16)
    normed_cols = lax.all_to_all(
        normed.reshape(batches, local_rows, columns, model_width),
        "seq",
        split_axis=2,
        concat_axis=1,
        tiled=True,
    )
    joint_flat = jnp.dot(
        normed_cols.reshape(-1, model_width), joint_weight, preferred_element_type=jnp.float32
    )
    joint_cols = joint_flat.astype(jnp.bfloat16).reshape(
        batches, normed_cols.shape[1], normed_cols.shape[2], 3 * feature
    )
    all_rows, col_share = (joint_cols.shape[1], joint_cols.shape[2])
    pieces = joint_cols.reshape(batches, all_rows, col_share, 3, head_count, HEAD_DIM)
    query_cols, key_cols, value_cols = (pieces[:, :, :, 0], pieces[:, :, :, 1], pieces[:, :, :, 2])
    out_cols, probs_cols = attend(query_cols, key_cols, value_cols, "blche", "bchlm")
    upstream_cols = lax.all_to_all(upstream, "seq", split_axis=2, concat_axis=1, tiled=True)
    upstream_cols = upstream_cols.reshape(batches, all_rows, col_share, head_count, HEAD_DIM)
    grads_cols = attend_back(
        query_cols, key_cols, value_cols, probs_cols, upstream_cols, "blche", "bchlm"
    )
    stacked = jnp.stack(grads_cols, axis=3).reshape(batches, all_rows, col_share, 3 * feature)
    used_normed = normed_cols.reshape(-1, model_width)
    used_grads = stacked.reshape(-1, 3 * feature)
    grad_local = jnp.dot(used_grads, joint_weight.T, preferred_element_type=jnp.float32).astype(
        jnp.bfloat16
    )
    seq_n = lax.axis_size("seq")
    dp_n = lax.axis_size("dp")
    orders = split_orders(seq_n, dp_n)
    out_orders = split_orders(seq_n, dp_n, z_first=True)
    core_odd = lax.axis_index("seq") % 2 == 1
    pair = [(member, member ^ 1) for member in range(seq_n)]
    core = lax.axis_index("seq") % 2

    def my_half(factor, orders=orders):
        arranged = by_split_order(factor, orders, core_odd, seq_n, dp_n)
        half = arranged.shape[1] // 2
        return lax.dynamic_slice_in_dim(arranged, core * half, half, axis=1)

    normed_peer, grads_peer = lax.ppermute((used_normed, used_grads), "seq", pair)
    joint_term = jnp.dot(
        my_half(jnp.concatenate([used_normed, normed_peer], axis=0)).T,
        jnp.concatenate([used_grads, grads_peer], axis=0),
        preferred_element_type=jnp.float32,
    )
    grad_normed = lax.all_to_all(
        grad_local.reshape(batches, all_rows, col_share, model_width),
        "seq",
        split_axis=1,
        concat_axis=2,
        tiled=True,
    )
    grad_normed = grad_normed.reshape(-1, model_width)
    (joint_sum,), grad_normed = reduce_rows((joint_term,), (orders,), seq_n, dp_n, grad_normed)
    grad_float = grad_normed.astype(jnp.float32)
    gain_term = jnp.sum(grad_float * hidden * inverse, axis=0)
    scaled = norm_gain * grad_float
    grad_hidden = (
        inverse * scaled - hidden * inverse**3 * jnp.mean(scaled * hidden, axis=-1, keepdims=True)
    ).astype(jnp.bfloat16)
    first_peer, hidden_peer, gain_peer = lax.ppermute((flat_first, grad_hidden, gain_term), "seq", pair)
    out_term = jnp.dot(
        my_half(jnp.concatenate([flat_first, first_peer], axis=0), out_orders).T,
        jnp.concatenate([grad_hidden, hidden_peer], axis=0),
        preferred_element_type=jnp.float32,
    )
    gain_term = my_half((gain_term + gain_peer)[None, :], out_orders)[0][:, None]
    out_width = out_term.shape[1]
    (out_sum,), out_cols = reduce_rows(
        (jnp.concatenate([out_term, gain_term], axis=1),), (out_orders,), seq_n, dp_n, out_cols
    )
    column_out = lax.all_to_all(
        out_cols.reshape(batches, all_rows, col_share, feature),
        "seq",
        split_axis=1,
        concat_axis=2,
        tiled=True,
    )
    replicas = (joint_sum, out_sum[:, :out_width], out_sum[:, out_width].astype(jnp.float32))
    grad_first = jnp.dot(grad_hidden, out_weight.T, preferred_element_type=jnp.float32).astype(
        jnp.bfloat16
    )
    grads_rows = attend_back(
        to_heads(first_query),
        to_heads(first_key),
        to_heads(first_value),
        probs_first,
        to_heads(grad_first),
        "glhe",
        "ghlm",
    )
    grad_query = grads_rows[0].reshape(batches, local_rows, columns, feature)
    grad_key = grads_rows[1].reshape(batches, local_rows, columns, feature)
    grad_value = grads_rows[2].reshape(batches, local_rows, columns, feature)
    return (
        grad_query,
        grad_key,
        grad_value,
        column_out,
        replicas[0].astype(jnp.bfloat16),
        replicas[1].astype(jnp.bfloat16),
        replicas[2],
    )


def solution(mesh):
    placed = (
        P("dp", "seq", None, None),
        P("dp", "seq", None, None),
        P("dp", "seq", None, None),
        P(),
        P(),
        P(),
        P("dp", "seq", None, None),
    )
    return jax.shard_map(
        on_device,
        mesh=mesh,
        in_specs=placed,
        out_specs=(
            P("dp", "seq", None, None),
            P("dp", "seq", None, None),
            P("dp", "seq", None, None),
            P("dp", "seq", None, None),
            P("seq", None),
            P("seq", None),
            P("seq"),
        ),
        check_vma=False,
    )
```

```python
import jax
import jax.numpy as jnp
from jax import lax
from jax.sharding import PartitionSpec as P

HEAD_DIM = 128


epsilon = 1e-06


def attend(queries, key_table, values, layout, scores_form):
    keyed = layout.replace("l", "m")
    scaling = HEAD_DIM ** (-0.5)
    scores = (
        jnp.einsum(
            layout + "," + keyed + "->" + scores_form,
            queries,
            key_table,
            preferred_element_type=jnp.float32,
        )
        * scaling
    )
    extent = scores.shape[-1]
    causal = jnp.arange(extent)[:, None] >= jnp.arange(extent)[None, :]
    scores = jnp.where(causal, scores, -1e30)
    peak = jnp.max(scores, axis=-1, keepdims=True)
    weights = jnp.exp(scores - peak)
    prob_table = weights / jnp.sum(weights, axis=-1, keepdims=True)
    rounded = prob_table.astype(jnp.bfloat16)
    output = jnp.einsum(
        scores_form + "," + keyed + "->" + layout,
        rounded,
        values,
        preferred_element_type=jnp.float32,
    )
    return (output.astype(jnp.bfloat16), prob_table)


def attend_back(queries, key_table, values, prob_table, upstream_part, layout, scores_form):
    keyed = layout.replace("l", "m")
    scaling = HEAD_DIM ** (-0.5)
    grad_prob = jnp.einsum(
        layout + "," + keyed + "->" + scores_form,
        upstream_part,
        values,
        preferred_element_type=jnp.float32,
    )
    row_inner = jnp.sum(prob_table * grad_prob, axis=-1, keepdims=True)
    grad_score = (prob_table * (grad_prob - row_inner) * scaling).astype(jnp.bfloat16)
    grad_query = jnp.einsum(
        scores_form + "," + keyed + "->" + layout,
        grad_score,
        key_table,
        preferred_element_type=jnp.float32,
    )
    grad_key = jnp.einsum(
        scores_form + "," + layout + "->" + keyed,
        grad_score,
        queries,
        preferred_element_type=jnp.float32,
    )
    rounded = prob_table.astype(jnp.bfloat16)
    grad_value = jnp.einsum(
        scores_form + "," + layout + "->" + keyed,
        rounded,
        upstream_part,
        preferred_element_type=jnp.float32,
    )
    return (
        grad_query.astype(jnp.bfloat16),
        grad_key.astype(jnp.bfloat16),
        grad_value.astype(jnp.bfloat16),
    )


def split_orders(seq_n, dp_n, z_first=False):
    bits = seq_n.bit_length() - 1
    dp_bits = dp_n.bit_length() - 1
    assert 1 << bits == seq_n and 1 << dp_bits == dp_n and bits >= 1
    seq_rest = [("s", k) for k in range(1, bits)]
    dp_all = [("d", k) for k in range(dp_bits)]
    even = seq_rest[:1] + dp_all[:1] + seq_rest[1:] + dp_all[1:]
    odd = list(even)
    if bits >= 3 and dp_bits >= 1:
        odd = dp_all[:1] + [seq_rest[1], seq_rest[0]] + seq_rest[2:] + dp_all[1:]
        if z_first:
            even = [seq_rest[1], seq_rest[0]] + dp_all[:1] + seq_rest[2:] + dp_all[1:]
            odd = [seq_rest[1]] + dp_all[:1] + [seq_rest[0]] + seq_rest[2:] + dp_all[1:]
    assert sorted(even) == sorted(odd)
    return even, odd


def by_split_order(matrix, orders, core_odd, seq_n, dp_n):
    bits = seq_n.bit_length() - 1
    dp_bits = dp_n.bit_length() - 1
    lead = matrix.shape[0]
    sub = matrix.shape[1] // (seq_n * dp_n)
    grid = matrix.reshape((lead,) + (2,) * (bits + dp_bits) + (sub,))

    def axis_of(item):
        kind, k = item
        return 1 + (bits - 1 - k) if kind == "s" else 1 + bits + (dp_bits - 1 - k)

    def arrange(order):
        axes = (0, axis_of(("s", 0))) + tuple(axis_of(item) for item in order) + (bits + dp_bits + 1,)
        return jnp.transpose(grid, axes).reshape(matrix.shape)

    even, odd = orders
    if even == odd:
        return arrange(even)
    return jnp.where(core_odd, arrange(odd), arrange(even))


def reduce_rows(parts, part_orders, seq_n, dp_n, tie):
    seq_at = lax.axis_index("seq")
    dp_at = lax.axis_index("dp")
    steps = len(part_orders[0][0])
    accs = tuple(p.reshape((2,) * steps + (p.shape[0] >> steps, p.shape[1])) for p in parts)

    def bit_value(item, seq_i, dp_i):
        kind, k = item
        return ((seq_i if kind == "s" else dp_i) >> k) & 1

    def flip(item, seq_i, dp_i):
        kind, k = item
        if kind == "s":
            return seq_i ^ (1 << k), dp_i
        return seq_i, dp_i ^ (1 << k)

    def traced_bit(item):
        kind, k = item
        return ((seq_at if kind == "s" else dp_at) // (1 << k)) % 2

    def half(pending, at):
        own, received = pending
        part = lax.dynamic_index_in_dim(own, at, 0, keepdims=False)
        if received is None:
            return part
        return part + lax.dynamic_index_in_dim(received, at, 0, keepdims=False).astype(jnp.float32)

    pendings = [(acc, None) for acc in accs]
    for step in range(steps):
        perms, kepts, givens = [], [], []
        for pending, (even, odd) in zip(pendings, part_orders):
            perm = []
            for dp_i in range(dp_n):
                for seq_i in range(seq_n):
                    item = (odd if seq_i % 2 else even)[step]
                    seq_j, dp_j = flip(item, seq_i, dp_i)
                    perm.append((dp_i * seq_n + seq_i, dp_j * seq_n + seq_j))
            keep_at = jnp.where(seq_at % 2 == 1, traced_bit(odd[step]), traced_bit(even[step]))
            perms.append(perm)
            kepts.append(half(pending, keep_at))
            givens.append(half(pending, 1 - keep_at).astype(jnp.bfloat16))
        if step == 0:
            givens, tie = lax.optimization_barrier((givens, tie))
        pendings = [
            (kept, lax.ppermute(given, ("dp", "seq"), perm))
            for kept, given, perm in zip(kepts, givens, perms)
        ]
    accs = tuple(own + received.astype(jnp.float32) for own, received in pendings)
    accs = tuple(acc.astype(jnp.bfloat16) for acc in accs)
    for step in range(dp_n.bit_length() - 1):
        perm = [(member, member ^ (1 << step)) for member in range(dp_n)]
        got = lax.ppermute(accs, "dp", perm)
        upper = (dp_at // (1 << step)) % 2 == 1
        accs = tuple(
            jnp.where(upper, jnp.concatenate([g, acc], axis=0), jnp.concatenate([acc, g], axis=0))
            for acc, g in zip(accs, got)
        )
    return accs, tie


def on_device(first_query, first_key, first_value, out_weight, norm_gain, joint_weight, upstream):
    batches, local_rows, columns, feature = first_query.shape
    head_count = feature // HEAD_DIM
    model_width = out_weight.shape[1]
    groups = batches * local_rows

    def to_heads(tensor):
        return tensor.reshape(groups, columns, head_count, HEAD_DIM)

    out_first, probs_first = attend(
        to_heads(first_query), to_heads(first_key), to_heads(first_value), "glhe", "ghlm"
    )
    flat_first = out_first.reshape(groups * columns, feature)
    hidden = jnp.dot(flat_first, out_weight, preferred_element_type=jnp.float32)
    inverse = lax.rsqrt(jnp.mean(hidden * hidden, axis=-1, keepdims=True) + epsilon)
    normed = (hidden * inverse * norm_gain).astype(jnp.bfloat16)
    normed_cols = lax.all_to_all(
        normed.reshape(batches, local_rows, columns, model_width),
        "seq",
        split_axis=2,
        concat_axis=1,
        tiled=True,
    )
    joint_flat = jnp.dot(
        normed_cols.reshape(-1, model_width), joint_weight, preferred_element_type=jnp.float32
    )
    joint_cols = joint_flat.astype(jnp.bfloat16).reshape(
        batches, normed_cols.shape[1], normed_cols.shape[2], 3 * feature
    )
    all_rows, col_share = (joint_cols.shape[1], joint_cols.shape[2])
    pieces = joint_cols.reshape(batches, all_rows, col_share, 3, head_count, HEAD_DIM)
    query_cols, key_cols, value_cols = (pieces[:, :, :, 0], pieces[:, :, :, 1], pieces[:, :, :, 2])
    out_cols, probs_cols = attend(query_cols, key_cols, value_cols, "blche", "bchlm")
    upstream_cols = lax.all_to_all(upstream, "seq", split_axis=2, concat_axis=1, tiled=True)
    upstream_cols = upstream_cols.reshape(batches, all_rows, col_share, head_count, HEAD_DIM)
    grads_cols = attend_back(
        query_cols, key_cols, value_cols, probs_cols, upstream_cols, "blche", "bchlm"
    )
    stacked = jnp.stack(grads_cols, axis=3).reshape(batches, all_rows, col_share, 3 * feature)
    used_normed = normed_cols.reshape(-1, model_width)
    used_grads = stacked.reshape(-1, 3 * feature)
    grad_local = jnp.dot(used_grads, joint_weight.T, preferred_element_type=jnp.float32).astype(
        jnp.bfloat16
    )
    seq_n = lax.axis_size("seq")
    dp_n = lax.axis_size("dp")
    orders = split_orders(seq_n, dp_n)
    out_orders = split_orders(seq_n, dp_n, z_first=True)
    core_odd = lax.axis_index("seq") % 2 == 1
    pair = [(member, member ^ 1) for member in range(seq_n)]
    core = lax.axis_index("seq") % 2

    def my_half(factor, orders=orders):
        arranged = by_split_order(factor, orders, core_odd, seq_n, dp_n)
        half = arranged.shape[1] // 2
        return lax.dynamic_slice_in_dim(arranged, core * half, half, axis=1)

    normed_peer, grads_peer = lax.ppermute((used_normed, used_grads), "seq", pair)
    joint_term = jnp.dot(
        my_half(jnp.concatenate([used_normed, normed_peer], axis=0)).T,
        jnp.concatenate([used_grads, grads_peer], axis=0),
        preferred_element_type=jnp.float32,
    )
    grad_normed = lax.all_to_all(
        grad_local.reshape(batches, all_rows, col_share, model_width),
        "seq",
        split_axis=1,
        concat_axis=2,
        tiled=True,
    )
    grad_normed = grad_normed.reshape(-1, model_width)
    (joint_sum,), grad_normed = reduce_rows((joint_term,), (orders,), seq_n, dp_n, grad_normed)
    grad_float = grad_normed.astype(jnp.float32)
    gain_term = jnp.sum(grad_float * hidden * inverse, axis=0)
    scaled = norm_gain * grad_float
    grad_hidden = (
        inverse * scaled - hidden * inverse**3 * jnp.mean(scaled * hidden, axis=-1, keepdims=True)
    ).astype(jnp.bfloat16)
    first_peer, hidden_peer, gain_peer = lax.ppermute((flat_first, grad_hidden, gain_term), "seq", pair)
    out_term = jnp.dot(
        my_half(jnp.concatenate([flat_first, first_peer], axis=0), out_orders).T,
        jnp.concatenate([grad_hidden, hidden_peer], axis=0),
        preferred_element_type=jnp.float32,
    )
    gain_term = my_half((gain_term + gain_peer)[None, :], out_orders)[0][:, None]
    out_width = out_term.shape[1]
    (out_sum,), out_cols = reduce_rows(
        (jnp.concatenate([out_term, gain_term], axis=1),), (out_orders,), seq_n, dp_n, out_cols
    )
    column_out = lax.all_to_all(
        out_cols.reshape(batches, all_rows, col_share, feature),
        "seq",
        split_axis=1,
        concat_axis=2,
        tiled=True,
    )
    replicas = (joint_sum, out_sum[:, :out_width], out_sum[:, out_width].astype(jnp.float32))
    grad_first = jnp.dot(grad_hidden, out_weight.T, preferred_element_type=jnp.float32).astype(
        jnp.bfloat16
    )
    grads_rows = attend_back(
        to_heads(first_query),
        to_heads(first_key),
        to_heads(first_value),
        probs_first,
        to_heads(grad_first),
        "glhe",
        "ghlm",
    )
    grad_query = grads_rows[0].reshape(batches, local_rows, columns, feature)
    grad_key = grads_rows[1].reshape(batches, local_rows, columns, feature)
    grad_value = grads_rows[2].reshape(batches, local_rows, columns, feature)
    return (
        grad_query,
        grad_key,
        grad_value,
        column_out,
        replicas[0].astype(jnp.bfloat16),
        replicas[1].astype(jnp.bfloat16),
        replicas[2],
    )


def solution(mesh):
    placed = (
        P("dp", "seq", None, None),
        P("dp", "seq", None, None),
        P("dp", "seq", None, None),
        P(),
        P(),
        P(),
        P("dp", "seq", None, None),
    )
    return jax.shard_map(
        on_device,
        mesh=mesh,
        in_specs=placed,
        out_specs=(
            P("dp", "seq", None, None),
            P("dp", "seq", None, None),
            P("dp", "seq", None, None),
            P("dp", "seq", None, None),
            P("seq", None),
            P("seq", None),
            P("seq"),
        ),
        check_vma=False,
    )
```

```python
import jax
import jax.numpy as jnp
from jax import lax
from jax.sharding import PartitionSpec as P

HEAD_DIM = 128


epsilon = 1e-06


def attend(queries, key_table, values, layout, scores_form):
    keyed = layout.replace("l", "m")
    scaling = HEAD_DIM ** (-0.5)
    scores = (
        jnp.einsum(
            layout + "," + keyed + "->" + scores_form,
            queries,
            key_table,
            preferred_element_type=jnp.float32,
        )
        * scaling
    )
    extent = scores.shape[-1]
    causal = jnp.arange(extent)[:, None] >= jnp.arange(extent)[None, :]
    scores = jnp.where(causal, scores, -1e30)
    peak = jnp.max(scores, axis=-1, keepdims=True)
    weights = jnp.exp(scores - peak)
    prob_table = weights / jnp.sum(weights, axis=-1, keepdims=True)
    rounded = prob_table.astype(jnp.bfloat16)
    output = jnp.einsum(
        scores_form + "," + keyed + "->" + layout,
        rounded,
        values,
        preferred_element_type=jnp.float32,
    )
    return (output.astype(jnp.bfloat16), prob_table)


def attend_back(queries, key_table, values, prob_table, upstream_part, layout, scores_form):
    keyed = layout.replace("l", "m")
    scaling = HEAD_DIM ** (-0.5)
    grad_prob = jnp.einsum(
        layout + "," + keyed + "->" + scores_form,
        upstream_part,
        values,
        preferred_element_type=jnp.float32,
    )
    row_inner = jnp.sum(prob_table * grad_prob, axis=-1, keepdims=True)
    grad_score = (prob_table * (grad_prob - row_inner) * scaling).astype(jnp.bfloat16)
    grad_query = jnp.einsum(
        scores_form + "," + keyed + "->" + layout,
        grad_score,
        key_table,
        preferred_element_type=jnp.float32,
    )
    grad_key = jnp.einsum(
        scores_form + "," + layout + "->" + keyed,
        grad_score,
        queries,
        preferred_element_type=jnp.float32,
    )
    rounded = prob_table.astype(jnp.bfloat16)
    grad_value = jnp.einsum(
        scores_form + "," + layout + "->" + keyed,
        rounded,
        upstream_part,
        preferred_element_type=jnp.float32,
    )
    return (
        grad_query.astype(jnp.bfloat16),
        grad_key.astype(jnp.bfloat16),
        grad_value.astype(jnp.bfloat16),
    )


def split_orders(seq_n, dp_n, z_first=False):
    bits = seq_n.bit_length() - 1
    dp_bits = dp_n.bit_length() - 1
    assert 1 << bits == seq_n and 1 << dp_bits == dp_n and bits >= 1
    seq_rest = [("s", k) for k in range(1, bits)]
    dp_all = [("d", k) for k in range(dp_bits)]
    even = seq_rest[:1] + dp_all[:1] + seq_rest[1:] + dp_all[1:]
    odd = list(even)
    if bits >= 3 and dp_bits >= 1:
        odd = dp_all[:1] + [seq_rest[1], seq_rest[0]] + seq_rest[2:] + dp_all[1:]
        if z_first:
            even = [seq_rest[1], seq_rest[0]] + dp_all[:1] + seq_rest[2:] + dp_all[1:]
            odd = [seq_rest[1]] + dp_all[:1] + [seq_rest[0]] + seq_rest[2:] + dp_all[1:]
    assert sorted(even) == sorted(odd)
    return even, odd


def by_split_order(matrix, orders, core_odd, seq_n, dp_n):
    bits = seq_n.bit_length() - 1
    dp_bits = dp_n.bit_length() - 1
    lead = matrix.shape[0]
    sub = matrix.shape[1] // (seq_n * dp_n)
    grid = matrix.reshape((lead,) + (2,) * (bits + dp_bits) + (sub,))

    def axis_of(item):
        kind, k = item
        return 1 + (bits - 1 - k) if kind == "s" else 1 + bits + (dp_bits - 1 - k)

    def arrange(order):
        axes = (0, axis_of(("s", 0))) + tuple(axis_of(item) for item in order) + (bits + dp_bits + 1,)
        return jnp.transpose(grid, axes).reshape(matrix.shape)

    even, odd = orders
    if even == odd:
        return arrange(even)
    return jnp.where(core_odd, arrange(odd), arrange(even))


def halving_steps(pendings, part_orders, seq_n, dp_n, steps, ties):
    seq_at = lax.axis_index("seq")
    dp_at = lax.axis_index("dp")

    def flip(item, seq_i, dp_i):
        kind, k = item
        if kind == "s":
            return seq_i ^ (1 << k), dp_i
        return seq_i, dp_i ^ (1 << k)

    def traced_bit(item):
        kind, k = item
        return ((seq_at if kind == "s" else dp_at) // (1 << k)) % 2

    def half(pending, at):
        own, received = pending
        part = lax.dynamic_index_in_dim(own, at, 0, keepdims=False)
        if received is None:
            return part
        return part + lax.dynamic_index_in_dim(received, at, 0, keepdims=False).astype(jnp.float32)

    ties = dict(ties)
    for step in steps:
        perms, kepts, givens = [], [], []
        for pending, (even, odd) in zip(pendings, part_orders):
            perm = []
            for dp_i in range(dp_n):
                for seq_i in range(seq_n):
                    item = (odd if seq_i % 2 else even)[step]
                    seq_j, dp_j = flip(item, seq_i, dp_i)
                    perm.append((dp_i * seq_n + seq_i, dp_j * seq_n + seq_j))
            keep_at = jnp.where(seq_at % 2 == 1, traced_bit(odd[step]), traced_bit(even[step]))
            perms.append(perm)
            kepts.append(half(pending, keep_at))
            givens.append(half(pending, 1 - keep_at).astype(jnp.bfloat16))
        if step in ties:
            givens, ties[step] = lax.optimization_barrier((givens, ties[step]))
        pendings = [
            (kept, lax.ppermute(given, ("dp", "seq"), perm))
            for kept, given, perm in zip(kepts, givens, perms)
        ]
    return pendings, ties


def start_rows(parts, seq_n, dp_n):
    steps = (seq_n.bit_length() - 1) + (dp_n.bit_length() - 1) - 1
    return [(p.reshape((2,) * steps + (p.shape[0] >> steps, p.shape[1])), None) for p in parts]


def finish_rows(pendings, dp_n):
    dp_at = lax.axis_index("dp")
    accs = tuple((own + received.astype(jnp.float32)).astype(jnp.bfloat16) for own, received in pendings)
    for step in range(dp_n.bit_length() - 1):
        perm = [(member, member ^ (1 << step)) for member in range(dp_n)]
        got = lax.ppermute(accs, "dp", perm)
        upper = (dp_at // (1 << step)) % 2 == 1
        accs = tuple(
            jnp.where(upper, jnp.concatenate([g, acc], axis=0), jnp.concatenate([acc, g], axis=0))
            for acc, g in zip(accs, got)
        )
    return accs


def on_device(first_query, first_key, first_value, out_weight, norm_gain, joint_weight, upstream):
    batches, local_rows, columns, feature = first_query.shape
    head_count = feature // HEAD_DIM
    model_width = out_weight.shape[1]
    groups = batches * local_rows

    def to_heads(tensor):
        return tensor.reshape(groups, columns, head_count, HEAD_DIM)

    out_first, probs_first = attend(
        to_heads(first_query), to_heads(first_key), to_heads(first_value), "glhe", "ghlm"
    )
    flat_first = out_first.reshape(groups * columns, feature)
    hidden = jnp.dot(flat_first, out_weight, preferred_element_type=jnp.float32)
    inverse = lax.rsqrt(jnp.mean(hidden * hidden, axis=-1, keepdims=True) + epsilon)
    normed = (hidden * inverse * norm_gain).astype(jnp.bfloat16)
    normed_cols = lax.all_to_all(
        normed.reshape(batches, local_rows, columns, model_width),
        "seq",
        split_axis=2,
        concat_axis=1,
        tiled=True,
    )
    joint_flat = jnp.dot(
        normed_cols.reshape(-1, model_width), joint_weight, preferred_element_type=jnp.float32
    )
    joint_cols = joint_flat.astype(jnp.bfloat16).reshape(
        batches, normed_cols.shape[1], normed_cols.shape[2], 3 * feature
    )
    all_rows, col_share = (joint_cols.shape[1], joint_cols.shape[2])
    pieces = joint_cols.reshape(batches, all_rows, col_share, 3, head_count, HEAD_DIM)
    query_cols, key_cols, value_cols = (pieces[:, :, :, 0], pieces[:, :, :, 1], pieces[:, :, :, 2])
    out_cols, probs_cols = attend(query_cols, key_cols, value_cols, "blche", "bchlm")
    upstream_cols = lax.all_to_all(upstream, "seq", split_axis=2, concat_axis=1, tiled=True)
    upstream_cols = upstream_cols.reshape(batches, all_rows, col_share, head_count, HEAD_DIM)
    grads_cols = attend_back(
        query_cols, key_cols, value_cols, probs_cols, upstream_cols, "blche", "bchlm"
    )
    stacked = jnp.stack(grads_cols, axis=3).reshape(batches, all_rows, col_share, 3 * feature)
    used_normed = normed_cols.reshape(-1, model_width)
    used_grads = stacked.reshape(-1, 3 * feature)
    grad_local = jnp.dot(used_grads, joint_weight.T, preferred_element_type=jnp.float32).astype(
        jnp.bfloat16
    )
    seq_n = lax.axis_size("seq")
    dp_n = lax.axis_size("dp")
    orders = split_orders(seq_n, dp_n)
    out_orders = split_orders(seq_n, dp_n, z_first=True)
    core_odd = lax.axis_index("seq") % 2 == 1
    pair = [(member, member ^ 1) for member in range(seq_n)]
    core = lax.axis_index("seq") % 2

    def my_half(factor, orders=orders):
        arranged = by_split_order(factor, orders, core_odd, seq_n, dp_n)
        half = arranged.shape[1] // 2
        return lax.dynamic_slice_in_dim(arranged, core * half, half, axis=1)

    normed_peer, grads_peer = lax.ppermute((used_normed, used_grads), "seq", pair)
    joint_term = jnp.dot(
        my_half(jnp.concatenate([used_normed, normed_peer], axis=0)).T,
        jnp.concatenate([used_grads, grads_peer], axis=0),
        preferred_element_type=jnp.float32,
    )
    grad_normed = lax.all_to_all(
        grad_local.reshape(batches, all_rows, col_share, model_width),
        "seq",
        split_axis=1,
        concat_axis=2,
        tiled=True,
    )
    grad_normed = grad_normed.reshape(-1, model_width)
    steps = len(orders[0])
    joint_rows, ties = halving_steps(
        start_rows((joint_term,), seq_n, dp_n), (orders,), seq_n, dp_n, [0], {0: grad_normed}
    )
    grad_normed = ties[0]
    grad_float = grad_normed.astype(jnp.float32)
    gain_term = jnp.sum(grad_float * hidden * inverse, axis=0)
    scaled = norm_gain * grad_float
    grad_hidden = (
        inverse * scaled - hidden * inverse**3 * jnp.mean(scaled * hidden, axis=-1, keepdims=True)
    ).astype(jnp.bfloat16)
    first_peer, hidden_peer, gain_peer = lax.ppermute((flat_first, grad_hidden, gain_term), "seq", pair)
    out_term = jnp.dot(
        my_half(jnp.concatenate([flat_first, first_peer], axis=0), out_orders).T,
        jnp.concatenate([grad_hidden, hidden_peer], axis=0),
        preferred_element_type=jnp.float32,
    )
    gain_term = my_half((gain_term + gain_peer)[None, :], out_orders)[0][:, None]
    out_width = out_term.shape[1]
    out_rows, ties = halving_steps(
        start_rows((jnp.concatenate([out_term, gain_term], axis=1),), seq_n, dp_n),
        (out_orders,),
        seq_n,
        dp_n,
        range(steps),
        {0: out_cols},
    )
    out_cols = ties[0]
    column_out = lax.all_to_all(
        out_cols.reshape(batches, all_rows, col_share, feature),
        "seq",
        split_axis=1,
        concat_axis=2,
        tiled=True,
    )
    grad_first = jnp.dot(grad_hidden, out_weight.T, preferred_element_type=jnp.float32).astype(
        jnp.bfloat16
    )
    grads_rows = attend_back(
        to_heads(first_query),
        to_heads(first_key),
        to_heads(first_value),
        probs_first,
        to_heads(grad_first),
        "glhe",
        "ghlm",
    )
    joint_rows, ties = halving_steps(
        joint_rows, (orders,), seq_n, dp_n, range(1, steps), {1: column_out, 2: grads_rows}
    )
    column_out, grads_rows = ties[1], ties[2]
    (joint_sum,) = finish_rows(joint_rows, dp_n)
    (out_sum,) = finish_rows(out_rows, dp_n)
    replicas = (joint_sum, out_sum[:, :out_width], out_sum[:, out_width].astype(jnp.float32))
    grad_query = grads_rows[0].reshape(batches, local_rows, columns, feature)
    grad_key = grads_rows[1].reshape(batches, local_rows, columns, feature)
    grad_value = grads_rows[2].reshape(batches, local_rows, columns, feature)
    return (
        grad_query,
        grad_key,
        grad_value,
        column_out,
        replicas[0].astype(jnp.bfloat16),
        replicas[1].astype(jnp.bfloat16),
        replicas[2],
    )


def solution(mesh):
    placed = (
        P("dp", "seq", None, None),
        P("dp", "seq", None, None),
        P("dp", "seq", None, None),
        P(),
        P(),
        P(),
        P("dp", "seq", None, None),
    )
    return jax.shard_map(
        on_device,
        mesh=mesh,
        in_specs=placed,
        out_specs=(
            P("dp", "seq", None, None),
            P("dp", "seq", None, None),
            P("dp", "seq", None, None),
            P("dp", "seq", None, None),
            P("seq", None),
            P("seq", None),
            P("seq"),
        ),
        check_vma=False,
    )
```

```python
import jax
import jax.numpy as jnp
from jax import lax
from jax.experimental import pallas as pl
from jax.experimental.pallas import tpu as pltpu
from jax.sharding import PartitionSpec as P

HEAD_DIM = 128


epsilon = 1e-06


def attend(queries, key_table, values, layout, scores_form):
    keyed = layout.replace("l", "m")
    scaling = HEAD_DIM ** (-0.5)
    scores = (
        jnp.einsum(
            layout + "," + keyed + "->" + scores_form,
            queries,
            key_table,
            preferred_element_type=jnp.float32,
        )
        * scaling
    )
    extent = scores.shape[-1]
    causal = jnp.arange(extent)[:, None] >= jnp.arange(extent)[None, :]
    scores = jnp.where(causal, scores, -1e30)
    peak = jnp.max(scores, axis=-1, keepdims=True)
    weights = jnp.exp(scores - peak)
    prob_table = weights / jnp.sum(weights, axis=-1, keepdims=True)
    rounded = prob_table.astype(jnp.bfloat16)
    output = jnp.einsum(
        scores_form + "," + keyed + "->" + layout,
        rounded,
        values,
        preferred_element_type=jnp.float32,
    )
    return (output.astype(jnp.bfloat16), prob_table)


def attend_back(queries, key_table, values, prob_table, upstream_part, layout, scores_form):
    keyed = layout.replace("l", "m")
    scaling = HEAD_DIM ** (-0.5)
    grad_prob = jnp.einsum(
        layout + "," + keyed + "->" + scores_form,
        upstream_part,
        values,
        preferred_element_type=jnp.float32,
    )
    row_inner = jnp.sum(prob_table * grad_prob, axis=-1, keepdims=True)
    grad_score = (prob_table * (grad_prob - row_inner) * scaling).astype(jnp.bfloat16)
    grad_query = jnp.einsum(
        scores_form + "," + keyed + "->" + layout,
        grad_score,
        key_table,
        preferred_element_type=jnp.float32,
    )
    grad_key = jnp.einsum(
        scores_form + "," + layout + "->" + keyed,
        grad_score,
        queries,
        preferred_element_type=jnp.float32,
    )
    rounded = prob_table.astype(jnp.bfloat16)
    grad_value = jnp.einsum(
        scores_form + "," + layout + "->" + keyed,
        rounded,
        upstream_part,
        preferred_element_type=jnp.float32,
    )
    return (
        grad_query.astype(jnp.bfloat16),
        grad_key.astype(jnp.bfloat16),
        grad_value.astype(jnp.bfloat16),
    )


def _times_kernel(x_ref, w_ref, o_ref):
    o_ref[...] = jnp.dot(x_ref[...], w_ref[...], preferred_element_type=jnp.float32).astype(o_ref.dtype)


def times_weight(x, w, tile=512):
    rows, inner = x.shape
    width = w.shape[1]
    return pl.pallas_call(
        _times_kernel,
        grid=(width // tile,),
        in_specs=[
            pl.BlockSpec((rows, inner), lambda j: (0, 0)),
            pl.BlockSpec((inner, tile), lambda j: (0, j)),
        ],
        out_specs=pl.BlockSpec((rows, tile), lambda j: (0, j)),
        out_shape=jax.ShapeDtypeStruct((rows, width), jnp.bfloat16),
    )(x, w)


def _times_t_kernel(x_ref, w_ref, o_ref, acc_ref):
    step = pl.program_id(0)

    @pl.when(step == 0)
    def _():
        acc_ref[...] = jnp.zeros_like(acc_ref)

    acc_ref[...] += lax.dot_general(
        x_ref[...], w_ref[...], (((1,), (1,)), ((), ())), preferred_element_type=jnp.float32
    )

    @pl.when(step == pl.num_programs(0) - 1)
    def _():
        o_ref[...] = acc_ref[...].astype(o_ref.dtype)


def times_weight_t(x, w, tile=512):
    rows, inner = x.shape
    width = w.shape[0]
    return pl.pallas_call(
        _times_t_kernel,
        grid=(inner // tile,),
        in_specs=[
            pl.BlockSpec((rows, tile), lambda k: (0, k)),
            pl.BlockSpec((width, tile), lambda k: (0, k)),
        ],
        out_specs=pl.BlockSpec((rows, width), lambda k: (0, 0)),
        out_shape=jax.ShapeDtypeStruct((rows, width), jnp.bfloat16),
        scratch_shapes=[pltpu.VMEM((rows, width), jnp.float32)],
    )(x, w)

def split_orders(seq_n, dp_n, z_first=False):
    bits = seq_n.bit_length() - 1
    dp_bits = dp_n.bit_length() - 1
    assert 1 << bits == seq_n and 1 << dp_bits == dp_n and bits >= 1
    seq_rest = [("s", k) for k in range(1, bits)]
    dp_all = [("d", k) for k in range(dp_bits)]
    even = seq_rest[:1] + dp_all[:1] + seq_rest[1:] + dp_all[1:]
    odd = list(even)
    if bits >= 3 and dp_bits >= 1:
        odd = dp_all[:1] + [seq_rest[1], seq_rest[0]] + seq_rest[2:] + dp_all[1:]
        if z_first:
            even = [seq_rest[1], seq_rest[0]] + dp_all[:1] + seq_rest[2:] + dp_all[1:]
            odd = [seq_rest[1]] + dp_all[:1] + [seq_rest[0]] + seq_rest[2:] + dp_all[1:]
    assert sorted(even) == sorted(odd)
    return even, odd


def by_split_order(matrix, orders, core_odd, seq_n, dp_n):
    bits = seq_n.bit_length() - 1
    dp_bits = dp_n.bit_length() - 1
    lead = matrix.shape[0]
    sub = matrix.shape[1] // (seq_n * dp_n)
    grid = matrix.reshape((lead,) + (2,) * (bits + dp_bits) + (sub,))

    def axis_of(item):
        kind, k = item
        return 1 + (bits - 1 - k) if kind == "s" else 1 + bits + (dp_bits - 1 - k)

    def arrange(order):
        axes = (0, axis_of(("s", 0))) + tuple(axis_of(item) for item in order) + (bits + dp_bits + 1,)
        return jnp.transpose(grid, axes).reshape(matrix.shape)

    even, odd = orders
    if even == odd:
        return arrange(even)
    return jnp.where(core_odd, arrange(odd), arrange(even))


def reduce_rows(parts, part_orders, seq_n, dp_n, tie):
    seq_at = lax.axis_index("seq")
    dp_at = lax.axis_index("dp")
    steps = len(part_orders[0][0])
    accs = tuple(p.reshape((2,) * steps + (p.shape[0] >> steps, p.shape[1])) for p in parts)

    def bit_value(item, seq_i, dp_i):
        kind, k = item
        return ((seq_i if kind == "s" else dp_i) >> k) & 1

    def flip(item, seq_i, dp_i):
        kind, k = item
        if kind == "s":
            return seq_i ^ (1 << k), dp_i
        return seq_i, dp_i ^ (1 << k)

    def traced_bit(item):
        kind, k = item
        return ((seq_at if kind == "s" else dp_at) // (1 << k)) % 2

    for step in range(steps):
        perms, kepts, givens = [], [], []
        for acc, (even, odd) in zip(accs, part_orders):
            perm = []
            for dp_i in range(dp_n):
                for seq_i in range(seq_n):
                    item = (odd if seq_i % 2 else even)[step]
                    seq_j, dp_j = flip(item, seq_i, dp_i)
                    perm.append((dp_i * seq_n + seq_i, dp_j * seq_n + seq_j))
            keep_at = jnp.where(seq_at % 2 == 1, traced_bit(odd[step]), traced_bit(even[step]))
            perms.append(perm)
            kepts.append(lax.dynamic_index_in_dim(acc, keep_at, 0, keepdims=False))
            givens.append(
                lax.dynamic_index_in_dim(acc, 1 - keep_at, 0, keepdims=False).astype(jnp.bfloat16)
            )
        if step == 0:
            givens, tie = lax.optimization_barrier((givens, tie))
        accs = tuple(
            kept + lax.ppermute(given, ("dp", "seq"), perm).astype(jnp.float32)
            for kept, given, perm in zip(kepts, givens, perms)
        )
    accs = tuple(acc.astype(jnp.bfloat16) for acc in accs)
    for step in range(dp_n.bit_length() - 1):
        perm = [(member, member ^ (1 << step)) for member in range(dp_n)]
        got = lax.ppermute(accs, "dp", perm)
        upper = (dp_at // (1 << step)) % 2 == 1
        accs = tuple(
            jnp.where(upper, jnp.concatenate([g, acc], axis=0), jnp.concatenate([acc, g], axis=0))
            for acc, g in zip(accs, got)
        )
    return accs, tie


def on_device(first_query, first_key, first_value, out_weight, norm_gain, joint_weight, upstream):
    batches, local_rows, columns, feature = first_query.shape
    head_count = feature // HEAD_DIM
    model_width = out_weight.shape[1]
    groups = batches * local_rows

    def to_heads(tensor):
        return tensor.reshape(groups, columns, head_count, HEAD_DIM)

    out_first, probs_first = attend(
        to_heads(first_query), to_heads(first_key), to_heads(first_value), "glhe", "ghlm"
    )
    flat_first = out_first.reshape(groups * columns, feature)
    hidden = jnp.dot(flat_first, out_weight, preferred_element_type=jnp.float32)
    inverse = lax.rsqrt(jnp.mean(hidden * hidden, axis=-1, keepdims=True) + epsilon)
    normed = (hidden * inverse * norm_gain).astype(jnp.bfloat16)
    normed_cols = lax.all_to_all(
        normed.reshape(batches, local_rows, columns, model_width),
        "seq",
        split_axis=2,
        concat_axis=1,
        tiled=True,
    )
    joint_flat = times_weight(normed_cols.reshape(-1, model_width), joint_weight)
    joint_cols = joint_flat.reshape(
        batches, normed_cols.shape[1], normed_cols.shape[2], 3 * feature
    )
    all_rows, col_share = (joint_cols.shape[1], joint_cols.shape[2])
    pieces = joint_cols.reshape(batches, all_rows, col_share, 3, head_count, HEAD_DIM)
    query_cols, key_cols, value_cols = (pieces[:, :, :, 0], pieces[:, :, :, 1], pieces[:, :, :, 2])
    out_cols, probs_cols = attend(query_cols, key_cols, value_cols, "blche", "bchlm")
    upstream_cols = lax.all_to_all(upstream, "seq", split_axis=2, concat_axis=1, tiled=True)
    upstream_cols = upstream_cols.reshape(batches, all_rows, col_share, head_count, HEAD_DIM)
    grads_cols = attend_back(
        query_cols, key_cols, value_cols, probs_cols, upstream_cols, "blche", "bchlm"
    )
    stacked = jnp.stack(grads_cols, axis=3).reshape(batches, all_rows, col_share, 3 * feature)
    used_normed = normed_cols.reshape(-1, model_width)
    used_grads = stacked.reshape(-1, 3 * feature)
    grad_local = times_weight_t(used_grads, joint_weight)
    seq_n = lax.axis_size("seq")
    dp_n = lax.axis_size("dp")
    orders = split_orders(seq_n, dp_n)
    out_orders = split_orders(seq_n, dp_n, z_first=True)
    core_odd = lax.axis_index("seq") % 2 == 1
    pair = [(member, member ^ 1) for member in range(seq_n)]
    core = lax.axis_index("seq") % 2

    def my_half(factor, orders=orders):
        arranged = by_split_order(factor, orders, core_odd, seq_n, dp_n)
        half = arranged.shape[1] // 2
        return lax.dynamic_slice_in_dim(arranged, core * half, half, axis=1)

    normed_peer, grads_peer = lax.ppermute((used_normed, used_grads), "seq", pair)
    joint_term = jnp.dot(
        my_half(jnp.concatenate([used_normed, normed_peer], axis=0)).T,
        jnp.concatenate([used_grads, grads_peer], axis=0),
        preferred_element_type=jnp.float32,
    )
    grad_normed = lax.all_to_all(
        grad_local.reshape(batches, all_rows, col_share, model_width),
        "seq",
        split_axis=1,
        concat_axis=2,
        tiled=True,
    )
    grad_normed = grad_normed.reshape(-1, model_width)
    (joint_sum,), grad_normed = reduce_rows((joint_term,), (orders,), seq_n, dp_n, grad_normed)
    grad_float = grad_normed.astype(jnp.float32)
    gain_term = jnp.sum(grad_float * hidden * inverse, axis=0)
    scaled = norm_gain * grad_float
    grad_hidden = (
        inverse * scaled - hidden * inverse**3 * jnp.mean(scaled * hidden, axis=-1, keepdims=True)
    ).astype(jnp.bfloat16)
    first_peer, hidden_peer, gain_peer = lax.ppermute((flat_first, grad_hidden, gain_term), "seq", pair)
    out_term = jnp.dot(
        my_half(jnp.concatenate([flat_first, first_peer], axis=0), out_orders).T,
        jnp.concatenate([grad_hidden, hidden_peer], axis=0),
        preferred_element_type=jnp.float32,
    )
    gain_term = my_half((gain_term + gain_peer)[None, :], out_orders)[0][:, None]
    out_width = out_term.shape[1]
    (out_sum,), out_cols = reduce_rows(
        (jnp.concatenate([out_term, gain_term], axis=1),), (out_orders,), seq_n, dp_n, out_cols
    )
    column_out = lax.all_to_all(
        out_cols.reshape(batches, all_rows, col_share, feature),
        "seq",
        split_axis=1,
        concat_axis=2,
        tiled=True,
    )
    replicas = (joint_sum, out_sum[:, :out_width], out_sum[:, out_width].astype(jnp.float32))
    grad_first = jnp.dot(grad_hidden, out_weight.T, preferred_element_type=jnp.float32).astype(
        jnp.bfloat16
    )
    grads_rows = attend_back(
        to_heads(first_query),
        to_heads(first_key),
        to_heads(first_value),
        probs_first,
        to_heads(grad_first),
        "glhe",
        "ghlm",
    )
    grad_query = grads_rows[0].reshape(batches, local_rows, columns, feature)
    grad_key = grads_rows[1].reshape(batches, local_rows, columns, feature)
    grad_value = grads_rows[2].reshape(batches, local_rows, columns, feature)
    return (
        grad_query,
        grad_key,
        grad_value,
        column_out,
        replicas[0].astype(jnp.bfloat16),
        replicas[1].astype(jnp.bfloat16),
        replicas[2],
    )


def solution(mesh):
    placed = (
        P("dp", "seq", None, None),
        P("dp", "seq", None, None),
        P("dp", "seq", None, None),
        P(),
        P(),
        P(),
        P("dp", "seq", None, None),
    )
    return jax.shard_map(
        on_device,
        mesh=mesh,
        in_specs=placed,
        out_specs=(
            P("dp", "seq", None, None),
            P("dp", "seq", None, None),
            P("dp", "seq", None, None),
            P("dp", "seq", None, None),
            P("seq", None),
            P("seq", None),
            P("seq"),
        ),
        check_vma=False,
    )
```

```python
import jax
import jax.numpy as jnp
from jax import lax
from jax.sharding import PartitionSpec as P

HEAD_DIM = 128


epsilon = 1e-06


def attend(queries, key_table, values, layout, scores_form):
    keyed = layout.replace("l", "m")
    scaling = HEAD_DIM ** (-0.5)
    scores = (
        jnp.einsum(
            layout + "," + keyed + "->" + scores_form,
            queries,
            key_table,
            preferred_element_type=jnp.float32,
        )
        * scaling
    )
    extent = scores.shape[-1]
    causal = jnp.arange(extent)[:, None] >= jnp.arange(extent)[None, :]
    scores = jnp.where(causal, scores, -1e30)
    peak = jnp.max(scores, axis=-1, keepdims=True)
    weights = jnp.exp(scores - peak)
    prob_table = weights / jnp.sum(weights, axis=-1, keepdims=True)
    rounded = prob_table.astype(jnp.bfloat16)
    output = jnp.einsum(
        scores_form + "," + keyed + "->" + layout,
        rounded,
        values,
        preferred_element_type=jnp.float32,
    )
    return (output.astype(jnp.bfloat16), prob_table)


def attend_back(queries, key_table, values, prob_table, upstream_part, layout, scores_form):
    keyed = layout.replace("l", "m")
    scaling = HEAD_DIM ** (-0.5)
    grad_prob = jnp.einsum(
        layout + "," + keyed + "->" + scores_form,
        upstream_part,
        values,
        preferred_element_type=jnp.float32,
    )
    row_inner = jnp.sum(prob_table * grad_prob, axis=-1, keepdims=True)
    grad_score = (prob_table * (grad_prob - row_inner) * scaling).astype(jnp.bfloat16)
    grad_query = jnp.einsum(
        scores_form + "," + keyed + "->" + layout,
        grad_score,
        key_table,
        preferred_element_type=jnp.float32,
    )
    grad_key = jnp.einsum(
        scores_form + "," + layout + "->" + keyed,
        grad_score,
        queries,
        preferred_element_type=jnp.float32,
    )
    rounded = prob_table.astype(jnp.bfloat16)
    grad_value = jnp.einsum(
        scores_form + "," + layout + "->" + keyed,
        rounded,
        upstream_part,
        preferred_element_type=jnp.float32,
    )
    return (
        grad_query.astype(jnp.bfloat16),
        grad_key.astype(jnp.bfloat16),
        grad_value.astype(jnp.bfloat16),
    )


def split_orders(seq_n, dp_n, z_first=False):
    bits = seq_n.bit_length() - 1
    dp_bits = dp_n.bit_length() - 1
    assert 1 << bits == seq_n and 1 << dp_bits == dp_n and bits >= 1
    seq_rest = [("s", k) for k in range(1, bits)]
    dp_all = [("d", k) for k in range(dp_bits)]
    even = seq_rest[:1] + dp_all[:1] + seq_rest[1:] + dp_all[1:]
    odd = list(even)
    if bits >= 3 and dp_bits >= 1:
        odd = dp_all[:1] + [seq_rest[1], seq_rest[0]] + seq_rest[2:] + dp_all[1:]
        if z_first:
            even = [seq_rest[1], seq_rest[0]] + dp_all[:1] + seq_rest[2:] + dp_all[1:]
            odd = [seq_rest[1]] + dp_all[:1] + [seq_rest[0]] + seq_rest[2:] + dp_all[1:]
    assert sorted(even) == sorted(odd)
    return even, odd


def by_split_order(matrix, orders, core_odd, seq_n, dp_n):
    bits = seq_n.bit_length() - 1
    dp_bits = dp_n.bit_length() - 1
    lead = matrix.shape[0]
    sub = matrix.shape[1] // (seq_n * dp_n)
    grid = matrix.reshape((lead,) + (2,) * (bits + dp_bits) + (sub,))

    def axis_of(item):
        kind, k = item
        return 1 + (bits - 1 - k) if kind == "s" else 1 + bits + (dp_bits - 1 - k)

    def arrange(order):
        axes = (0, axis_of(("s", 0))) + tuple(axis_of(item) for item in order) + (bits + dp_bits + 1,)
        return jnp.transpose(grid, axes).reshape(matrix.shape)

    even, odd = orders
    if even == odd:
        return arrange(even)
    return jnp.where(core_odd, arrange(odd), arrange(even))


def reduce_rows(parts, part_orders, seq_n, dp_n, tie):
    seq_at = lax.axis_index("seq")
    dp_at = lax.axis_index("dp")
    steps = len(part_orders[0][0])
    accs = tuple(p.reshape((2,) * steps + (p.shape[0] >> steps, p.shape[1])) for p in parts)

    def bit_value(item, seq_i, dp_i):
        kind, k = item
        return ((seq_i if kind == "s" else dp_i) >> k) & 1

    def flip(item, seq_i, dp_i):
        kind, k = item
        if kind == "s":
            return seq_i ^ (1 << k), dp_i
        return seq_i, dp_i ^ (1 << k)

    def traced_bit(item):
        kind, k = item
        return ((seq_at if kind == "s" else dp_at) // (1 << k)) % 2

    for step in range(steps):
        perms, kepts, givens = [], [], []
        for acc, (even, odd) in zip(accs, part_orders):
            perm = []
            for dp_i in range(dp_n):
                for seq_i in range(seq_n):
                    item = (odd if seq_i % 2 else even)[step]
                    seq_j, dp_j = flip(item, seq_i, dp_i)
                    perm.append((dp_i * seq_n + seq_i, dp_j * seq_n + seq_j))
            keep_at = jnp.where(seq_at % 2 == 1, traced_bit(odd[step]), traced_bit(even[step]))
            perms.append(perm)
            kepts.append(lax.dynamic_index_in_dim(acc, keep_at, 0, keepdims=False))
            givens.append(
                lax.dynamic_index_in_dim(acc, 1 - keep_at, 0, keepdims=False).astype(jnp.bfloat16)
            )
        if step == 0:
            givens, tie = lax.optimization_barrier((givens, tie))
        accs = tuple(
            kept + lax.ppermute(given, ("dp", "seq"), perm).astype(jnp.float32)
            for kept, given, perm in zip(kepts, givens, perms)
        )
    accs = tuple(acc.astype(jnp.bfloat16) for acc in accs)
    for step in range(dp_n.bit_length() - 1):
        perm = [(member, member ^ (1 << step)) for member in range(dp_n)]
        got = lax.ppermute(accs, "dp", perm)
        upper = (dp_at // (1 << step)) % 2 == 1
        accs = tuple(
            jnp.where(upper, jnp.concatenate([g, acc], axis=0), jnp.concatenate([acc, g], axis=0))
            for acc, g in zip(accs, got)
        )
    return accs, tie


def on_device(first_query, first_key, first_value, out_weight, norm_gain, joint_weight, upstream):
    batches, local_rows, columns, feature = first_query.shape
    head_count = feature // HEAD_DIM
    model_width = out_weight.shape[1]
    groups = batches * local_rows

    def to_heads(tensor):
        return tensor.reshape(groups, columns, head_count, HEAD_DIM)

    out_first, probs_first = attend(
        to_heads(first_query), to_heads(first_key), to_heads(first_value), "glhe", "ghlm"
    )
    flat_first = out_first.reshape(groups * columns, feature)
    hidden = jnp.dot(flat_first, out_weight, preferred_element_type=jnp.float32)
    inverse = lax.rsqrt(jnp.mean(hidden * hidden, axis=-1, keepdims=True) + epsilon)
    normed = (hidden * inverse * norm_gain).astype(jnp.bfloat16)
    normed_cols = lax.all_to_all(
        normed.reshape(batches, local_rows, columns, model_width),
        "seq",
        split_axis=2,
        concat_axis=1,
        tiled=True,
    )
    joint_flat = jnp.dot(
        normed_cols.reshape(-1, model_width), joint_weight, preferred_element_type=jnp.float32
    )
    joint_cols = joint_flat.astype(jnp.bfloat16).reshape(
        batches, normed_cols.shape[1], normed_cols.shape[2], 3 * feature
    )
    all_rows, col_share = (joint_cols.shape[1], joint_cols.shape[2])
    pieces = joint_cols.reshape(batches, all_rows, col_share, 3, head_count, HEAD_DIM)
    query_cols, key_cols, value_cols = (pieces[:, :, :, 0], pieces[:, :, :, 1], pieces[:, :, :, 2])
    out_cols, probs_cols = attend(query_cols, key_cols, value_cols, "blche", "bchlm")
    upstream_cols = lax.all_to_all(upstream, "seq", split_axis=2, concat_axis=1, tiled=True)
    upstream_cols = upstream_cols.reshape(batches, all_rows, col_share, head_count, HEAD_DIM)
    grads_cols = attend_back(
        query_cols, key_cols, value_cols, probs_cols, upstream_cols, "blche", "bchlm"
    )
    stacked = jnp.stack(grads_cols, axis=3).reshape(batches, all_rows, col_share, 3 * feature)
    used_normed = normed_cols.reshape(-1, model_width)
    used_grads = stacked.reshape(-1, 3 * feature)
    grad_local = jnp.dot(used_grads, joint_weight.T, preferred_element_type=jnp.float32).astype(
        jnp.bfloat16
    )
    seq_n = lax.axis_size("seq")
    dp_n = lax.axis_size("dp")
    orders = split_orders(seq_n, dp_n)
    out_orders = split_orders(seq_n, dp_n, z_first=True)
    core_odd = lax.axis_index("seq") % 2 == 1
    pair = [(member, member ^ 1) for member in range(seq_n)]
    core = lax.axis_index("seq") % 2

    def my_half(factor, orders=orders):
        arranged = by_split_order(factor, orders, core_odd, seq_n, dp_n)
        half = arranged.shape[1] // 2
        return lax.dynamic_slice_in_dim(arranged, core * half, half, axis=1)

    normed_peer = lax.ppermute(used_normed, "seq", pair)
    grads_peer = jnp.stack(lax.ppermute(grads_cols, "seq", pair), axis=3).reshape(-1, 3 * feature)
    joint_term = jnp.dot(
        my_half(jnp.concatenate([used_normed, normed_peer], axis=0)).T,
        jnp.concatenate([used_grads, grads_peer], axis=0),
        preferred_element_type=jnp.float32,
    )
    grad_normed = lax.all_to_all(
        grad_local.reshape(batches, all_rows, col_share, model_width),
        "seq",
        split_axis=1,
        concat_axis=2,
        tiled=True,
    )
    grad_normed = grad_normed.reshape(-1, model_width)
    (joint_sum,), grad_normed = reduce_rows((joint_term,), (orders,), seq_n, dp_n, grad_normed)
    grad_float = grad_normed.astype(jnp.float32)
    gain_term = jnp.sum(grad_float * hidden * inverse, axis=0)
    scaled = norm_gain * grad_float
    grad_hidden = (
        inverse * scaled - hidden * inverse**3 * jnp.mean(scaled * hidden, axis=-1, keepdims=True)
    ).astype(jnp.bfloat16)
    first_peer, hidden_peer, gain_peer = lax.ppermute((flat_first, grad_hidden, gain_term), "seq", pair)
    out_term = jnp.dot(
        my_half(jnp.concatenate([flat_first, first_peer], axis=0), out_orders).T,
        jnp.concatenate([grad_hidden, hidden_peer], axis=0),
        preferred_element_type=jnp.float32,
    )
    gain_term = my_half((gain_term + gain_peer)[None, :], out_orders)[0][:, None]
    out_width = out_term.shape[1]
    (out_sum,), out_cols = reduce_rows(
        (jnp.concatenate([out_term, gain_term], axis=1),), (out_orders,), seq_n, dp_n, out_cols
    )
    column_out = lax.all_to_all(
        out_cols.reshape(batches, all_rows, col_share, feature),
        "seq",
        split_axis=1,
        concat_axis=2,
        tiled=True,
    )
    replicas = (joint_sum, out_sum[:, :out_width], out_sum[:, out_width].astype(jnp.float32))
    grad_first = jnp.dot(grad_hidden, out_weight.T, preferred_element_type=jnp.float32).astype(
        jnp.bfloat16
    )
    grads_rows = attend_back(
        to_heads(first_query),
        to_heads(first_key),
        to_heads(first_value),
        probs_first,
        to_heads(grad_first),
        "glhe",
        "ghlm",
    )
    grad_query = grads_rows[0].reshape(batches, local_rows, columns, feature)
    grad_key = grads_rows[1].reshape(batches, local_rows, columns, feature)
    grad_value = grads_rows[2].reshape(batches, local_rows, columns, feature)
    return (
        grad_query,
        grad_key,
        grad_value,
        column_out,
        replicas[0].astype(jnp.bfloat16),
        replicas[1].astype(jnp.bfloat16),
        replicas[2],
    )


def solution(mesh):
    placed = (
        P("dp", "seq", None, None),
        P("dp", "seq", None, None),
        P("dp", "seq", None, None),
        P(),
        P(),
        P(),
        P("dp", "seq", None, None),
    )
    return jax.shard_map(
        on_device,
        mesh=mesh,
        in_specs=placed,
        out_specs=(
            P("dp", "seq", None, None),
            P("dp", "seq", None, None),
            P("dp", "seq", None, None),
            P("dp", "seq", None, None),
            P("seq", None),
            P("seq", None),
            P("seq"),
        ),
        check_vma=False,
    )
```

```python
import jax
import jax.numpy as jnp
from jax import lax
from jax.sharding import PartitionSpec as P

HEAD_DIM = 128


epsilon = 1e-06


def attend(queries, key_table, values, layout, scores_form):
    keyed = layout.replace("l", "m")
    scaling = HEAD_DIM ** (-0.5)
    scores = (
        jnp.einsum(
            layout + "," + keyed + "->" + scores_form,
            queries,
            key_table,
            preferred_element_type=jnp.float32,
        )
        * scaling
    )
    extent = scores.shape[-1]
    causal = jnp.arange(extent)[:, None] >= jnp.arange(extent)[None, :]
    scores = jnp.where(causal, scores, -1e30)
    peak = jnp.max(scores, axis=-1, keepdims=True)
    weights = jnp.exp(scores - peak)
    prob_table = weights / jnp.sum(weights, axis=-1, keepdims=True)
    rounded = prob_table.astype(jnp.bfloat16)
    output = jnp.einsum(
        scores_form + "," + keyed + "->" + layout,
        rounded,
        values,
        preferred_element_type=jnp.float32,
    )
    return (output.astype(jnp.bfloat16), prob_table)


def attend_back(queries, key_table, values, prob_table, upstream_part, layout, scores_form):
    keyed = layout.replace("l", "m")
    scaling = HEAD_DIM ** (-0.5)
    grad_prob = jnp.einsum(
        layout + "," + keyed + "->" + scores_form,
        upstream_part,
        values,
        preferred_element_type=jnp.float32,
    )
    row_inner = jnp.sum(prob_table * grad_prob, axis=-1, keepdims=True)
    grad_score = (prob_table * (grad_prob - row_inner) * scaling).astype(jnp.bfloat16)
    grad_query = jnp.einsum(
        scores_form + "," + keyed + "->" + layout,
        grad_score,
        key_table,
        preferred_element_type=jnp.float32,
    )
    grad_key = jnp.einsum(
        scores_form + "," + layout + "->" + keyed,
        grad_score,
        queries,
        preferred_element_type=jnp.float32,
    )
    rounded = prob_table.astype(jnp.bfloat16)
    grad_value = jnp.einsum(
        scores_form + "," + layout + "->" + keyed,
        rounded,
        upstream_part,
        preferred_element_type=jnp.float32,
    )
    return (
        grad_query.astype(jnp.bfloat16),
        grad_key.astype(jnp.bfloat16),
        grad_value.astype(jnp.bfloat16),
    )


def split_orders(seq_n, dp_n, z_first=False):
    bits = seq_n.bit_length() - 1
    dp_bits = dp_n.bit_length() - 1
    assert 1 << bits == seq_n and 1 << dp_bits == dp_n and bits >= 1
    seq_rest = [("s", k) for k in range(1, bits)]
    dp_all = [("d", k) for k in range(dp_bits)]
    even = seq_rest[:1] + dp_all[:1] + seq_rest[1:] + dp_all[1:]
    odd = list(even)
    if bits >= 3 and dp_bits >= 1:
        odd = dp_all[:1] + [seq_rest[1], seq_rest[0]] + seq_rest[2:] + dp_all[1:]
        if z_first:
            even = [seq_rest[1], seq_rest[0]] + dp_all[:1] + seq_rest[2:] + dp_all[1:]
            odd = [seq_rest[1]] + dp_all[:1] + [seq_rest[0]] + seq_rest[2:] + dp_all[1:]
    assert sorted(even) == sorted(odd)
    return even, odd


def by_split_order(matrix, orders, core_odd, seq_n, dp_n):
    bits = seq_n.bit_length() - 1
    dp_bits = dp_n.bit_length() - 1
    lead = matrix.shape[0]
    sub = matrix.shape[1] // (seq_n * dp_n)
    grid = matrix.reshape((lead,) + (2,) * (bits + dp_bits) + (sub,))

    def axis_of(item):
        kind, k = item
        return 1 + (bits - 1 - k) if kind == "s" else 1 + bits + (dp_bits - 1 - k)

    def arrange(order):
        axes = (0, axis_of(("s", 0))) + tuple(axis_of(item) for item in order) + (bits + dp_bits + 1,)
        return jnp.transpose(grid, axes).reshape(matrix.shape)

    even, odd = orders
    if even == odd:
        return arrange(even)
    return jnp.where(core_odd, arrange(odd), arrange(even))


def reduce_rows(parts, part_orders, seq_n, dp_n, tie):
    seq_at = lax.axis_index("seq")
    dp_at = lax.axis_index("dp")
    steps = len(part_orders[0][0])
    accs = tuple(p.reshape((2,) * steps + (p.shape[0] >> steps, p.shape[1])) for p in parts)

    def bit_value(item, seq_i, dp_i):
        kind, k = item
        return ((seq_i if kind == "s" else dp_i) >> k) & 1

    def flip(item, seq_i, dp_i):
        kind, k = item
        if kind == "s":
            return seq_i ^ (1 << k), dp_i
        return seq_i, dp_i ^ (1 << k)

    def traced_bit(item):
        kind, k = item
        return ((seq_at if kind == "s" else dp_at) // (1 << k)) % 2

    for step in range(steps):
        perms, kepts, givens = [], [], []
        for acc, (even, odd) in zip(accs, part_orders):
            perm = []
            for dp_i in range(dp_n):
                for seq_i in range(seq_n):
                    item = (odd if seq_i % 2 else even)[step]
                    seq_j, dp_j = flip(item, seq_i, dp_i)
                    perm.append((dp_i * seq_n + seq_i, dp_j * seq_n + seq_j))
            keep_at = jnp.where(seq_at % 2 == 1, traced_bit(odd[step]), traced_bit(even[step]))
            perms.append(perm)
            kepts.append(lax.dynamic_index_in_dim(acc, keep_at, 0, keepdims=False))
            givens.append(
                lax.dynamic_index_in_dim(acc, 1 - keep_at, 0, keepdims=False).astype(jnp.bfloat16)
            )
        if step == 0:
            givens, tie = lax.optimization_barrier((givens, tie))
        accs = tuple(
            kept + lax.ppermute(given, ("dp", "seq"), perm).astype(jnp.float32)
            for kept, given, perm in zip(kepts, givens, perms)
        )
    accs = tuple(acc.astype(jnp.bfloat16) for acc in accs)
    for step in range(dp_n.bit_length() - 1):
        perm = [(member, member ^ (1 << step)) for member in range(dp_n)]
        got = lax.ppermute(accs, "dp", perm)
        upper = (dp_at // (1 << step)) % 2 == 1
        accs = tuple(
            jnp.where(upper, jnp.concatenate([g, acc], axis=0), jnp.concatenate([acc, g], axis=0))
            for acc, g in zip(accs, got)
        )
    return accs, tie


def on_device(first_query, first_key, first_value, out_weight, norm_gain, joint_weight, upstream):
    batches, local_rows, columns, feature = first_query.shape
    head_count = feature // HEAD_DIM
    model_width = out_weight.shape[1]
    groups = batches * local_rows

    def to_heads(tensor):
        return tensor.reshape(groups, columns, head_count, HEAD_DIM)

    out_first, probs_first = attend(
        to_heads(first_query), to_heads(first_key), to_heads(first_value), "glhe", "ghlm"
    )
    flat_first = out_first.reshape(groups * columns, feature)
    hidden = jnp.dot(flat_first, out_weight, preferred_element_type=jnp.float32)
    inverse = lax.rsqrt(jnp.mean(hidden * hidden, axis=-1, keepdims=True) + epsilon)
    normed = (hidden * inverse * norm_gain).astype(jnp.bfloat16)
    normed_cols = lax.all_to_all(
        normed.reshape(batches, local_rows, columns, model_width),
        "seq",
        split_axis=2,
        concat_axis=1,
        tiled=True,
    )
    joint_flat = jnp.dot(
        normed_cols.reshape(-1, model_width), joint_weight, preferred_element_type=jnp.float32
    )
    joint_cols = joint_flat.astype(jnp.bfloat16).reshape(
        batches, normed_cols.shape[1], normed_cols.shape[2], 3 * feature
    )
    all_rows, col_share = (joint_cols.shape[1], joint_cols.shape[2])
    pieces = joint_cols.reshape(batches, all_rows, col_share, 3, head_count, HEAD_DIM)
    query_cols, key_cols, value_cols = (pieces[:, :, :, 0], pieces[:, :, :, 1], pieces[:, :, :, 2])
    out_cols, probs_cols = attend(query_cols, key_cols, value_cols, "blche", "bchlm")
    upstream_cols = lax.all_to_all(upstream, "seq", split_axis=2, concat_axis=1, tiled=True)
    upstream_cols = upstream_cols.reshape(batches, all_rows, col_share, head_count, HEAD_DIM)
    grads_cols = attend_back(
        query_cols, key_cols, value_cols, probs_cols, upstream_cols, "blche", "bchlm"
    )
    stacked = jnp.stack(grads_cols, axis=3).reshape(batches, all_rows, col_share, 3 * feature)
    used_normed = normed_cols.reshape(-1, model_width)
    used_grads = stacked.reshape(-1, 3 * feature)
    grad_local = jnp.dot(used_grads, joint_weight.T, preferred_element_type=jnp.float32).astype(
        jnp.bfloat16
    )
    seq_n = lax.axis_size("seq")
    dp_n = lax.axis_size("dp")
    orders = split_orders(seq_n, dp_n)
    out_orders = split_orders(seq_n, dp_n, z_first=True)
    core_odd = lax.axis_index("seq") % 2 == 1
    pair = [(member, member ^ 1) for member in range(seq_n)]
    core = lax.axis_index("seq") % 2

    def my_half(factor, orders=orders):
        arranged = by_split_order(factor, orders, core_odd, seq_n, dp_n)
        half = arranged.shape[1] // 2
        return lax.dynamic_slice_in_dim(arranged, core * half, half, axis=1)

    normed_peer, grads_peer = lax.ppermute((used_normed, used_grads), "seq", pair)
    joint_term = jnp.dot(
        my_half(jnp.concatenate([used_normed, normed_peer], axis=0)).T,
        jnp.concatenate([used_grads, grads_peer], axis=0),
        preferred_element_type=jnp.float32,
    )
    grad_normed = lax.all_to_all(
        grad_local.reshape(batches, all_rows, col_share, model_width),
        "seq",
        split_axis=1,
        concat_axis=2,
        tiled=True,
    )
    grad_normed = grad_normed.reshape(-1, model_width)
    (joint_sum,), grad_normed = reduce_rows((joint_term,), (orders,), seq_n, dp_n, grad_normed)
    grad_float = grad_normed.astype(jnp.float32)
    gain_term = jnp.sum(grad_float * hidden * inverse, axis=0)
    scaled = norm_gain * grad_float
    grad_hidden = (
        inverse * scaled - hidden * inverse**3 * jnp.mean(scaled * hidden, axis=-1, keepdims=True)
    ).astype(jnp.bfloat16)
    out_term = jnp.dot(flat_first.T, grad_hidden, preferred_element_type=jnp.float32)
    out_width = out_term.shape[1]
    out_terms = jnp.concatenate([out_term, gain_term[:, None]], axis=1).astype(jnp.bfloat16)
    out_terms, out_cols = lax.optimization_barrier((out_terms, out_cols))
    out_sum = lax.psum_scatter(out_terms, ("seq", "dp"), scatter_dimension=0, tiled=True)
    out_sum = lax.all_gather(out_sum, "dp", axis=0, tiled=True)
    column_out = lax.all_to_all(
        out_cols.reshape(batches, all_rows, col_share, feature),
        "seq",
        split_axis=1,
        concat_axis=2,
        tiled=True,
    )
    replicas = (joint_sum, out_sum[:, :out_width], out_sum[:, out_width].astype(jnp.float32))
    grad_first = jnp.dot(grad_hidden, out_weight.T, preferred_element_type=jnp.float32).astype(
        jnp.bfloat16
    )
    grads_rows = attend_back(
        to_heads(first_query),
        to_heads(first_key),
        to_heads(first_value),
        probs_first,
        to_heads(grad_first),
        "glhe",
        "ghlm",
    )
    grad_query = grads_rows[0].reshape(batches, local_rows, columns, feature)
    grad_key = grads_rows[1].reshape(batches, local_rows, columns, feature)
    grad_value = grads_rows[2].reshape(batches, local_rows, columns, feature)
    return (
        grad_query,
        grad_key,
        grad_value,
        column_out,
        replicas[0].astype(jnp.bfloat16),
        replicas[1].astype(jnp.bfloat16),
        replicas[2],
    )


def solution(mesh):
    placed = (
        P("dp", "seq", None, None),
        P("dp", "seq", None, None),
        P("dp", "seq", None, None),
        P(),
        P(),
        P(),
        P("dp", "seq", None, None),
    )
    return jax.shard_map(
        on_device,
        mesh=mesh,
        in_specs=placed,
        out_specs=(
            P("dp", "seq", None, None),
            P("dp", "seq", None, None),
            P("dp", "seq", None, None),
            P("dp", "seq", None, None),
            P("seq", None),
            P("seq", None),
            P("seq"),
        ),
        check_vma=False,
    )
```

```python
import jax
import jax.numpy as jnp
from jax import lax
from jax.sharding import PartitionSpec as P

HEAD_DIM = 128


epsilon = 1e-06


def attend(queries, key_table, values, layout, scores_form):
    keyed = layout.replace("l", "m")
    scaling = HEAD_DIM ** (-0.5)
    scores = (
        jnp.einsum(
            layout + "," + keyed + "->" + scores_form,
            queries,
            key_table,
            preferred_element_type=jnp.float32,
        )
        * scaling
    )
    extent = scores.shape[-1]
    causal = jnp.arange(extent)[:, None] >= jnp.arange(extent)[None, :]
    scores = jnp.where(causal, scores, -1e30)
    peak = jnp.max(scores, axis=-1, keepdims=True)
    weights = jnp.exp(scores - peak)
    prob_table = weights / jnp.sum(weights, axis=-1, keepdims=True)
    rounded = prob_table.astype(jnp.bfloat16)
    output = jnp.einsum(
        scores_form + "," + keyed + "->" + layout,
        rounded,
        values,
        preferred_element_type=jnp.float32,
    )
    return (output.astype(jnp.bfloat16), prob_table)


def attend_back(queries, key_table, values, prob_table, upstream_part, layout, scores_form):
    keyed = layout.replace("l", "m")
    scaling = HEAD_DIM ** (-0.5)
    grad_prob = jnp.einsum(
        layout + "," + keyed + "->" + scores_form,
        upstream_part,
        values,
        preferred_element_type=jnp.float32,
    )
    row_inner = jnp.sum(prob_table * grad_prob, axis=-1, keepdims=True)
    grad_score = (prob_table * (grad_prob - row_inner) * scaling).astype(jnp.bfloat16)
    grad_query = jnp.einsum(
        scores_form + "," + keyed + "->" + layout,
        grad_score,
        key_table,
        preferred_element_type=jnp.float32,
    )
    grad_key = jnp.einsum(
        scores_form + "," + layout + "->" + keyed,
        grad_score,
        queries,
        preferred_element_type=jnp.float32,
    )
    rounded = prob_table.astype(jnp.bfloat16)
    grad_value = jnp.einsum(
        scores_form + "," + layout + "->" + keyed,
        rounded,
        upstream_part,
        preferred_element_type=jnp.float32,
    )
    return (
        grad_query.astype(jnp.bfloat16),
        grad_key.astype(jnp.bfloat16),
        grad_value.astype(jnp.bfloat16),
    )


def split_orders(seq_n, dp_n, z_first=False):
    bits = seq_n.bit_length() - 1
    dp_bits = dp_n.bit_length() - 1
    assert 1 << bits == seq_n and 1 << dp_bits == dp_n and bits >= 1
    seq_rest = [("s", k) for k in range(1, bits)]
    dp_all = [("d", k) for k in range(dp_bits)]
    even = seq_rest[:1] + dp_all[:1] + seq_rest[1:] + dp_all[1:]
    odd = list(even)
    if bits >= 3 and dp_bits >= 1:
        odd = dp_all[:1] + [seq_rest[1], seq_rest[0]] + seq_rest[2:] + dp_all[1:]
        if z_first:
            even = [seq_rest[1], seq_rest[0]] + dp_all[:1] + seq_rest[2:] + dp_all[1:]
            odd = [seq_rest[1]] + dp_all[:1] + [seq_rest[0]] + seq_rest[2:] + dp_all[1:]
    assert sorted(even) == sorted(odd)
    return even, odd


def by_split_order(matrix, orders, core_odd, seq_n, dp_n):
    bits = seq_n.bit_length() - 1
    dp_bits = dp_n.bit_length() - 1
    lead = matrix.shape[0]
    sub = matrix.shape[1] // (seq_n * dp_n)
    grid = matrix.reshape((lead,) + (2,) * (bits + dp_bits) + (sub,))

    def axis_of(item):
        kind, k = item
        return 1 + (bits - 1 - k) if kind == "s" else 1 + bits + (dp_bits - 1 - k)

    def arrange(order):
        axes = (0, axis_of(("s", 0))) + tuple(axis_of(item) for item in order) + (bits + dp_bits + 1,)
        return jnp.transpose(grid, axes).reshape(matrix.shape)

    even, odd = orders
    if even == odd:
        return arrange(even)
    return jnp.where(core_odd, arrange(odd), arrange(even))


def reduce_rows(parts, part_orders, seq_n, dp_n, tie):
    seq_at = lax.axis_index("seq")
    dp_at = lax.axis_index("dp")
    steps = len(part_orders[0][0])
    accs = tuple(p.reshape((2,) * steps + (p.shape[0] >> steps, p.shape[1])) for p in parts)

    def bit_value(item, seq_i, dp_i):
        kind, k = item
        return ((seq_i if kind == "s" else dp_i) >> k) & 1

    def flip(item, seq_i, dp_i):
        kind, k = item
        if kind == "s":
            return seq_i ^ (1 << k), dp_i
        return seq_i, dp_i ^ (1 << k)

    def traced_bit(item):
        kind, k = item
        return ((seq_at if kind == "s" else dp_at) // (1 << k)) % 2

    def half(pending, at):
        own, received = pending
        part = lax.dynamic_index_in_dim(own, at, 0, keepdims=False)
        if received is None:
            return part
        return part + lax.dynamic_index_in_dim(received, at, 0, keepdims=False).astype(jnp.float32)

    pendings = [(acc, None) for acc in accs]
    for step in range(steps):
        perms, kepts, givens = [], [], []
        for pending, (even, odd) in zip(pendings, part_orders):
            perm = []
            for dp_i in range(dp_n):
                for seq_i in range(seq_n):
                    item = (odd if seq_i % 2 else even)[step]
                    seq_j, dp_j = flip(item, seq_i, dp_i)
                    perm.append((dp_i * seq_n + seq_i, dp_j * seq_n + seq_j))
            keep_at = jnp.where(seq_at % 2 == 1, traced_bit(odd[step]), traced_bit(even[step]))
            perms.append(perm)
            kepts.append(half(pending, keep_at))
            givens.append(half(pending, 1 - keep_at).astype(jnp.bfloat16))
        if step == 0:
            givens, tie = lax.optimization_barrier((givens, tie))
        pendings = [
            (kept, lax.ppermute(given, ("dp", "seq"), perm))
            for kept, given, perm in zip(kepts, givens, perms)
        ]
    accs = tuple(own + received.astype(jnp.float32) for own, received in pendings)
    accs = tuple(acc.astype(jnp.bfloat16) for acc in accs)
    for step in range(dp_n.bit_length() - 1):
        perm = [(member, member ^ (1 << step)) for member in range(dp_n)]
        got = lax.ppermute(accs, "dp", perm)
        upper = (dp_at // (1 << step)) % 2 == 1
        accs = tuple(
            jnp.where(upper, jnp.concatenate([g, acc], axis=0), jnp.concatenate([acc, g], axis=0))
            for acc, g in zip(accs, got)
        )
    return accs, tie


def on_device(first_query, first_key, first_value, out_weight, norm_gain, joint_weight, upstream):
    batches, local_rows, columns, feature = first_query.shape
    head_count = feature // HEAD_DIM
    model_width = out_weight.shape[1]
    groups = batches * local_rows

    def to_heads(tensor):
        return tensor.reshape(groups, columns, head_count, HEAD_DIM)

    out_first, probs_first = attend(
        to_heads(first_query), to_heads(first_key), to_heads(first_value), "glhe", "ghlm"
    )
    flat_first = out_first.reshape(groups * columns, feature)
    hidden = jnp.dot(flat_first, out_weight, preferred_element_type=jnp.float32)
    inverse = lax.rsqrt(jnp.mean(hidden * hidden, axis=-1, keepdims=True) + epsilon)
    normed = (hidden * inverse * norm_gain).astype(jnp.bfloat16)
    normed_cols = lax.all_to_all(
        normed.reshape(batches, local_rows, columns, model_width),
        "seq",
        split_axis=2,
        concat_axis=1,
        tiled=True,
    )
    joint_flat = jnp.dot(
        normed_cols.reshape(-1, model_width), joint_weight, preferred_element_type=jnp.float32
    )
    joint_cols = joint_flat.astype(jnp.bfloat16).reshape(
        batches, normed_cols.shape[1], normed_cols.shape[2], 3 * feature
    )
    all_rows, col_share = (joint_cols.shape[1], joint_cols.shape[2])
    pieces = joint_cols.reshape(batches, all_rows, col_share, 3, head_count, HEAD_DIM)
    query_cols, key_cols, value_cols = (pieces[:, :, :, 0], pieces[:, :, :, 1], pieces[:, :, :, 2])
    out_cols, probs_cols = attend(query_cols, key_cols, value_cols, "blche", "bchlm")
    upstream_cols = lax.all_to_all(upstream, "seq", split_axis=2, concat_axis=1, tiled=True)
    upstream_cols = upstream_cols.reshape(batches, all_rows, col_share, head_count, HEAD_DIM)
    grads_cols = attend_back(
        query_cols, key_cols, value_cols, probs_cols, upstream_cols, "blche", "bchlm"
    )
    stacked = jnp.stack(grads_cols, axis=3).reshape(batches, all_rows, col_share, 3 * feature)
    used_normed = normed_cols.reshape(-1, model_width)
    used_grads = stacked.reshape(-1, 3 * feature)
    grad_local = jnp.dot(used_grads, joint_weight.T, preferred_element_type=jnp.float32).astype(
        jnp.bfloat16
    )
    seq_n = lax.axis_size("seq")
    dp_n = lax.axis_size("dp")
    orders = split_orders(seq_n, dp_n)
    out_orders = split_orders(seq_n, dp_n, z_first=True)
    core_odd = lax.axis_index("seq") % 2 == 1
    pair = [(member, member ^ 1) for member in range(seq_n)]
    core = lax.axis_index("seq") % 2

    def my_half(factor, orders=orders):
        arranged = by_split_order(factor, orders, core_odd, seq_n, dp_n)
        half = arranged.shape[1] // 2
        return lax.dynamic_slice_in_dim(arranged, core * half, half, axis=1)

    normed_peer, grads_peer = lax.ppermute((used_normed, used_grads), "seq", pair)
    joint_term = jnp.dot(
        my_half(jnp.concatenate([used_normed, normed_peer], axis=0)).T,
        jnp.concatenate([used_grads, grads_peer], axis=0),
        preferred_element_type=jnp.float32,
    )
    grad_normed = lax.all_to_all(
        grad_local.reshape(batches, all_rows, col_share, model_width),
        "seq",
        split_axis=1,
        concat_axis=2,
        tiled=True,
    )
    grad_normed = grad_normed.reshape(-1, model_width)
    (joint_sum,), grad_normed = reduce_rows((joint_term,), (orders,), seq_n, dp_n, grad_normed)
    grad_float = grad_normed.astype(jnp.float32)
    gain_term = jnp.sum(grad_float * hidden * inverse, axis=0)
    scaled = norm_gain * grad_float
    grad_hidden = (
        inverse * scaled - hidden * inverse**3 * jnp.mean(scaled * hidden, axis=-1, keepdims=True)
    ).astype(jnp.bfloat16)
    out_cols, grad_hidden = lax.optimization_barrier((out_cols, grad_hidden))
    first_peer, hidden_peer, gain_peer = lax.ppermute((flat_first, grad_hidden, gain_term), "seq", pair)
    out_term = jnp.dot(
        my_half(jnp.concatenate([flat_first, first_peer], axis=0), out_orders).T,
        jnp.concatenate([grad_hidden, hidden_peer], axis=0),
        preferred_element_type=jnp.float32,
    )
    gain_term = my_half((gain_term + gain_peer)[None, :], out_orders)[0][:, None]
    out_width = out_term.shape[1]
    column_out = lax.all_to_all(
        out_cols.reshape(batches, all_rows, col_share, feature),
        "seq",
        split_axis=1,
        concat_axis=2,
        tiled=True,
    )
    (out_sum,), column_out = reduce_rows(
        (jnp.concatenate([out_term, gain_term], axis=1),), (out_orders,), seq_n, dp_n, column_out
    )
    replicas = (joint_sum, out_sum[:, :out_width], out_sum[:, out_width].astype(jnp.float32))
    grad_first = jnp.dot(grad_hidden, out_weight.T, preferred_element_type=jnp.float32).astype(
        jnp.bfloat16
    )
    grads_rows = attend_back(
        to_heads(first_query),
        to_heads(first_key),
        to_heads(first_value),
        probs_first,
        to_heads(grad_first),
        "glhe",
        "ghlm",
    )
    grad_query = grads_rows[0].reshape(batches, local_rows, columns, feature)
    grad_key = grads_rows[1].reshape(batches, local_rows, columns, feature)
    grad_value = grads_rows[2].reshape(batches, local_rows, columns, feature)
    return (
        grad_query,
        grad_key,
        grad_value,
        column_out,
        replicas[0].astype(jnp.bfloat16),
        replicas[1].astype(jnp.bfloat16),
        replicas[2],
    )


def solution(mesh):
    placed = (
        P("dp", "seq", None, None),
        P("dp", "seq", None, None),
        P("dp", "seq", None, None),
        P(),
        P(),
        P(),
        P("dp", "seq", None, None),
    )
    return jax.shard_map(
        on_device,
        mesh=mesh,
        in_specs=placed,
        out_specs=(
            P("dp", "seq", None, None),
            P("dp", "seq", None, None),
            P("dp", "seq", None, None),
            P("dp", "seq", None, None),
            P("seq", None),
            P("seq", None),
            P("seq"),
        ),
        check_vma=False,
    )
```

```python
import jax
import jax.numpy as jnp
from jax import lax
from jax.sharding import PartitionSpec as P

HEAD_DIM = 128


epsilon = 1e-06


def attend(queries, key_table, values, layout, scores_form):
    keyed = layout.replace("l", "m")
    scaling = HEAD_DIM ** (-0.5)
    scores = (
        jnp.einsum(
            layout + "," + keyed + "->" + scores_form,
            queries,
            key_table,
            preferred_element_type=jnp.float32,
        )
        * scaling
    )
    extent = scores.shape[-1]
    causal = jnp.arange(extent)[:, None] >= jnp.arange(extent)[None, :]
    scores = jnp.where(causal, scores, -1e30)
    peak = jnp.max(scores, axis=-1, keepdims=True)
    weights = jnp.exp(scores - peak)
    prob_table = weights / jnp.sum(weights, axis=-1, keepdims=True)
    rounded = prob_table.astype(jnp.bfloat16)
    output = jnp.einsum(
        scores_form + "," + keyed + "->" + layout,
        rounded,
        values,
        preferred_element_type=jnp.float32,
    )
    return (output.astype(jnp.bfloat16), prob_table)


def attend_back(queries, key_table, values, prob_table, upstream_part, layout, scores_form):
    keyed = layout.replace("l", "m")
    scaling = HEAD_DIM ** (-0.5)
    grad_prob = jnp.einsum(
        layout + "," + keyed + "->" + scores_form,
        upstream_part,
        values,
        preferred_element_type=jnp.float32,
    )
    row_inner = jnp.sum(prob_table * grad_prob, axis=-1, keepdims=True)
    grad_score = (prob_table * (grad_prob - row_inner) * scaling).astype(jnp.bfloat16)
    grad_query = jnp.einsum(
        scores_form + "," + keyed + "->" + layout,
        grad_score,
        key_table,
        preferred_element_type=jnp.float32,
    )
    grad_key = jnp.einsum(
        scores_form + "," + layout + "->" + keyed,
        grad_score,
        queries,
        preferred_element_type=jnp.float32,
    )
    rounded = prob_table.astype(jnp.bfloat16)
    grad_value = jnp.einsum(
        scores_form + "," + layout + "->" + keyed,
        rounded,
        upstream_part,
        preferred_element_type=jnp.float32,
    )
    return (
        grad_query.astype(jnp.bfloat16),
        grad_key.astype(jnp.bfloat16),
        grad_value.astype(jnp.bfloat16),
    )


def to_cols(rows_block):
    b, one, c, f = rows_block.shape
    n = lax.axis_size("seq")
    grouped = rows_block.reshape(b, n, c // n, f)
    return lax.all_to_all(grouped, "seq", split_axis=1, concat_axis=1, tiled=True)


def to_rows(cols_block):
    b, n, share, f = cols_block.shape
    gathered = lax.all_to_all(cols_block, "seq", split_axis=1, concat_axis=1, tiled=True)
    return gathered.reshape(b, 1, n * share, f)

def split_orders(seq_n, dp_n, z_first=False):
    bits = seq_n.bit_length() - 1
    dp_bits = dp_n.bit_length() - 1
    assert 1 << bits == seq_n and 1 << dp_bits == dp_n and bits >= 1
    seq_rest = [("s", k) for k in range(1, bits)]
    dp_all = [("d", k) for k in range(dp_bits)]
    even = seq_rest[:1] + dp_all[:1] + seq_rest[1:] + dp_all[1:]
    odd = list(even)
    if bits >= 3 and dp_bits >= 1:
        odd = dp_all[:1] + [seq_rest[1], seq_rest[0]] + seq_rest[2:] + dp_all[1:]
        if z_first:
            even = [seq_rest[1], seq_rest[0]] + dp_all[:1] + seq_rest[2:] + dp_all[1:]
            odd = [seq_rest[1]] + dp_all[:1] + [seq_rest[0]] + seq_rest[2:] + dp_all[1:]
    assert sorted(even) == sorted(odd)
    return even, odd


def by_split_order(matrix, orders, core_odd, seq_n, dp_n):
    bits = seq_n.bit_length() - 1
    dp_bits = dp_n.bit_length() - 1
    lead = matrix.shape[0]
    sub = matrix.shape[1] // (seq_n * dp_n)
    grid = matrix.reshape((lead,) + (2,) * (bits + dp_bits) + (sub,))

    def axis_of(item):
        kind, k = item
        return 1 + (bits - 1 - k) if kind == "s" else 1 + bits + (dp_bits - 1 - k)

    def arrange(order):
        axes = (0, axis_of(("s", 0))) + tuple(axis_of(item) for item in order) + (bits + dp_bits + 1,)
        return jnp.transpose(grid, axes).reshape(matrix.shape)

    even, odd = orders
    if even == odd:
        return arrange(even)
    return jnp.where(core_odd, arrange(odd), arrange(even))


def reduce_rows(parts, part_orders, seq_n, dp_n, tie):
    seq_at = lax.axis_index("seq")
    dp_at = lax.axis_index("dp")
    steps = len(part_orders[0][0])
    accs = tuple(p.reshape((2,) * steps + (p.shape[0] >> steps, p.shape[1])) for p in parts)

    def bit_value(item, seq_i, dp_i):
        kind, k = item
        return ((seq_i if kind == "s" else dp_i) >> k) & 1

    def flip(item, seq_i, dp_i):
        kind, k = item
        if kind == "s":
            return seq_i ^ (1 << k), dp_i
        return seq_i, dp_i ^ (1 << k)

    def traced_bit(item):
        kind, k = item
        return ((seq_at if kind == "s" else dp_at) // (1 << k)) % 2

    for step in range(steps):
        perms, kepts, givens = [], [], []
        for acc, (even, odd) in zip(accs, part_orders):
            perm = []
            for dp_i in range(dp_n):
                for seq_i in range(seq_n):
                    item = (odd if seq_i % 2 else even)[step]
                    seq_j, dp_j = flip(item, seq_i, dp_i)
                    perm.append((dp_i * seq_n + seq_i, dp_j * seq_n + seq_j))
            keep_at = jnp.where(seq_at % 2 == 1, traced_bit(odd[step]), traced_bit(even[step]))
            perms.append(perm)
            kepts.append(lax.dynamic_index_in_dim(acc, keep_at, 0, keepdims=False))
            givens.append(
                lax.dynamic_index_in_dim(acc, 1 - keep_at, 0, keepdims=False).astype(jnp.bfloat16)
            )
        if step == 0:
            givens, tie = lax.optimization_barrier((givens, tie))
        accs = tuple(
            kept + lax.ppermute(given, ("dp", "seq"), perm).astype(jnp.float32)
            for kept, given, perm in zip(kepts, givens, perms)
        )
    accs = tuple(acc.astype(jnp.bfloat16) for acc in accs)
    for step in range(dp_n.bit_length() - 1):
        perm = [(member, member ^ (1 << step)) for member in range(dp_n)]
        got = lax.ppermute(accs, "dp", perm)
        upper = (dp_at // (1 << step)) % 2 == 1
        accs = tuple(
            jnp.where(upper, jnp.concatenate([g, acc], axis=0), jnp.concatenate([acc, g], axis=0))
            for acc, g in zip(accs, got)
        )
    return accs, tie


def on_device(first_query, first_key, first_value, out_weight, norm_gain, joint_weight, upstream):
    batches, local_rows, columns, feature = first_query.shape
    head_count = feature // HEAD_DIM
    model_width = out_weight.shape[1]
    groups = batches * local_rows

    def to_heads(tensor):
        return tensor.reshape(groups, columns, head_count, HEAD_DIM)

    out_first, probs_first = attend(
        to_heads(first_query), to_heads(first_key), to_heads(first_value), "glhe", "ghlm"
    )
    flat_first = out_first.reshape(groups * columns, feature)
    hidden = jnp.dot(flat_first, out_weight, preferred_element_type=jnp.float32)
    inverse = lax.rsqrt(jnp.mean(hidden * hidden, axis=-1, keepdims=True) + epsilon)
    normed = (hidden * inverse * norm_gain).astype(jnp.bfloat16)
    normed_cols = to_cols(normed.reshape(batches, local_rows, columns, model_width))
    joint_flat = jnp.dot(
        normed_cols.reshape(-1, model_width), joint_weight, preferred_element_type=jnp.float32
    )
    joint_cols = joint_flat.astype(jnp.bfloat16).reshape(
        batches, normed_cols.shape[1], normed_cols.shape[2], 3 * feature
    )
    all_rows, col_share = (joint_cols.shape[1], joint_cols.shape[2])
    pieces = joint_cols.reshape(batches, all_rows, col_share, 3, head_count, HEAD_DIM)
    query_cols, key_cols, value_cols = (pieces[:, :, :, 0], pieces[:, :, :, 1], pieces[:, :, :, 2])
    out_cols, probs_cols = attend(query_cols, key_cols, value_cols, "blche", "bchlm")
    upstream_cols = to_cols(upstream)
    upstream_cols = upstream_cols.reshape(batches, all_rows, col_share, head_count, HEAD_DIM)
    grads_cols = attend_back(
        query_cols, key_cols, value_cols, probs_cols, upstream_cols, "blche", "bchlm"
    )
    stacked = jnp.stack(grads_cols, axis=3).reshape(batches, all_rows, col_share, 3 * feature)
    used_normed = normed_cols.reshape(-1, model_width)
    used_grads = stacked.reshape(-1, 3 * feature)
    grad_local = jnp.dot(used_grads, joint_weight.T, preferred_element_type=jnp.float32).astype(
        jnp.bfloat16
    )
    seq_n = lax.axis_size("seq")
    dp_n = lax.axis_size("dp")
    orders = split_orders(seq_n, dp_n)
    out_orders = split_orders(seq_n, dp_n, z_first=True)
    core_odd = lax.axis_index("seq") % 2 == 1
    pair = [(member, member ^ 1) for member in range(seq_n)]
    core = lax.axis_index("seq") % 2

    def my_half(factor, orders=orders):
        arranged = by_split_order(factor, orders, core_odd, seq_n, dp_n)
        half = arranged.shape[1] // 2
        return lax.dynamic_slice_in_dim(arranged, core * half, half, axis=1)

    normed_peer, grads_peer = lax.ppermute((used_normed, used_grads), "seq", pair)
    joint_term = jnp.dot(
        my_half(jnp.concatenate([used_normed, normed_peer], axis=0)).T,
        jnp.concatenate([used_grads, grads_peer], axis=0),
        preferred_element_type=jnp.float32,
    )
    grad_normed = to_rows(grad_local.reshape(batches, all_rows, col_share, model_width))
    grad_normed = grad_normed.reshape(-1, model_width)
    (joint_sum,), grad_normed = reduce_rows((joint_term,), (orders,), seq_n, dp_n, grad_normed)
    grad_float = grad_normed.astype(jnp.float32)
    gain_term = jnp.sum(grad_float * hidden * inverse, axis=0)
    scaled = norm_gain * grad_float
    grad_hidden = (
        inverse * scaled - hidden * inverse**3 * jnp.mean(scaled * hidden, axis=-1, keepdims=True)
    ).astype(jnp.bfloat16)
    first_peer, hidden_peer, gain_peer = lax.ppermute((flat_first, grad_hidden, gain_term), "seq", pair)
    out_term = jnp.dot(
        my_half(jnp.concatenate([flat_first, first_peer], axis=0), out_orders).T,
        jnp.concatenate([grad_hidden, hidden_peer], axis=0),
        preferred_element_type=jnp.float32,
    )
    gain_term = my_half((gain_term + gain_peer)[None, :], out_orders)[0][:, None]
    out_width = out_term.shape[1]
    (out_sum,), out_cols = reduce_rows(
        (jnp.concatenate([out_term, gain_term], axis=1),), (out_orders,), seq_n, dp_n, out_cols
    )
    column_out = to_rows(out_cols.reshape(batches, all_rows, col_share, feature))
    replicas = (joint_sum, out_sum[:, :out_width], out_sum[:, out_width].astype(jnp.float32))
    grad_first = jnp.dot(grad_hidden, out_weight.T, preferred_element_type=jnp.float32).astype(
        jnp.bfloat16
    )
    grads_rows = attend_back(
        to_heads(first_query),
        to_heads(first_key),
        to_heads(first_value),
        probs_first,
        to_heads(grad_first),
        "glhe",
        "ghlm",
    )
    grad_query = grads_rows[0].reshape(batches, local_rows, columns, feature)
    grad_key = grads_rows[1].reshape(batches, local_rows, columns, feature)
    grad_value = grads_rows[2].reshape(batches, local_rows, columns, feature)
    return (
        grad_query,
        grad_key,
        grad_value,
        column_out,
        replicas[0].astype(jnp.bfloat16),
        replicas[1].astype(jnp.bfloat16),
        replicas[2],
    )


def solution(mesh):
    placed = (
        P("dp", "seq", None, None),
        P("dp", "seq", None, None),
        P("dp", "seq", None, None),
        P(),
        P(),
        P(),
        P("dp", "seq", None, None),
    )
    return jax.shard_map(
        on_device,
        mesh=mesh,
        in_specs=placed,
        out_specs=(
            P("dp", "seq", None, None),
            P("dp", "seq", None, None),
            P("dp", "seq", None, None),
            P("dp", "seq", None, None),
            P("seq", None),
            P("seq", None),
            P("seq"),
        ),
        check_vma=False,
    )
```

```python
import jax
import jax.numpy as jnp
from jax import lax
from jax.sharding import PartitionSpec as P

HEAD_DIM = 128


epsilon = 1e-06


def attend(queries, key_table, values, layout, scores_form):
    keyed = layout.replace("l", "m")
    scaling = HEAD_DIM ** (-0.5)
    scores = (
        jnp.einsum(
            layout + "," + keyed + "->" + scores_form,
            queries,
            key_table,
            preferred_element_type=jnp.float32,
        )
        * scaling
    )
    extent = scores.shape[-1]
    causal = jnp.arange(extent)[:, None] >= jnp.arange(extent)[None, :]
    scores = jnp.where(causal, scores, -1e30)
    peak = jnp.max(scores, axis=-1, keepdims=True)
    weights = jnp.exp(scores - peak)
    prob_table = weights / jnp.sum(weights, axis=-1, keepdims=True)
    rounded = prob_table.astype(jnp.bfloat16)
    output = jnp.einsum(
        scores_form + "," + keyed + "->" + layout,
        rounded,
        values,
        preferred_element_type=jnp.float32,
    )
    return (output.astype(jnp.bfloat16), prob_table)


def attend_back(queries, key_table, values, prob_table, upstream_part, layout, scores_form):
    keyed = layout.replace("l", "m")
    scaling = HEAD_DIM ** (-0.5)
    grad_prob = jnp.einsum(
        layout + "," + keyed + "->" + scores_form,
        upstream_part,
        values,
        preferred_element_type=jnp.float32,
    )
    row_inner = jnp.sum(prob_table * grad_prob, axis=-1, keepdims=True)
    grad_score = (prob_table * (grad_prob - row_inner) * scaling).astype(jnp.bfloat16)
    grad_query = jnp.einsum(
        scores_form + "," + keyed + "->" + layout,
        grad_score,
        key_table,
        preferred_element_type=jnp.float32,
    )
    grad_key = jnp.einsum(
        scores_form + "," + layout + "->" + keyed,
        grad_score,
        queries,
        preferred_element_type=jnp.float32,
    )
    rounded = prob_table.astype(jnp.bfloat16)
    grad_value = jnp.einsum(
        scores_form + "," + layout + "->" + keyed,
        rounded,
        upstream_part,
        preferred_element_type=jnp.float32,
    )
    return (
        grad_query.astype(jnp.bfloat16),
        grad_key.astype(jnp.bfloat16),
        grad_value.astype(jnp.bfloat16),
    )


def split_orders(seq_n, dp_n, z_first=False):
    bits = seq_n.bit_length() - 1
    dp_bits = dp_n.bit_length() - 1
    assert 1 << bits == seq_n and 1 << dp_bits == dp_n and bits >= 1
    seq_rest = [("s", k) for k in range(1, bits)]
    dp_all = [("d", k) for k in range(dp_bits)]
    even = seq_rest[:1] + dp_all[:1] + seq_rest[1:] + dp_all[1:]
    odd = list(even)
    if bits >= 3 and dp_bits >= 1:
        odd = dp_all[:1] + [seq_rest[1], seq_rest[0]] + seq_rest[2:] + dp_all[1:]
        if z_first:
            even = [seq_rest[1], seq_rest[0]] + dp_all[:1] + seq_rest[2:] + dp_all[1:]
            odd = [seq_rest[1]] + dp_all[:1] + [seq_rest[0]] + seq_rest[2:] + dp_all[1:]
    assert sorted(even) == sorted(odd)
    return even, odd


def by_split_order(matrix, orders, core_odd, seq_n, dp_n):
    bits = seq_n.bit_length() - 1
    dp_bits = dp_n.bit_length() - 1
    lead = matrix.shape[0]
    sub = matrix.shape[1] // (seq_n * dp_n)
    grid = matrix.reshape((lead,) + (2,) * (bits + dp_bits) + (sub,))

    def axis_of(item):
        kind, k = item
        return 1 + (bits - 1 - k) if kind == "s" else 1 + bits + (dp_bits - 1 - k)

    def arrange(order):
        axes = (0, axis_of(("s", 0))) + tuple(axis_of(item) for item in order) + (bits + dp_bits + 1,)
        return jnp.transpose(grid, axes).reshape(matrix.shape)

    even, odd = orders
    if even == odd:
        return arrange(even)
    return jnp.where(core_odd, arrange(odd), arrange(even))


def reduce_rows(parts, part_orders, seq_n, dp_n, tie):
    seq_at = lax.axis_index("seq")
    dp_at = lax.axis_index("dp")
    steps = len(part_orders[0][0])
    accs = tuple(p.reshape((2,) * steps + (p.shape[0] >> steps, p.shape[1])) for p in parts)

    def bit_value(item, seq_i, dp_i):
        kind, k = item
        return ((seq_i if kind == "s" else dp_i) >> k) & 1

    def flip(item, seq_i, dp_i):
        kind, k = item
        if kind == "s":
            return seq_i ^ (1 << k), dp_i
        return seq_i, dp_i ^ (1 << k)

    def traced_bit(item):
        kind, k = item
        return ((seq_at if kind == "s" else dp_at) // (1 << k)) % 2

    for step in range(steps):
        perms, kepts, givens = [], [], []
        for acc, (even, odd) in zip(accs, part_orders):
            perm = []
            for dp_i in range(dp_n):
                for seq_i in range(seq_n):
                    item = (odd if seq_i % 2 else even)[step]
                    seq_j, dp_j = flip(item, seq_i, dp_i)
                    perm.append((dp_i * seq_n + seq_i, dp_j * seq_n + seq_j))
            keep_at = jnp.where(seq_at % 2 == 1, traced_bit(odd[step]), traced_bit(even[step]))
            perms.append(perm)
            kepts.append(lax.dynamic_index_in_dim(acc, keep_at, 0, keepdims=False))
            givens.append(
                lax.dynamic_index_in_dim(acc, 1 - keep_at, 0, keepdims=False).astype(jnp.bfloat16)
            )
        if step == 0:
            givens, tie = lax.optimization_barrier((givens, tie))
        accs = tuple(
            kept + lax.ppermute(given, ("dp", "seq"), perm).astype(jnp.float32)
            for kept, given, perm in zip(kepts, givens, perms)
        )
    accs = tuple(acc.astype(jnp.bfloat16) for acc in accs)
    for step in range(dp_n.bit_length() - 1):
        perm = [(member, member ^ (1 << step)) for member in range(dp_n)]
        got = lax.ppermute(accs, "dp", perm)
        upper = (dp_at // (1 << step)) % 2 == 1
        accs = tuple(
            jnp.where(upper, jnp.concatenate([g, acc], axis=0), jnp.concatenate([acc, g], axis=0))
            for acc, g in zip(accs, got)
        )
    return accs, tie


def on_device(first_query, first_key, first_value, out_weight, norm_gain, joint_weight, upstream):
    batches, local_rows, columns, feature = first_query.shape
    head_count = feature // HEAD_DIM
    model_width = out_weight.shape[1]
    groups = batches * local_rows

    def to_heads(tensor):
        return tensor.reshape(groups, columns, head_count, HEAD_DIM)

    out_first, probs_first = attend(
        to_heads(first_query), to_heads(first_key), to_heads(first_value), "glhe", "ghlm"
    )
    flat_first = out_first.reshape(groups * columns, feature)
    hidden = jnp.dot(flat_first, out_weight, preferred_element_type=jnp.float32)
    inverse = lax.rsqrt(jnp.mean(hidden * hidden, axis=-1, keepdims=True) + epsilon)
    normed = (hidden * inverse * norm_gain).astype(jnp.bfloat16)
    normed_cols = lax.all_to_all(
        normed.reshape(batches, local_rows, columns, model_width),
        "seq",
        split_axis=2,
        concat_axis=1,
        tiled=True,
    )
    joint_flat = jnp.dot(
        normed_cols.reshape(-1, model_width), joint_weight, preferred_element_type=jnp.float32
    )
    joint_cols = joint_flat.astype(jnp.bfloat16).reshape(
        batches, normed_cols.shape[1], normed_cols.shape[2], 3 * feature
    )
    all_rows, col_share = (joint_cols.shape[1], joint_cols.shape[2])
    pieces = joint_cols.reshape(batches, all_rows, col_share, 3, head_count, HEAD_DIM)
    query_cols, key_cols, value_cols = (pieces[:, :, :, 0], pieces[:, :, :, 1], pieces[:, :, :, 2])
    out_cols, probs_cols = attend(query_cols, key_cols, value_cols, "blche", "bchlm")
    upstream_cols = lax.all_to_all(upstream, "seq", split_axis=2, concat_axis=1, tiled=True)
    upstream_cols = upstream_cols.reshape(batches, all_rows, col_share, head_count, HEAD_DIM)
    grads_cols = attend_back(
        query_cols, key_cols, value_cols, probs_cols, upstream_cols, "blche", "bchlm"
    )
    stacked = jnp.stack(grads_cols, axis=3).reshape(batches, all_rows, col_share, 3 * feature)
    used_normed = normed_cols.reshape(-1, model_width)
    used_grads = stacked.reshape(-1, 3 * feature)
    grad_local = jnp.dot(used_grads, joint_weight.T, preferred_element_type=jnp.float32).astype(
        jnp.bfloat16
    )
    seq_n = lax.axis_size("seq")
    dp_n = lax.axis_size("dp")
    orders = split_orders(seq_n, dp_n)
    out_orders = split_orders(seq_n, dp_n, z_first=True)
    core_odd = lax.axis_index("seq") % 2 == 1
    pair = [(member, member ^ 1) for member in range(seq_n)]
    core = lax.axis_index("seq") % 2

    def my_half(factor, orders=orders):
        arranged = by_split_order(factor, orders, core_odd, seq_n, dp_n)
        half = arranged.shape[1] // 2
        return lax.dynamic_slice_in_dim(arranged, core * half, half, axis=1)

    normed_peer, grads_peer = lax.ppermute((used_normed, used_grads), "seq", pair)
    joint_term = jnp.dot(
        my_half(jnp.concatenate([used_normed, normed_peer], axis=0)).T,
        jnp.concatenate([used_grads, grads_peer], axis=0),
        preferred_element_type=jnp.float32,
    )
    (joint_sum,), grad_local = reduce_rows((joint_term,), (orders,), seq_n, dp_n, grad_local)
    grad_normed = lax.all_to_all(
        grad_local.reshape(batches, all_rows, col_share, model_width),
        "seq",
        split_axis=1,
        concat_axis=2,
        tiled=True,
    )
    grad_normed = grad_normed.reshape(-1, model_width)
    grad_float = grad_normed.astype(jnp.float32)
    gain_term = jnp.sum(grad_float * hidden * inverse, axis=0)
    scaled = norm_gain * grad_float
    grad_hidden = (
        inverse * scaled - hidden * inverse**3 * jnp.mean(scaled * hidden, axis=-1, keepdims=True)
    ).astype(jnp.bfloat16)
    first_peer, hidden_peer, gain_peer = lax.ppermute((flat_first, grad_hidden, gain_term), "seq", pair)
    out_term = jnp.dot(
        my_half(jnp.concatenate([flat_first, first_peer], axis=0), out_orders).T,
        jnp.concatenate([grad_hidden, hidden_peer], axis=0),
        preferred_element_type=jnp.float32,
    )
    gain_term = my_half((gain_term + gain_peer)[None, :], out_orders)[0][:, None]
    out_width = out_term.shape[1]
    (out_sum,), out_cols = reduce_rows(
        (jnp.concatenate([out_term, gain_term], axis=1),), (out_orders,), seq_n, dp_n, out_cols
    )
    column_out = lax.all_to_all(
        out_cols.reshape(batches, all_rows, col_share, feature),
        "seq",
        split_axis=1,
        concat_axis=2,
        tiled=True,
    )
    replicas = (joint_sum, out_sum[:, :out_width], out_sum[:, out_width].astype(jnp.float32))
    grad_first = jnp.dot(grad_hidden, out_weight.T, preferred_element_type=jnp.float32).astype(
        jnp.bfloat16
    )
    grads_rows = attend_back(
        to_heads(first_query),
        to_heads(first_key),
        to_heads(first_value),
        probs_first,
        to_heads(grad_first),
        "glhe",
        "ghlm",
    )
    grad_query = grads_rows[0].reshape(batches, local_rows, columns, feature)
    grad_key = grads_rows[1].reshape(batches, local_rows, columns, feature)
    grad_value = grads_rows[2].reshape(batches, local_rows, columns, feature)
    return (
        grad_query,
        grad_key,
        grad_value,
        column_out,
        replicas[0].astype(jnp.bfloat16),
        replicas[1].astype(jnp.bfloat16),
        replicas[2],
    )


def solution(mesh):
    placed = (
        P("dp", "seq", None, None),
        P("dp", "seq", None, None),
        P("dp", "seq", None, None),
        P(),
        P(),
        P(),
        P("dp", "seq", None, None),
    )
    return jax.shard_map(
        on_device,
        mesh=mesh,
        in_specs=placed,
        out_specs=(
            P("dp", "seq", None, None),
            P("dp", "seq", None, None),
            P("dp", "seq", None, None),
            P("dp", "seq", None, None),
            P("seq", None),
            P("seq", None),
            P("seq"),
        ),
        check_vma=False,
    )
```

```python
import jax
import jax.numpy as jnp
from jax import lax
from jax.sharding import PartitionSpec as P

HEAD_DIM = 128


epsilon = 1e-06


def attend(queries, key_table, values, layout, scores_form):
    keyed = layout.replace("l", "m")
    scaling = HEAD_DIM ** (-0.5)
    scores = (
        jnp.einsum(
            layout + "," + keyed + "->" + scores_form,
            queries,
            key_table,
            preferred_element_type=jnp.float32,
        )
        * scaling
    )
    extent = scores.shape[-1]
    causal = jnp.arange(extent)[:, None] >= jnp.arange(extent)[None, :]
    scores = jnp.where(causal, scores, -1e30)
    peak = jnp.max(scores, axis=-1, keepdims=True)
    weights = jnp.exp(scores - peak)
    prob_table = weights / jnp.sum(weights, axis=-1, keepdims=True)
    rounded = prob_table.astype(jnp.bfloat16)
    output = jnp.einsum(
        scores_form + "," + keyed + "->" + layout,
        rounded,
        values,
        preferred_element_type=jnp.float32,
    )
    return (output.astype(jnp.bfloat16), prob_table)


def attend_back(queries, key_table, values, prob_table, upstream_part, layout, scores_form):
    keyed = layout.replace("l", "m")
    scaling = HEAD_DIM ** (-0.5)
    grad_prob = jnp.einsum(
        layout + "," + keyed + "->" + scores_form,
        upstream_part,
        values,
        preferred_element_type=jnp.float32,
    )
    row_inner = jnp.sum(prob_table * grad_prob, axis=-1, keepdims=True)
    grad_score = (prob_table * (grad_prob - row_inner) * scaling).astype(jnp.bfloat16)
    grad_query = jnp.einsum(
        scores_form + "," + keyed + "->" + layout,
        grad_score,
        key_table,
        preferred_element_type=jnp.float32,
    )
    grad_key = jnp.einsum(
        scores_form + "," + layout + "->" + keyed,
        grad_score,
        queries,
        preferred_element_type=jnp.float32,
    )
    rounded = prob_table.astype(jnp.bfloat16)
    grad_value = jnp.einsum(
        scores_form + "," + layout + "->" + keyed,
        rounded,
        upstream_part,
        preferred_element_type=jnp.float32,
    )
    return (
        grad_query.astype(jnp.bfloat16),
        grad_key.astype(jnp.bfloat16),
        grad_value.astype(jnp.bfloat16),
    )


def split_orders(seq_n, dp_n, z_first=False):
    bits = seq_n.bit_length() - 1
    dp_bits = dp_n.bit_length() - 1
    assert 1 << bits == seq_n and 1 << dp_bits == dp_n and bits >= 1
    seq_rest = [("s", k) for k in range(1, bits)]
    dp_all = [("d", k) for k in range(dp_bits)]
    even = seq_rest[:1] + dp_all[:1] + seq_rest[1:] + dp_all[1:]
    odd = list(even)
    if bits >= 3 and dp_bits >= 1:
        odd = dp_all[:1] + [seq_rest[1], seq_rest[0]] + seq_rest[2:] + dp_all[1:]
        if z_first:
            even = [seq_rest[1], seq_rest[0]] + dp_all[:1] + seq_rest[2:] + dp_all[1:]
            odd = [seq_rest[1]] + dp_all[:1] + [seq_rest[0]] + seq_rest[2:] + dp_all[1:]
    assert sorted(even) == sorted(odd)
    return even, odd


def by_split_order(matrix, orders, core_odd, seq_n, dp_n):
    bits = seq_n.bit_length() - 1
    dp_bits = dp_n.bit_length() - 1
    lead = matrix.shape[0]
    sub = matrix.shape[1] // (seq_n * dp_n)
    grid = matrix.reshape((lead,) + (2,) * (bits + dp_bits) + (sub,))

    def axis_of(item):
        kind, k = item
        return 1 + (bits - 1 - k) if kind == "s" else 1 + bits + (dp_bits - 1 - k)

    def arrange(order):
        axes = (0, axis_of(("s", 0))) + tuple(axis_of(item) for item in order) + (bits + dp_bits + 1,)
        return jnp.transpose(grid, axes).reshape(matrix.shape)

    even, odd = orders
    if even == odd:
        return arrange(even)
    return jnp.where(core_odd, arrange(odd), arrange(even))


def reduce_rows(parts, part_orders, seq_n, dp_n, tie):
    seq_at = lax.axis_index("seq")
    dp_at = lax.axis_index("dp")
    steps = len(part_orders[0][0])
    accs = tuple(p.reshape((2,) * steps + (p.shape[0] >> steps, p.shape[1])) for p in parts)

    def bit_value(item, seq_i, dp_i):
        kind, k = item
        return ((seq_i if kind == "s" else dp_i) >> k) & 1

    def flip(item, seq_i, dp_i):
        kind, k = item
        if kind == "s":
            return seq_i ^ (1 << k), dp_i
        return seq_i, dp_i ^ (1 << k)

    def traced_bit(item):
        kind, k = item
        return ((seq_at if kind == "s" else dp_at) // (1 << k)) % 2

    for step in range(steps):
        perms, kepts, givens = [], [], []
        for acc, (even, odd) in zip(accs, part_orders):
            perm = []
            for dp_i in range(dp_n):
                for seq_i in range(seq_n):
                    item = (odd if seq_i % 2 else even)[step]
                    seq_j, dp_j = flip(item, seq_i, dp_i)
                    perm.append((dp_i * seq_n + seq_i, dp_j * seq_n + seq_j))
            keep_at = jnp.where(seq_at % 2 == 1, traced_bit(odd[step]), traced_bit(even[step]))
            perms.append(perm)
            kepts.append(lax.dynamic_index_in_dim(acc, keep_at, 0, keepdims=False))
            givens.append(
                lax.dynamic_index_in_dim(acc, 1 - keep_at, 0, keepdims=False).astype(jnp.bfloat16)
            )
        if step == 0:
            givens, tie = lax.optimization_barrier((givens, tie))
        accs = tuple(
            kept + lax.ppermute(given, ("dp", "seq"), perm).astype(jnp.float32)
            for kept, given, perm in zip(kepts, givens, perms)
        )
    accs = tuple(acc.astype(jnp.bfloat16) for acc in accs)
    for step in range(dp_n.bit_length() - 1):
        perm = [(member, member ^ (1 << step)) for member in range(dp_n)]
        got = lax.ppermute(accs, "dp", perm)
        upper = (dp_at // (1 << step)) % 2 == 1
        accs = tuple(
            jnp.concatenate([jnp.where(upper, g, acc), jnp.where(upper, acc, g)], axis=0)
            for acc, g in zip(accs, got)
        )
    return accs, tie


def on_device(first_query, first_key, first_value, out_weight, norm_gain, joint_weight, upstream):
    batches, local_rows, columns, feature = first_query.shape
    head_count = feature // HEAD_DIM
    model_width = out_weight.shape[1]
    groups = batches * local_rows

    def to_heads(tensor):
        return tensor.reshape(groups, columns, head_count, HEAD_DIM)

    out_first, probs_first = attend(
        to_heads(first_query), to_heads(first_key), to_heads(first_value), "glhe", "ghlm"
    )
    flat_first = out_first.reshape(groups * columns, feature)
    hidden = jnp.dot(flat_first, out_weight, preferred_element_type=jnp.float32)
    inverse = lax.rsqrt(jnp.mean(hidden * hidden, axis=-1, keepdims=True) + epsilon)
    normed = (hidden * inverse * norm_gain).astype(jnp.bfloat16)
    normed_cols = lax.all_to_all(
        normed.reshape(batches, local_rows, columns, model_width),
        "seq",
        split_axis=2,
        concat_axis=1,
        tiled=True,
    )
    joint_flat = jnp.dot(
        normed_cols.reshape(-1, model_width), joint_weight, preferred_element_type=jnp.float32
    )
    joint_cols = joint_flat.astype(jnp.bfloat16).reshape(
        batches, normed_cols.shape[1], normed_cols.shape[2], 3 * feature
    )
    all_rows, col_share = (joint_cols.shape[1], joint_cols.shape[2])
    pieces = joint_cols.reshape(batches, all_rows, col_share, 3, head_count, HEAD_DIM)
    query_cols, key_cols, value_cols = (pieces[:, :, :, 0], pieces[:, :, :, 1], pieces[:, :, :, 2])
    out_cols, probs_cols = attend(query_cols, key_cols, value_cols, "blche", "bchlm")
    upstream_cols = lax.all_to_all(upstream, "seq", split_axis=2, concat_axis=1, tiled=True)
    upstream_cols = upstream_cols.reshape(batches, all_rows, col_share, head_count, HEAD_DIM)
    grads_cols = attend_back(
        query_cols, key_cols, value_cols, probs_cols, upstream_cols, "blche", "bchlm"
    )
    stacked = jnp.stack(grads_cols, axis=3).reshape(batches, all_rows, col_share, 3 * feature)
    used_normed = normed_cols.reshape(-1, model_width)
    used_grads = stacked.reshape(-1, 3 * feature)
    grad_local = jnp.dot(used_grads, joint_weight.T, preferred_element_type=jnp.float32).astype(
        jnp.bfloat16
    )
    seq_n = lax.axis_size("seq")
    dp_n = lax.axis_size("dp")
    orders = split_orders(seq_n, dp_n)
    out_orders = split_orders(seq_n, dp_n, z_first=True)
    core_odd = lax.axis_index("seq") % 2 == 1
    pair = [(member, member ^ 1) for member in range(seq_n)]
    core = lax.axis_index("seq") % 2

    def my_half(factor, orders=orders):
        arranged = by_split_order(factor, orders, core_odd, seq_n, dp_n)
        half = arranged.shape[1] // 2
        return lax.dynamic_slice_in_dim(arranged, core * half, half, axis=1)

    normed_peer, grads_peer = lax.ppermute((used_normed, used_grads), "seq", pair)
    joint_term = jnp.dot(
        my_half(jnp.concatenate([used_normed, normed_peer], axis=0)).T,
        jnp.concatenate([used_grads, grads_peer], axis=0),
        preferred_element_type=jnp.float32,
    )
    grad_normed = lax.all_to_all(
        grad_local.reshape(batches, all_rows, col_share, model_width),
        "seq",
        split_axis=1,
        concat_axis=2,
        tiled=True,
    )
    grad_normed = grad_normed.reshape(-1, model_width)
    (joint_sum,), grad_normed = reduce_rows((joint_term,), (orders,), seq_n, dp_n, grad_normed)
    grad_float = grad_normed.astype(jnp.float32)
    gain_term = jnp.sum(grad_float * hidden * inverse, axis=0)
    scaled = norm_gain * grad_float
    grad_hidden = (
        inverse * scaled - hidden * inverse**3 * jnp.mean(scaled * hidden, axis=-1, keepdims=True)
    ).astype(jnp.bfloat16)
    first_peer, hidden_peer, gain_peer = lax.ppermute((flat_first, grad_hidden, gain_term), "seq", pair)
    out_term = jnp.dot(
        my_half(jnp.concatenate([flat_first, first_peer], axis=0), out_orders).T,
        jnp.concatenate([grad_hidden, hidden_peer], axis=0),
        preferred_element_type=jnp.float32,
    )
    gain_term = my_half((gain_term + gain_peer)[None, :], out_orders)[0][:, None]
    out_width = out_term.shape[1]
    (out_sum,), out_cols = reduce_rows(
        (jnp.concatenate([out_term, gain_term], axis=1),), (out_orders,), seq_n, dp_n, out_cols
    )
    column_out = lax.all_to_all(
        out_cols.reshape(batches, all_rows, col_share, feature),
        "seq",
        split_axis=1,
        concat_axis=2,
        tiled=True,
    )
    replicas = (joint_sum, out_sum[:, :out_width], out_sum[:, out_width].astype(jnp.float32))
    grad_first = jnp.dot(grad_hidden, out_weight.T, preferred_element_type=jnp.float32).astype(
        jnp.bfloat16
    )
    grads_rows = attend_back(
        to_heads(first_query),
        to_heads(first_key),
        to_heads(first_value),
        probs_first,
        to_heads(grad_first),
        "glhe",
        "ghlm",
    )
    grad_query = grads_rows[0].reshape(batches, local_rows, columns, feature)
    grad_key = grads_rows[1].reshape(batches, local_rows, columns, feature)
    grad_value = grads_rows[2].reshape(batches, local_rows, columns, feature)
    return (
        grad_query,
        grad_key,
        grad_value,
        column_out,
        replicas[0].astype(jnp.bfloat16),
        replicas[1].astype(jnp.bfloat16),
        replicas[2],
    )


def solution(mesh):
    placed = (
        P("dp", "seq", None, None),
        P("dp", "seq", None, None),
        P("dp", "seq", None, None),
        P(),
        P(),
        P(),
        P("dp", "seq", None, None),
    )
    return jax.shard_map(
        on_device,
        mesh=mesh,
        in_specs=placed,
        out_specs=(
            P("dp", "seq", None, None),
            P("dp", "seq", None, None),
            P("dp", "seq", None, None),
            P("dp", "seq", None, None),
            P("seq", None),
            P("seq", None),
            P("seq"),
        ),
        check_vma=False,
    )
```

```python
import jax
import jax.numpy as jnp
from jax import lax
from jax.sharding import PartitionSpec as P

HEAD_DIM = 128


epsilon = 1e-06


def attend(queries, key_table, values, layout, scores_form):
    keyed = layout.replace("l", "m")
    scaling = HEAD_DIM ** (-0.5)
    scores = (
        jnp.einsum(
            layout + "," + keyed + "->" + scores_form,
            queries,
            key_table,
            preferred_element_type=jnp.float32,
        )
        * scaling
    )
    extent = scores.shape[-1]
    causal = jnp.arange(extent)[:, None] >= jnp.arange(extent)[None, :]
    scores = jnp.where(causal, scores, -1e30)
    peak = jnp.max(scores, axis=-1, keepdims=True)
    weights = jnp.exp(scores - peak)
    prob_table = weights / jnp.sum(weights, axis=-1, keepdims=True)
    rounded = prob_table.astype(jnp.bfloat16)
    output = jnp.einsum(
        scores_form + "," + keyed + "->" + layout,
        rounded,
        values,
        preferred_element_type=jnp.float32,
    )
    return (output.astype(jnp.bfloat16), prob_table)


def attend_back(queries, key_table, values, prob_table, upstream_part, layout, scores_form):
    keyed = layout.replace("l", "m")
    scaling = HEAD_DIM ** (-0.5)
    grad_prob = jnp.einsum(
        layout + "," + keyed + "->" + scores_form,
        upstream_part,
        values,
        preferred_element_type=jnp.float32,
    )
    row_inner = jnp.sum(prob_table * grad_prob, axis=-1, keepdims=True)
    grad_score = (prob_table * (grad_prob - row_inner) * scaling).astype(jnp.bfloat16)
    grad_query = jnp.einsum(
        scores_form + "," + keyed + "->" + layout,
        grad_score,
        key_table,
        preferred_element_type=jnp.float32,
    )
    grad_key = jnp.einsum(
        scores_form + "," + layout + "->" + keyed,
        grad_score,
        queries,
        preferred_element_type=jnp.float32,
    )
    rounded = prob_table.astype(jnp.bfloat16)
    grad_value = jnp.einsum(
        scores_form + "," + layout + "->" + keyed,
        rounded,
        upstream_part,
        preferred_element_type=jnp.float32,
    )
    return (
        grad_query.astype(jnp.bfloat16),
        grad_key.astype(jnp.bfloat16),
        grad_value.astype(jnp.bfloat16),
    )


def split_orders(seq_n, dp_n, z_first=False):
    bits = seq_n.bit_length() - 1
    dp_bits = dp_n.bit_length() - 1
    assert 1 << bits == seq_n and 1 << dp_bits == dp_n and bits >= 1
    seq_rest = [("s", k) for k in range(1, bits)]
    dp_all = [("d", k) for k in range(dp_bits)]
    even = seq_rest[:1] + dp_all[:1] + seq_rest[1:] + dp_all[1:]
    odd = list(even)
    if bits >= 3 and dp_bits >= 1:
        odd = dp_all[:1] + [seq_rest[1], seq_rest[0]] + seq_rest[2:] + dp_all[1:]
        if z_first:
            even = [seq_rest[1], seq_rest[0]] + dp_all[:1] + seq_rest[2:] + dp_all[1:]
            odd = [seq_rest[1]] + dp_all[:1] + [seq_rest[0]] + seq_rest[2:] + dp_all[1:]
    assert sorted(even) == sorted(odd)
    return even, odd


def by_split_order(matrix, orders, core_odd, seq_n, dp_n):
    bits = seq_n.bit_length() - 1
    dp_bits = dp_n.bit_length() - 1
    lead = matrix.shape[0]
    sub = matrix.shape[1] // (seq_n * dp_n)
    grid = matrix.reshape((lead,) + (2,) * (bits + dp_bits) + (sub,))

    def axis_of(item):
        kind, k = item
        return 1 + (bits - 1 - k) if kind == "s" else 1 + bits + (dp_bits - 1 - k)

    def arrange(order):
        axes = (0, axis_of(("s", 0))) + tuple(axis_of(item) for item in order) + (bits + dp_bits + 1,)
        return jnp.transpose(grid, axes).reshape(matrix.shape)

    even, odd = orders
    if even == odd:
        return arrange(even)
    return jnp.where(core_odd, arrange(odd), arrange(even))


def reduce_rows(parts, part_orders, seq_n, dp_n, tie):
    seq_at = lax.axis_index("seq")
    dp_at = lax.axis_index("dp")
    steps = len(part_orders[0][0])
    accs = tuple(p.reshape((2,) * steps + (p.shape[0] >> steps, p.shape[1])) for p in parts)

    def bit_value(item, seq_i, dp_i):
        kind, k = item
        return ((seq_i if kind == "s" else dp_i) >> k) & 1

    def flip(item, seq_i, dp_i):
        kind, k = item
        if kind == "s":
            return seq_i ^ (1 << k), dp_i
        return seq_i, dp_i ^ (1 << k)

    def traced_bit(item):
        kind, k = item
        return ((seq_at if kind == "s" else dp_at) // (1 << k)) % 2

    for step in range(steps):
        perms, kepts, givens = [], [], []
        for acc, (even, odd) in zip(accs, part_orders):
            perm = []
            for dp_i in range(dp_n):
                for seq_i in range(seq_n):
                    item = (odd if seq_i % 2 else even)[step]
                    seq_j, dp_j = flip(item, seq_i, dp_i)
                    perm.append((dp_i * seq_n + seq_i, dp_j * seq_n + seq_j))
            keep_at = jnp.where(seq_at % 2 == 1, traced_bit(odd[step]), traced_bit(even[step]))
            perms.append(perm)
            kepts.append(lax.dynamic_index_in_dim(acc, keep_at, 0, keepdims=False))
            givens.append(
                lax.dynamic_index_in_dim(acc, 1 - keep_at, 0, keepdims=False).astype(jnp.bfloat16)
            )
        if step == 0:
            givens, tie = lax.optimization_barrier((givens, tie))
        accs = tuple(
            kept + lax.ppermute(given, ("dp", "seq"), perm).astype(jnp.float32)
            for kept, given, perm in zip(kepts, givens, perms)
        )
    accs = tuple(acc.astype(jnp.bfloat16) for acc in accs)
    for step in range(dp_n.bit_length() - 1):
        perm = [(member, member ^ (1 << step)) for member in range(dp_n)]
        got = lax.ppermute(accs, "dp", perm)
        upper = (dp_at // (1 << step)) % 2 == 1
        accs = tuple(
            jnp.where(upper, jnp.concatenate([g, acc], axis=0), jnp.concatenate([acc, g], axis=0))
            for acc, g in zip(accs, got)
        )
    return accs, tie


def on_device(first_query, first_key, first_value, out_weight, norm_gain, joint_weight, upstream):
    batches, local_rows, columns, feature = first_query.shape
    head_count = feature // HEAD_DIM
    model_width = out_weight.shape[1]
    groups = batches * local_rows

    def to_heads(tensor):
        return tensor.reshape(groups, columns, head_count, HEAD_DIM)

    out_first, probs_first = attend(
        to_heads(first_query), to_heads(first_key), to_heads(first_value), "glhe", "ghlm"
    )
    flat_first = out_first.reshape(groups * columns, feature)
    hidden = jnp.dot(flat_first, out_weight, preferred_element_type=jnp.float32)
    inverse = lax.rsqrt(jnp.mean(hidden * hidden, axis=-1, keepdims=True) + epsilon)
    normed = (hidden * inverse * norm_gain).astype(jnp.bfloat16)
    normed_cols = lax.all_to_all(
        normed.reshape(batches, local_rows, columns, model_width),
        "seq",
        split_axis=2,
        concat_axis=1,
        tiled=True,
    )
    joint_flat = jnp.dot(
        normed_cols.reshape(-1, model_width), joint_weight, preferred_element_type=jnp.float32
    )
    joint_cols = joint_flat.astype(jnp.bfloat16).reshape(
        batches, normed_cols.shape[1], normed_cols.shape[2], 3 * feature
    )
    all_rows, col_share = (joint_cols.shape[1], joint_cols.shape[2])
    pieces = joint_cols.reshape(batches, all_rows, col_share, 3, head_count, HEAD_DIM)
    query_cols, key_cols, value_cols = (pieces[:, :, :, 0], pieces[:, :, :, 1], pieces[:, :, :, 2])
    out_cols, probs_cols = attend(query_cols, key_cols, value_cols, "blche", "bchlm")
    upstream_cols = lax.all_to_all(upstream, "seq", split_axis=2, concat_axis=1, tiled=True)
    upstream_cols = upstream_cols.reshape(batches, all_rows, col_share, head_count, HEAD_DIM)
    grads_cols = attend_back(
        query_cols, key_cols, value_cols, probs_cols, upstream_cols, "blche", "bchlm"
    )
    stacked = jnp.stack(grads_cols, axis=3).reshape(batches, all_rows, col_share, 3 * feature)
    used_normed = normed_cols.reshape(-1, model_width)
    used_grads = stacked.reshape(-1, 3 * feature)
    grad_local = jnp.dot(used_grads, joint_weight.T, preferred_element_type=jnp.float32).astype(
        jnp.bfloat16
    )
    seq_n = lax.axis_size("seq")
    dp_n = lax.axis_size("dp")
    orders = split_orders(seq_n, dp_n)
    out_orders = orders
    core_odd = lax.axis_index("seq") % 2 == 1
    pair = [(member, member ^ 1) for member in range(seq_n)]
    core = lax.axis_index("seq") % 2

    def my_half(factor, orders=orders):
        arranged = by_split_order(factor, orders, core_odd, seq_n, dp_n)
        half = arranged.shape[1] // 2
        return lax.dynamic_slice_in_dim(arranged, core * half, half, axis=1)

    normed_peer, grads_peer = lax.ppermute((used_normed, used_grads), "seq", pair)
    joint_term = jnp.dot(
        my_half(jnp.concatenate([used_normed, normed_peer], axis=0)).T,
        jnp.concatenate([used_grads, grads_peer], axis=0),
        preferred_element_type=jnp.float32,
    )
    grad_normed = lax.all_to_all(
        grad_local.reshape(batches, all_rows, col_share, model_width),
        "seq",
        split_axis=1,
        concat_axis=2,
        tiled=True,
    )
    grad_normed = grad_normed.reshape(-1, model_width)
    (joint_sum,), grad_normed = reduce_rows((joint_term,), (orders,), seq_n, dp_n, grad_normed)
    grad_float = grad_normed.astype(jnp.float32)
    gain_term = jnp.sum(grad_float * hidden * inverse, axis=0)
    scaled = norm_gain * grad_float
    grad_hidden = (
        inverse * scaled - hidden * inverse**3 * jnp.mean(scaled * hidden, axis=-1, keepdims=True)
    ).astype(jnp.bfloat16)
    first_peer, hidden_peer, gain_peer = lax.ppermute((flat_first, grad_hidden, gain_term), "seq", pair)
    out_term = jnp.dot(
        my_half(jnp.concatenate([flat_first, first_peer], axis=0), out_orders).T,
        jnp.concatenate([grad_hidden, hidden_peer], axis=0),
        preferred_element_type=jnp.float32,
    )
    gain_term = my_half((gain_term + gain_peer)[None, :], out_orders)[0][:, None]
    out_width = out_term.shape[1]
    (out_sum,), out_cols = reduce_rows(
        (jnp.concatenate([out_term, gain_term], axis=1),), (out_orders,), seq_n, dp_n, out_cols
    )
    column_out = lax.all_to_all(
        out_cols.reshape(batches, all_rows, col_share, feature),
        "seq",
        split_axis=1,
        concat_axis=2,
        tiled=True,
    )
    replicas = (joint_sum, out_sum[:, :out_width], out_sum[:, out_width].astype(jnp.float32))
    grad_first = jnp.dot(grad_hidden, out_weight.T, preferred_element_type=jnp.float32).astype(
        jnp.bfloat16
    )
    grads_rows = attend_back(
        to_heads(first_query),
        to_heads(first_key),
        to_heads(first_value),
        probs_first,
        to_heads(grad_first),
        "glhe",
        "ghlm",
    )
    grad_query = grads_rows[0].reshape(batches, local_rows, columns, feature)
    grad_key = grads_rows[1].reshape(batches, local_rows, columns, feature)
    grad_value = grads_rows[2].reshape(batches, local_rows, columns, feature)
    return (
        grad_query,
        grad_key,
        grad_value,
        column_out,
        replicas[0].astype(jnp.bfloat16),
        replicas[1].astype(jnp.bfloat16),
        replicas[2],
    )


def solution(mesh):
    placed = (
        P("dp", "seq", None, None),
        P("dp", "seq", None, None),
        P("dp", "seq", None, None),
        P(),
        P(),
        P(),
        P("dp", "seq", None, None),
    )
    return jax.shard_map(
        on_device,
        mesh=mesh,
        in_specs=placed,
        out_specs=(
            P("dp", "seq", None, None),
            P("dp", "seq", None, None),
            P("dp", "seq", None, None),
            P("dp", "seq", None, None),
            P("seq", None),
            P("seq", None),
            P("seq"),
        ),
        check_vma=False,
    )
```
